32 devices in a mesh: seq: 16 (over z, y, x), head: 2 (over core).
Axes of the slice: x: 2, y: 2, z: 4, core: 2. Of those that a mesh axis runs over, the one named last changes fastest.
Arguments:
- query_raw: bfloat16 [2048, 1024], P('seq', 'head'), may hold values from -448 to 448
- key_raw: bfloat16 [2048, 1024], P('seq', 'head'), may hold values from -448 to 448
- value_raw: bfloat16 [2048, 2048], P('seq', 'head'), may hold values from -448 to 448
- query_scale: float32 [2048, 8], P('seq', 'head'), may hold values from 0.004 to 0.04
- key_block_scale: float32 [2048, 8], P('seq', 'head'), may hold values from 0.004 to 0.04
- value_scale: float32 [2048, 16], P('seq', 'head'), may hold values from 0.004 to 0.04
- conv_query: bfloat16 [4, 1024], P(None, 'head'), may hold values from -3 to 3
- key_filter_taps: bfloat16 [4, 1024], P(None, 'head'), may hold values from -3 to 3
- conv_value: bfloat16 [4, 2048], P(None, 'head'), may hold values from -3 to 3
- gate_input: float32 [2048, 16], P('seq', 'head'), may hold values from -7 to 28672
- beta_logit: float32 [2048, 16], P('seq', 'head'), may hold values from -12 to 5
- decay_base: float32 [16], replicated, may hold values from -16 to 0
- step_bias: float32 [16], replicated, may hold values from -3 to 3
- output_gate: bfloat16 [2048, 2048], P('seq', 'head'), may hold values from -6 to 6
- norm_gain: float32 [128], replicated, may hold values from 0.5 to 1.5
Outputs:
- output: bfloat16 [2048, 2048], P('seq', 'head')
The draws below stay inside these ranges and needn't reach their ends.
All inputs are finite; a program needn't handle non-finite values.
Results may differ from the reference program's by a relative error of at most 0.0048.
Values may be sent and summed in bfloat16 or wider, within the bound.
No kernel may reach another device: no remote copies, remote signals or barrier semaphores. Data moves between devices by JAX's collectives and lax.ppermute only.
A program may use at most 512 MiB of HBM per device.

```python
import math
import jax
import jax.numpy as jnp
from jax import lax

DK = 128
HK = 8
HV = 16
KW = 4
CH = 64
TOK_DEV = 128
PROMPT_TOKENS = 2048


def head_plan(key, slow_count):
    order = jax.random.permutation(jax.random.fold_in(key, 101), HV)
    sluggish_heads = order < slow_count
    strength = jax.random.uniform(jax.random.fold_in(key, 102), (HV,), jnp.float32, 0.1, 0.5)
    fast_rate = jnp.exp(jax.random.uniform(jax.random.fold_in(key, 103), (HV,), jnp.float32, jnp.log(0.02), jnp.log(0.06)))
    return (sluggish_heads, strength, fast_rate)


def quiet_rows(key, sluggish_heads):
    shard_count = PROMPT_TOKENS // TOK_DEV
    span_shards = min(6, shard_count // 2)
    first_shard = jax.random.randint(jax.random.fold_in(key, 110), (HV,), shard_count // 4, shard_count - span_shards + 1)
    shard_of = jnp.arange(PROMPT_TOKENS) // TOK_DEV
    inside = (shard_of[:, None] >= first_shard[None, :]) & (shard_of[:, None] < first_shard[None, :] + span_shards)
    return inside & jnp.logical_not(sluggish_heads)[None, :]


def draw_decay_base(key, part):
    slow_count = HV // 2
    sluggish_heads, strength, fast_rate = head_plan(key, slow_count)
    rates = jnp.where(sluggish_heads, strength / PROMPT_TOKENS, fast_rate)
    return jnp.log(rates).astype(jnp.float32)


def draw_gate_input(key, part):
    slow_count = HV // 2
    baseline_rows = jnp.clip(jax.random.normal(jax.random.fold_in(key, 104), (PROMPT_TOKENS, HV), jnp.float32), -4.0, 4.0)
    sluggish_heads, strength, fast_rate = head_plan(key, slow_count)
    shard_count = PROMPT_TOKENS // TOK_DEV
    shard_shift = jnp.clip(jax.random.normal(jax.random.fold_in(key, 105), (shard_count, HV), jnp.float32), -3.0, 3.0)
    baseline_rows = baseline_rows + jnp.repeat(shard_shift, TOK_DEV, axis=0)
    spike_positions = jax.random.randint(jax.random.fold_in(key, 106), (4,), 0, PROMPT_TOKENS)
    losses = jax.random.uniform(jax.random.fold_in(key, 107), (4,), jnp.float32, 0.2, 0.5)
    spike_matches = (jnp.arange(PROMPT_TOKENS)[:, None] == spike_positions[None, :]).astype(jnp.float32)
    raised_values = -jnp.log1p(-losses)[:, None] * PROMPT_TOKENS / strength[None, :]
    spike_rows = jnp.sum(spike_matches[:, :, None] * raised_values[None, :, :], axis=1)
    spiked_rows = jnp.sum(spike_matches, axis=1) > 0
    spiked = jnp.where(spiked_rows[:, None] & sluggish_heads[None, :], spike_rows, baseline_rows)
    quiet = quiet_rows(key, sluggish_heads)
    quiet_gate = jax.random.uniform(jax.random.fold_in(key, 111), (PROMPT_TOKENS, HV), jnp.float32, -7.0, -6.0)
    return jnp.where(quiet, quiet_gate, spiked).astype(jnp.float32)


def draw_beta_logit(key, part):
    slow_count = HV // 2
    fast_logit = jnp.clip(1.5 * jax.random.normal(jax.random.fold_in(key, 109), (PROMPT_TOKENS, HV), jnp.float32), -5.0, 5.0)
    sluggish_heads, strength, fast_rate = head_plan(key, slow_count)
    spread = jnp.exp(jax.random.uniform(jax.random.fold_in(key, 108), (PROMPT_TOKENS, HV), jnp.float32, jnp.log(0.5), jnp.log(2.0)))
    slow_beta = spread * DK / (4.0 * PROMPT_TOKENS)
    slow_logit = jnp.log(slow_beta) - jnp.log1p(-slow_beta)
    chosen = jnp.where(sluggish_heads[None, :], slow_logit, fast_logit)
    quiet = quiet_rows(key, sluggish_heads)
    quiet_logit = jax.random.uniform(jax.random.fold_in(key, 112), (PROMPT_TOKENS, HV), jnp.float32, -12.0, -10.0)
    return jnp.where(quiet, quiet_logit, chosen).astype(jnp.float32)


def block_levels(own_key, dims, pieces, least, top_value):
    loudness = 1.0
    for axis_at, parts in pieces:
        steps = jax.random.uniform(jax.random.fold_in(jax.random.fold_in(own_key, 6), axis_at), (parts,), jnp.float32, least / len(pieces), top_value / len(pieces))
        loudness = loudness * jnp.repeat(jnp.exp(steps), dims[axis_at] // parts).reshape((-1,) + (1,) * (len(dims) - 1 - axis_at))
    return loudness


def scatter_about(stream_key, shape, scale, limit, split=(), held_as=jnp.bfloat16):
    drawn = scale * jax.random.normal(stream_key, shape, jnp.float32)
    if split:
        drawn = drawn * block_levels(stream_key, shape, split, -0.22, 0.18)
    return jnp.clip(drawn, -limit, limit).astype(held_as)


def setup_inputs(seed: int = 0) -> dict:
    key_of = jax.random.split(jax.random.key(seed), 16)
    return {
        "query_raw": scatter_about(key_of[0], (PROMPT_TOKENS, HK * DK), 64.0, 448.0, ((0, 16), (1, 2))),
        "key_raw": scatter_about(key_of[1], (PROMPT_TOKENS, HK * DK), 64.0, 448.0, ((0, 16), (1, 2))),
        "value_raw": scatter_about(key_of[2], (PROMPT_TOKENS, HV * DK), 64.0, 448.0, ((0, 16), (1, 2))),
        "query_scale": jnp.clip(jnp.exp(math.log(0.04) - 2.30258502 * jax.random.uniform(key_of[3], (PROMPT_TOKENS, HK), jnp.float32) ** block_levels(key_of[3], (PROMPT_TOKENS, HK), ((0, 16), (1, 2)), -0.2, 0.2)), 0.004, 0.04),
        "key_block_scale": jnp.clip(jnp.exp(math.log(0.04) - 2.30258502 * jax.random.uniform(key_of[4], (PROMPT_TOKENS, HK), jnp.float32) ** block_levels(key_of[4], (PROMPT_TOKENS, HK), ((0, 16), (1, 2)), -0.2, 0.2)), 0.004, 0.04),
        "value_scale": jnp.clip(jnp.exp(math.log(0.04) - 2.30258502 * jax.random.uniform(key_of[5], (PROMPT_TOKENS, HV), jnp.float32) ** block_levels(key_of[5], (PROMPT_TOKENS, HV), ((0, 16), (1, 2)), -0.2, 0.2)), 0.004, 0.04),
        "conv_query": scatter_about(key_of[6], (KW, HK * DK), KW ** -0.5, 3.0, ((1, 2),)),
        "key_filter_taps": scatter_about(key_of[7], (KW, HK * DK), KW ** -0.5, 3.0, ((1, 2),)),
        "conv_value": scatter_about(key_of[8], (KW, HV * DK), KW ** -0.5, 3.0, ((1, 2),)),
        "gate_input": draw_gate_input(jax.random.fold_in(key_of[15], 71), 0),
        "beta_logit": draw_beta_logit(jax.random.fold_in(key_of[15], 71), 0),
        "decay_base": draw_decay_base(jax.random.fold_in(key_of[15], 71), 0),
        "step_bias": scatter_about(key_of[12], (HV,), 1.0, 3.0, (), jnp.float32),
        "output_gate": scatter_about(key_of[13], (PROMPT_TOKENS, HV * DK), 1.0, 6.0, ((0, 16), (1, 2))),
        "norm_gain": jnp.clip(1.0 + 0.1 * jax.random.normal(key_of[14], (DK,), jnp.float32), 0.5, 1.5),
    }


HIGHEST = lax.Precision.HIGHEST
EPSILON = 1e-06

def expand_quantized(raw_rows, scales):
    row_count = raw_rows.shape[0]
    head_count = scales.shape[1]
    shaped = raw_rows.astype(jnp.float32).reshape(row_count, head_count, -1) * scales[:, :, None]
    return shaped.reshape(row_count, -1)

def causal_filter(window, weights):
    kernel_span = weights.shape[0]
    row_count = window.shape[0] - kernel_span + 1
    summed = jnp.zeros((row_count, window.shape[1]), jnp.float32)
    for offset_tap in range(kernel_span):
        summed = summed + window[offset_tap:offset_tap + row_count] * weights[offset_tap].astype(jnp.float32)
    return lax.optimization_barrier(jax.nn.silu(summed).astype(jnp.bfloat16))

def unit_heads(conv_rows, head_width):
    row_count = conv_rows.shape[0]
    shaped = conv_rows.astype(jnp.float32).reshape(row_count, -1, head_width)
    return shaped * lax.rsqrt(lax.optimization_barrier(jnp.sum(shaped * shaped, axis=-1, keepdims=True)) + EPSILON)

def head_inputs(query_conv, key_filtered, value_conv, gate_rows, beta_rows, decay_base, step_bias, head_width, block):
    row_count = query_conv.shape[0]
    queries = unit_heads(query_conv, head_width) * head_width ** (-0.5)
    key_units = unit_heads(key_filtered, head_width)
    value_units = value_conv.astype(jnp.float32).reshape(row_count, -1, head_width)
    repeats = value_units.shape[1] // key_units.shape[1]
    queries = jnp.repeat(queries, repeats, axis=1)
    key_units = jnp.repeat(key_units, repeats, axis=1)
    logdec = -jnp.exp(decay_base)[None, :] * jax.nn.softplus(gate_rows + step_bias[None, :])
    betas_all = jax.nn.sigmoid(beta_rows)
    block_count = row_count // block

    def to_blocks(array):
        return array.reshape(block_count, block, array.shape[1], -1).transpose(0, 2, 1, 3)

    def to_block_rows(array):
        return array.reshape(block_count, block, -1).transpose(0, 2, 1)
    return (to_blocks(queries), to_blocks(key_units), to_blocks(value_units), to_block_rows(logdec), to_block_rows(betas_all))

def unit_lower_inverse(strict_part):
    length = strict_part.shape[-1]
    negated = -strict_part
    inverse = jnp.eye(length, dtype=jnp.float32) + negated
    power = negated
    span = 2
    while span < length:
        power = jnp.einsum('bhij,bhjk->bhik', power, power, precision=HIGHEST)
        inverse = inverse + jnp.einsum('bhij,bhjk->bhik', inverse, power, precision=HIGHEST)
        span = span * 2
    return inverse

def block_terms(queries, key_units, value_units, logdec, beta_units):
    length = logdec.shape[-1]
    positions = jnp.arange(length)
    lower_incl = positions[:, None] >= positions[None, :]
    lower_strict = positions[:, None] > positions[None, :]
    cumulative = jnp.cumsum(logdec, axis=-1)
    differ = cumulative[..., :, None] - cumulative[..., None, :]
    decay_incl = jnp.where(lower_incl, jnp.exp(jnp.where(lower_incl, differ, 0.0)), 0.0)
    decay_strict = jnp.where(lower_strict, decay_incl, 0.0)
    key_gram = jnp.einsum('bhid,bhjd->bhij', key_units, key_units, precision=HIGHEST)
    inverse = unit_lower_inverse(beta_units[..., :, None] * key_gram * decay_strict)
    growth = jnp.exp(cumulative)
    stacked = jnp.concatenate([beta_units[..., None] * value_units, (beta_units * growth)[..., None] * key_units], axis=-1)
    solved = jnp.einsum('bhij,bhjd->bhid', inverse, stacked, precision=HIGHEST)
    value_width = value_units.shape[-1]
    weight_values = solved[..., :value_width]
    weight_keys = solved[..., value_width:]
    mixing = decay_incl * jnp.einsum('bhid,bhjd->bhij', queries, key_units, precision=HIGHEST)
    zero_out = jnp.einsum('bhij,bhjd->bhid', mixing, weight_values, precision=HIGHEST)
    readout = growth[..., None] * queries - jnp.einsum('bhij,bhjd->bhid', mixing, weight_keys, precision=HIGHEST)
    fading = jnp.exp(cumulative[..., -1:] - cumulative)[..., None] * key_units
    eye_key = jnp.eye(key_units.shape[-1], dtype=jnp.float32)
    transition = growth[..., -1][..., None, None] * eye_key - jnp.einsum('bhjd,bhje->bhde', fading, weight_keys, precision=HIGHEST)
    offset = jnp.einsum('bhjd,bhje->bhde', fading, weight_values, precision=HIGHEST)
    return (zero_out, readout, transition, offset)

def product(left, right):
    return jnp.einsum('hde,hef->hdf', left, right, precision=HIGHEST)

def to_rows(blocks):
    return blocks.transpose(0, 2, 1, 3).reshape(-1, blocks.shape[1], blocks.shape[3])

def gated_norm(delta_rows, gate_raw, norm_gain):
    meansq = lax.optimization_barrier(jnp.mean(delta_rows * delta_rows, axis=-1, keepdims=True))
    normed = delta_rows * lax.rsqrt(meansq + EPSILON) * norm_gain
    gate_float = gate_raw.astype(jnp.float32).reshape(delta_rows.shape)
    return (normed * jax.nn.silu(gate_float)).reshape(delta_rows.shape[0], -1).astype(jnp.bfloat16)

def reference(query_raw, key_raw, value_raw, query_scale, key_block_scale, value_scale, conv_query, key_filter_taps, conv_value, gate_input, beta_logit, decay_base, step_bias, output_gate, norm_gain):
    margin = KW - 1

    def padding_above(array):
        return jnp.concatenate([jnp.zeros((margin, array.shape[1]), array.dtype), array], axis=0)
    pad_query = padding_above(query_raw)
    padded_key = padding_above(key_raw)
    pad_value = padding_above(value_raw)
    pad_qscale = padding_above(query_scale)
    padded_key_scale = padding_above(key_block_scale)
    pad_vscale = padding_above(value_scale)
    block_count = PROMPT_TOKENS // CH

    def advance(state_now, block_index):
        first_row = (block_index * CH).astype(jnp.int32)

        def including_margin(array):
            return lax.dynamic_slice_in_dim(array, first_row, CH + margin, 0)

        def plain_rows(array):
            return lax.dynamic_slice_in_dim(array, first_row, CH, 0)
        query_conv = causal_filter(expand_quantized(including_margin(pad_query), including_margin(pad_qscale)), conv_query)
        key_filtered = causal_filter(expand_quantized(including_margin(padded_key), including_margin(padded_key_scale)), key_filter_taps)
        value_conv = causal_filter(expand_quantized(including_margin(pad_value), including_margin(pad_vscale)), conv_value)
        zero_out, readout, transition, offset = block_terms(*head_inputs(query_conv, key_filtered, value_conv, plain_rows(gate_input), plain_rows(beta_logit), decay_base, step_bias, DK, CH))
        outputs = zero_out + jnp.einsum('bhid,hde->bhie', readout, state_now, precision=HIGHEST)
        state_next = product(transition[0], state_now) + offset[0]
        gated_rows = gated_norm(to_rows(outputs), plain_rows(output_gate), norm_gain)
        return (state_next, gated_rows)
    initial = jnp.zeros((HV, DK, DK), jnp.float32)
    _, blocks = lax.scan(advance, initial, jnp.arange(block_count, dtype=jnp.int32))
    return blocks.reshape(PROMPT_TOKENS, HV * DK)
```

```python
import jax
import jax.numpy as jnp
from jax import lax
from jax.sharding import PartitionSpec as P

CH = 64


HIGHEST = lax.Precision.HIGHEST
EPSILON = 1e-06


def from_behind(value, axis, steps):
    count = lax.axis_size(axis)
    first, last = (max(0, -steps), min(count, count - steps))
    return lax.ppermute(value, axis, [(source, source + steps) for source in range(first, last)])


def scan_states(trans, offset, axis):
    devices, mine = (lax.axis_size(axis), lax.axis_index(axis))
    span = 1
    while span < devices:
        pairs = [(source, source + span) for source in range(devices - span)]
        if 2 * span < devices:
            trans_in, offset_in = lax.ppermute((trans, offset), axis, pairs)
            offset = product(trans, offset_in) + offset
            trans = jnp.where(mine >= span, product(trans, trans_in), trans)
        else:
            offset_in = lax.ppermute(offset, axis, pairs)
            offset = product(trans, offset_in) + offset
        span = span * 2
    return from_behind(offset, axis, 1)


def expand_quantized(raw_rows, scales):
    row_count = raw_rows.shape[0]
    head_count = scales.shape[1]
    shaped = raw_rows.astype(jnp.float32).reshape(row_count, head_count, -1) * scales[:, :, None]
    return shaped.reshape(row_count, -1)


def causal_filter(window, weights):
    kernel_span = weights.shape[0]
    row_count = window.shape[0] - kernel_span + 1
    summed = jnp.zeros((row_count, window.shape[1]), jnp.float32)
    for offset_tap in range(kernel_span):
        summed = summed + window[offset_tap : offset_tap + row_count] * weights[offset_tap].astype(
            jnp.float32
        )
    return lax.optimization_barrier(jax.nn.silu(summed).astype(jnp.bfloat16))


def unit_heads(conv_rows, head_width):
    row_count = conv_rows.shape[0]
    shaped = conv_rows.astype(jnp.float32).reshape(row_count, -1, head_width)
    return shaped * lax.rsqrt(jnp.sum(shaped * shaped, axis=-1, keepdims=True) + EPSILON)


def head_inputs(
    query_conv,
    key_filtered,
    value_conv,
    gate_rows,
    beta_rows,
    decay_base,
    step_bias,
    head_width,
    block,
):
    row_count = query_conv.shape[0]
    queries = unit_heads(query_conv, head_width) * head_width ** (-0.5)
    key_units = unit_heads(key_filtered, head_width)
    value_units = value_conv.astype(jnp.float32).reshape(row_count, -1, head_width)
    repeats = value_units.shape[1] // key_units.shape[1]
    queries = jnp.repeat(queries, repeats, axis=1)
    key_units = jnp.repeat(key_units, repeats, axis=1)
    logdec = -jnp.exp(decay_base)[None, :] * jax.nn.softplus(gate_rows + step_bias[None, :])
    betas_all = jax.nn.sigmoid(beta_rows)
    block_count = row_count // block

    def to_blocks(array):
        return array.reshape(block_count, block, array.shape[1], -1).transpose(0, 2, 1, 3)

    def to_block_rows(array):
        return array.reshape(block_count, block, -1).transpose(0, 2, 1)

    return (
        to_blocks(queries),
        to_blocks(key_units),
        to_blocks(value_units),
        to_block_rows(logdec),
        to_block_rows(betas_all),
    )


def unit_lower_inverse(strict_part):
    length = strict_part.shape[-1]
    negated = -strict_part
    inverse = jnp.eye(length, dtype=jnp.float32) + negated
    power = negated
    span = 2
    while span < length:
        power = jnp.einsum("bhij,bhjk->bhik", power, power, precision=HIGHEST)
        inverse = inverse + jnp.einsum("bhij,bhjk->bhik", inverse, power, precision=HIGHEST)
        span = span * 2
    return inverse


def block_terms(queries, key_units, value_units, logdec, beta_units):
    length = logdec.shape[-1]
    positions = jnp.arange(length)
    lower_incl = positions[:, None] >= positions[None, :]
    lower_strict = positions[:, None] > positions[None, :]
    cumulative = jnp.cumsum(logdec, axis=-1)
    differ = cumulative[..., :, None] - cumulative[..., None, :]
    decay_incl = jnp.where(lower_incl, jnp.exp(jnp.where(lower_incl, differ, 0.0)), 0.0)
    decay_strict = jnp.where(lower_strict, decay_incl, 0.0)
    key_gram = jnp.einsum("bhid,bhjd->bhij", key_units, key_units, precision=HIGHEST)
    inverse = unit_lower_inverse(beta_units[..., :, None] * key_gram * decay_strict)
    growth = jnp.exp(cumulative)
    stacked = jnp.concatenate(
        [beta_units[..., None] * value_units, (beta_units * growth)[..., None] * key_units], axis=-1
    )
    solved = jnp.einsum("bhij,bhjd->bhid", inverse, stacked, precision=HIGHEST)
    value_width = value_units.shape[-1]
    weight_values = solved[..., :value_width]
    weight_keys = solved[..., value_width:]
    mixing = decay_incl * jnp.einsum("bhid,bhjd->bhij", queries, key_units, precision=HIGHEST)
    zero_out = jnp.einsum("bhij,bhjd->bhid", mixing, weight_values, precision=HIGHEST)
    readout = growth[..., None] * queries - jnp.einsum(
        "bhij,bhjd->bhid", mixing, weight_keys, precision=HIGHEST
    )
    fading = jnp.exp(cumulative[..., -1:] - cumulative)[..., None] * key_units
    eye_key = jnp.eye(key_units.shape[-1], dtype=jnp.float32)
    transition = growth[..., -1][..., None, None] * eye_key - jnp.einsum(
        "bhjd,bhje->bhde", fading, weight_keys, precision=HIGHEST
    )
    offset = jnp.einsum("bhjd,bhje->bhde", fading, weight_values, precision=HIGHEST)
    return (zero_out, readout, transition, offset)


def product(left, right):
    return jnp.einsum("hde,hef->hdf", left, right, precision=HIGHEST)


def chain_blocks(transition, offset):
    head_count = offset.shape[1]
    key_width = offset.shape[2]
    value_width = offset.shape[3]
    initial = (
        jnp.zeros((head_count, key_width, value_width), jnp.float32),
        jnp.broadcast_to(jnp.eye(key_width, dtype=jnp.float32), (head_count, key_width, key_width)),
    )

    def chain_advance(carried, block_items):
        state_now, map_now = carried
        trans_now, offset_now = block_items
        following = (product(trans_now, state_now) + offset_now, product(trans_now, map_now))
        return (following, ())

    return lax.scan(chain_advance, initial, (transition, offset))


def replay_blocks(transition, offset, incoming):

    def replay_advance(state_now, block_items):
        trans_now, offset_now = block_items
        return (product(trans_now, state_now) + offset_now, state_now)

    _, starts = lax.scan(replay_advance, incoming, (transition, offset))
    return starts


def combine_maps(earlier, later):
    trans_early, offset_early = earlier
    trans_late, offset_late = later
    return (product(trans_late, trans_early), product(trans_late, offset_early) + offset_late)


def to_rows(blocks):
    return blocks.transpose(0, 2, 1, 3).reshape(-1, blocks.shape[1], blocks.shape[3])


def gated_norm(delta_rows, gate_raw, norm_gain):
    meansq = jnp.mean(delta_rows * delta_rows, axis=-1, keepdims=True)
    normed = delta_rows * lax.rsqrt(meansq + EPSILON) * norm_gain
    gate_float = gate_raw.astype(jnp.float32).reshape(delta_rows.shape)
    return (normed * jax.nn.silu(gate_float)).reshape(delta_rows.shape[0], -1).astype(jnp.bfloat16)


def identity_of(trans_like, offset_like):
    return (
        jnp.broadcast_to(jnp.eye(trans_like.shape[1], dtype=jnp.float32), trans_like.shape),
        jnp.zeros_like(offset_like),
    )


def shards(
    query_raw,
    key_raw,
    value_raw,
    query_scale,
    key_block_scale,
    value_scale,
    conv_query,
    key_filter_taps,
    conv_value,
    gate_input,
    beta_logit,
    decay_base,
    step_bias,
    output_gate,
    norm_gain,
):
    head_width = norm_gain.shape[0]
    margin = conv_query.shape[0] - 1
    query_deq = expand_quantized(query_raw, query_scale)
    key_deq = expand_quantized(key_raw, key_block_scale)
    value_deq = expand_quantized(value_raw, value_scale)
    query_width, key_width = (query_deq.shape[1], key_deq.shape[1])
    tails = from_behind(
        jnp.concatenate([query_deq[-margin:], key_deq[-margin:], value_deq[-margin:]], axis=1),
        "seq",
        1,
    )
    tail_rows = (
        tails[:, :query_width],
        tails[:, query_width : query_width + key_width],
        tails[:, query_width + key_width :],
    )
    query_conv = causal_filter(jnp.concatenate([tail_rows[0], query_deq], axis=0), conv_query)
    key_filtered = causal_filter(jnp.concatenate([tail_rows[1], key_deq], axis=0), key_filter_taps)
    value_conv = causal_filter(jnp.concatenate([tail_rows[2], value_deq], axis=0), conv_value)
    local_heads = gate_input.shape[1]
    first_head = lax.axis_index("head") * local_heads
    base_part = lax.dynamic_slice_in_dim(decay_base, first_head, local_heads)
    bias_part = lax.dynamic_slice_in_dim(step_bias, first_head, local_heads)
    zero_out, readout, transition, offset = block_terms(
        *head_inputs(
            query_conv,
            key_filtered,
            value_conv,
            gate_input,
            beta_logit,
            base_part,
            bias_part,
            head_width,
            CH,
        )
    )
    finals, emitted = chain_blocks(transition, offset)
    dev_offset, dev_trans = finals
    incoming = scan_states(dev_trans, dev_offset, "seq")
    starts = replay_blocks(transition, offset, incoming)
    outputs = zero_out + jnp.einsum("bhid,bhde->bhie", readout, starts, precision=HIGHEST)
    gated_rows = gated_norm(to_rows(outputs), output_gate, norm_gain)
    return gated_rows


def solution(mesh):
    placed = (
        P("seq", "head"),
        P("seq", "head"),
        P("seq", "head"),
        P("seq", "head"),
        P("seq", "head"),
        P("seq", "head"),
        P(None, "head"),
        P(None, "head"),
        P(None, "head"),
        P("seq", "head"),
        P("seq", "head"),
        P(),
        P(),
        P("seq", "head"),
        P(),
    )
    return jax.shard_map(
        shards, mesh=mesh, in_specs=placed, out_specs=P("seq", "head"), check_vma=False
    )
```

```python
import jax
import jax.numpy as jnp
from jax import lax
from jax.sharding import PartitionSpec as P

CH = 64


HIGHEST = lax.Precision.HIGHEST
EPSILON = 1e-06


def from_behind(value, axis, steps):
    count = lax.axis_size(axis)
    first, last = (max(0, -steps), min(count, count - steps))
    return lax.ppermute(value, axis, [(source, source + steps) for source in range(first, last)])


def compose(later, earlier, width):
    merged = jnp.einsum("hde,hef->hdf", later[..., :width], earlier, precision=HIGHEST)
    return merged.at[..., width:].add(later[..., width:])


def scan_states(trans, offset, axis):
    devices, mine = (lax.axis_size(axis), lax.axis_index(axis))
    width = trans.shape[-1]
    inclusive = jnp.concatenate([trans, offset], axis=-1)
    exclusive = None
    state = jnp.zeros_like(offset)
    span = 1
    while span < devices:
        pairs = [(source, source + span) for source in range(devices - span)]
        if 2 * span >= devices:
            earlier_state = lax.ppermute(inclusive[..., width:], axis, pairs)
            if exclusive is None:
                state = earlier_state
            else:
                state = state + product(exclusive[..., :width], earlier_state)
            break
        earlier = lax.ppermute(inclusive, axis, pairs)
        exclusive = earlier if exclusive is None else compose(exclusive, earlier, width)
        state = exclusive[..., width:]
        if 4 * span < devices:
            inclusive = jnp.where(mine >= span, compose(inclusive, earlier, width), inclusive)
        else:
            inclusive = inclusive.at[..., width:].add(product(inclusive[..., :width], earlier[..., width:]))
        span = span * 2
    return state


def expand_quantized(raw_rows, scales):
    row_count = raw_rows.shape[0]
    head_count = scales.shape[1]
    shaped = raw_rows.astype(jnp.float32).reshape(row_count, head_count, -1) * scales[:, :, None]
    return shaped.reshape(row_count, -1)


def causal_filter(window, weights):
    kernel_span = weights.shape[0]
    row_count = window.shape[0] - kernel_span + 1
    summed = jnp.zeros((row_count, window.shape[1]), jnp.float32)
    for offset_tap in range(kernel_span):
        summed = summed + window[offset_tap : offset_tap + row_count] * weights[offset_tap].astype(
            jnp.float32
        )
    return lax.optimization_barrier(jax.nn.silu(summed).astype(jnp.bfloat16))


def unit_heads(conv_rows, head_width):
    row_count = conv_rows.shape[0]
    shaped = conv_rows.astype(jnp.float32).reshape(row_count, -1, head_width)
    return shaped * lax.rsqrt(jnp.sum(shaped * shaped, axis=-1, keepdims=True) + EPSILON)


def head_inputs(
    query_conv,
    key_filtered,
    value_conv,
    gate_rows,
    beta_rows,
    decay_base,
    step_bias,
    head_width,
    block,
):
    row_count = query_conv.shape[0]
    queries = unit_heads(query_conv, head_width) * head_width ** (-0.5)
    key_units = unit_heads(key_filtered, head_width)
    value_units = value_conv.astype(jnp.float32).reshape(row_count, -1, head_width)
    repeats = value_units.shape[1] // key_units.shape[1]
    queries = jnp.repeat(queries, repeats, axis=1)
    key_units = jnp.repeat(key_units, repeats, axis=1)
    logdec = -jnp.exp(decay_base)[None, :] * jax.nn.softplus(gate_rows + step_bias[None, :])
    betas_all = jax.nn.sigmoid(beta_rows)
    block_count = row_count // block

    def to_blocks(array):
        return array.reshape(block_count, block, array.shape[1], -1).transpose(0, 2, 1, 3)

    def to_block_rows(array):
        return array.reshape(block_count, block, -1).transpose(0, 2, 1)

    return (
        to_blocks(queries),
        to_blocks(key_units),
        to_blocks(value_units),
        to_block_rows(logdec),
        to_block_rows(betas_all),
    )


def unit_lower_inverse(strict_part):
    length = strict_part.shape[-1]
    negated = -strict_part
    inverse = jnp.eye(length, dtype=jnp.float32) + negated
    power = negated
    span = 2
    while span < length:
        power = jnp.einsum("bhij,bhjk->bhik", power, power, precision=HIGHEST)
        inverse = inverse + jnp.einsum("bhij,bhjk->bhik", inverse, power, precision=HIGHEST)
        span = span * 2
    return inverse


def block_terms(queries, key_units, value_units, logdec, beta_units):
    length = logdec.shape[-1]
    positions = jnp.arange(length)
    lower_incl = positions[:, None] >= positions[None, :]
    lower_strict = positions[:, None] > positions[None, :]
    cumulative = jnp.cumsum(logdec, axis=-1)
    differ = cumulative[..., :, None] - cumulative[..., None, :]
    decay_incl = jnp.where(lower_incl, jnp.exp(jnp.where(lower_incl, differ, 0.0)), 0.0)
    decay_strict = jnp.where(lower_strict, decay_incl, 0.0)
    key_gram = jnp.einsum("bhid,bhjd->bhij", key_units, key_units, precision=HIGHEST)
    inverse = unit_lower_inverse(beta_units[..., :, None] * key_gram * decay_strict)
    growth = jnp.exp(cumulative)
    stacked = jnp.concatenate(
        [beta_units[..., None] * value_units, (beta_units * growth)[..., None] * key_units], axis=-1
    )
    solved = jnp.einsum("bhij,bhjd->bhid", inverse, stacked, precision=HIGHEST)
    value_width = value_units.shape[-1]
    weight_values = solved[..., :value_width]
    weight_keys = solved[..., value_width:]
    mixing = decay_incl * jnp.einsum("bhid,bhjd->bhij", queries, key_units, precision=HIGHEST)
    zero_out = jnp.einsum("bhij,bhjd->bhid", mixing, weight_values, precision=HIGHEST)
    readout = growth[..., None] * queries - jnp.einsum(
        "bhij,bhjd->bhid", mixing, weight_keys, precision=HIGHEST
    )
    fading = jnp.exp(cumulative[..., -1:] - cumulative)[..., None] * key_units
    eye_key = jnp.eye(key_units.shape[-1], dtype=jnp.float32)
    transition = growth[..., -1][..., None, None] * eye_key - jnp.einsum(
        "bhjd,bhje->bhde", fading, weight_keys, precision=HIGHEST
    )
    offset = jnp.einsum("bhjd,bhje->bhde", fading, weight_values, precision=HIGHEST)
    return (zero_out, readout, transition, offset)


def product(left, right):
    return jnp.einsum("hde,hef->hdf", left, right, precision=HIGHEST)


def chain_blocks(transition, offset):
    head_count = offset.shape[1]
    key_width = offset.shape[2]
    value_width = offset.shape[3]
    initial = (
        jnp.zeros((head_count, key_width, value_width), jnp.float32),
        jnp.broadcast_to(jnp.eye(key_width, dtype=jnp.float32), (head_count, key_width, key_width)),
    )

    def chain_advance(carried, block_items):
        state_now, map_now = carried
        trans_now, offset_now = block_items
        following = (product(trans_now, state_now) + offset_now, product(trans_now, map_now))
        return (following, ())

    return lax.scan(chain_advance, initial, (transition, offset))


def replay_blocks(transition, offset, incoming):

    def replay_advance(state_now, block_items):
        trans_now, offset_now = block_items
        return (product(trans_now, state_now) + offset_now, state_now)

    _, starts = lax.scan(replay_advance, incoming, (transition, offset))
    return starts


def combine_maps(earlier, later):
    trans_early, offset_early = earlier
    trans_late, offset_late = later
    return (product(trans_late, trans_early), product(trans_late, offset_early) + offset_late)


def to_rows(blocks):
    return blocks.transpose(0, 2, 1, 3).reshape(-1, blocks.shape[1], blocks.shape[3])


def gated_norm(delta_rows, gate_raw, norm_gain):
    meansq = jnp.mean(delta_rows * delta_rows, axis=-1, keepdims=True)
    normed = delta_rows * lax.rsqrt(meansq + EPSILON) * norm_gain
    gate_float = gate_raw.astype(jnp.float32).reshape(delta_rows.shape)
    return (normed * jax.nn.silu(gate_float)).reshape(delta_rows.shape[0], -1).astype(jnp.bfloat16)


def identity_of(trans_like, offset_like):
    return (
        jnp.broadcast_to(jnp.eye(trans_like.shape[1], dtype=jnp.float32), trans_like.shape),
        jnp.zeros_like(offset_like),
    )


def shards(
    query_raw,
    key_raw,
    value_raw,
    query_scale,
    key_block_scale,
    value_scale,
    conv_query,
    key_filter_taps,
    conv_value,
    gate_input,
    beta_logit,
    decay_base,
    step_bias,
    output_gate,
    norm_gain,
):
    head_width = norm_gain.shape[0]
    margin = conv_query.shape[0] - 1
    query_deq = expand_quantized(query_raw, query_scale)
    key_deq = expand_quantized(key_raw, key_block_scale)
    value_deq = expand_quantized(value_raw, value_scale)
    query_width, key_width = (query_deq.shape[1], key_deq.shape[1])
    tails = from_behind(
        jnp.concatenate([query_deq[-margin:], key_deq[-margin:], value_deq[-margin:]], axis=1),
        "seq",
        1,
    )
    tail_rows = (
        tails[:, :query_width],
        tails[:, query_width : query_width + key_width],
        tails[:, query_width + key_width :],
    )
    query_conv = causal_filter(jnp.concatenate([tail_rows[0], query_deq], axis=0), conv_query)
    key_filtered = causal_filter(jnp.concatenate([tail_rows[1], key_deq], axis=0), key_filter_taps)
    value_conv = causal_filter(jnp.concatenate([tail_rows[2], value_deq], axis=0), conv_value)
    local_heads = gate_input.shape[1]
    first_head = lax.axis_index("head") * local_heads
    base_part = lax.dynamic_slice_in_dim(decay_base, first_head, local_heads)
    bias_part = lax.dynamic_slice_in_dim(step_bias, first_head, local_heads)
    zero_out, readout, transition, offset = block_terms(
        *head_inputs(
            query_conv,
            key_filtered,
            value_conv,
            gate_input,
            beta_logit,
            base_part,
            bias_part,
            head_width,
            CH,
        )
    )
    finals, emitted = chain_blocks(transition, offset)
    dev_offset, dev_trans = finals
    incoming = scan_states(dev_trans, dev_offset, "seq")
    starts = replay_blocks(transition, offset, incoming)
    outputs = zero_out + jnp.einsum("bhid,bhde->bhie", readout, starts, precision=HIGHEST)
    gated_rows = gated_norm(to_rows(outputs), output_gate, norm_gain)
    return gated_rows


def solution(mesh):
    placed = (
        P("seq", "head"),
        P("seq", "head"),
        P("seq", "head"),
        P("seq", "head"),
        P("seq", "head"),
        P("seq", "head"),
        P(None, "head"),
        P(None, "head"),
        P(None, "head"),
        P("seq", "head"),
        P("seq", "head"),
        P(),
        P(),
        P("seq", "head"),
        P(),
    )
    return jax.shard_map(
        shards, mesh=mesh, in_specs=placed, out_specs=P("seq", "head"), check_vma=False
    )
```

```python
import jax
import jax.numpy as jnp
from jax import lax
from jax.sharding import PartitionSpec as P

CH = 64


HIGHEST = lax.Precision.HIGHEST
EPSILON = 1e-06


def from_behind(value, axis, steps):
    count = lax.axis_size(axis)
    first, last = (max(0, -steps), min(count, count - steps))
    return lax.ppermute(value, axis, [(source, source + steps) for source in range(first, last)])


def scan_states(trans, offset, axis):
    devices, mine = (lax.axis_size(axis), lax.axis_index(axis))
    spans = []
    span = 1
    while span < devices:
        spans.append(span)
        span = span * 2
    inclusive_maps, exclusive_maps = ([], [None])
    inclusive = trans
    for span in spans[:-1]:
        pairs = [(source, source + span) for source in range(devices - span)]
        inclusive_maps.append(inclusive)
        earlier = lax.ppermute(inclusive, axis, pairs)
        last_map = exclusive_maps[-1]
        exclusive_maps.append(earlier if last_map is None else product(last_map, earlier))
        if 4 * span < devices:
            inclusive = jnp.where(mine >= span, product(inclusive, earlier), inclusive)
    state = jnp.zeros_like(offset)
    carried = offset
    for step, span in enumerate(spans):
        pairs = [(source, source + span) for source in range(devices - span)]
        earlier = lax.ppermute(carried, axis, pairs)
        last_map = exclusive_maps[step]
        state = earlier if last_map is None else state + product(last_map, earlier)
        if step + 1 < len(spans):
            carried = product(inclusive_maps[step], earlier) + carried
    return state


def expand_quantized(raw_rows, scales):
    row_count = raw_rows.shape[0]
    head_count = scales.shape[1]
    shaped = raw_rows.astype(jnp.float32).reshape(row_count, head_count, -1) * scales[:, :, None]
    return shaped.reshape(row_count, -1)


def causal_filter(window, weights):
    kernel_span = weights.shape[0]
    row_count = window.shape[0] - kernel_span + 1
    summed = jnp.zeros((row_count, window.shape[1]), jnp.float32)
    for offset_tap in range(kernel_span):
        summed = summed + window[offset_tap : offset_tap + row_count] * weights[offset_tap].astype(
            jnp.float32
        )
    return lax.optimization_barrier(jax.nn.silu(summed).astype(jnp.bfloat16))


def unit_heads(conv_rows, head_width):
    row_count = conv_rows.shape[0]
    shaped = conv_rows.astype(jnp.float32).reshape(row_count, -1, head_width)
    return shaped * lax.rsqrt(jnp.sum(shaped * shaped, axis=-1, keepdims=True) + EPSILON)


def head_inputs(
    query_conv,
    key_filtered,
    value_conv,
    gate_rows,
    beta_rows,
    decay_base,
    step_bias,
    head_width,
    block,
):
    row_count = query_conv.shape[0]
    queries = unit_heads(query_conv, head_width) * head_width ** (-0.5)
    key_units = unit_heads(key_filtered, head_width)
    value_units = value_conv.astype(jnp.float32).reshape(row_count, -1, head_width)
    repeats = value_units.shape[1] // key_units.shape[1]
    queries = jnp.repeat(queries, repeats, axis=1)
    key_units = jnp.repeat(key_units, repeats, axis=1)
    logdec = -jnp.exp(decay_base)[None, :] * jax.nn.softplus(gate_rows + step_bias[None, :])
    betas_all = jax.nn.sigmoid(beta_rows)
    block_count = row_count // block

    def to_blocks(array):
        return array.reshape(block_count, block, array.shape[1], -1).transpose(0, 2, 1, 3)

    def to_block_rows(array):
        return array.reshape(block_count, block, -1).transpose(0, 2, 1)

    return (
        to_blocks(queries),
        to_blocks(key_units),
        to_blocks(value_units),
        to_block_rows(logdec),
        to_block_rows(betas_all),
    )


def unit_lower_inverse(strict_part):
    length = strict_part.shape[-1]
    negated = -strict_part
    inverse = jnp.eye(length, dtype=jnp.float32) + negated
    power = negated
    span = 2
    while span < length:
        power = jnp.einsum("bhij,bhjk->bhik", power, power, precision=HIGHEST)
        inverse = inverse + jnp.einsum("bhij,bhjk->bhik", inverse, power, precision=HIGHEST)
        span = span * 2
    return inverse


def block_terms(queries, key_units, value_units, logdec, beta_units):
    length = logdec.shape[-1]
    positions = jnp.arange(length)
    lower_incl = positions[:, None] >= positions[None, :]
    lower_strict = positions[:, None] > positions[None, :]
    cumulative = jnp.cumsum(logdec, axis=-1)
    differ = cumulative[..., :, None] - cumulative[..., None, :]
    decay_incl = jnp.where(lower_incl, jnp.exp(jnp.where(lower_incl, differ, 0.0)), 0.0)
    decay_strict = jnp.where(lower_strict, decay_incl, 0.0)
    key_gram = jnp.einsum("bhid,bhjd->bhij", key_units, key_units, precision=HIGHEST)
    inverse = unit_lower_inverse(beta_units[..., :, None] * key_gram * decay_strict)
    growth = jnp.exp(cumulative)
    stacked = jnp.concatenate(
        [beta_units[..., None] * value_units, (beta_units * growth)[..., None] * key_units], axis=-1
    )
    solved = jnp.einsum("bhij,bhjd->bhid", inverse, stacked, precision=HIGHEST)
    value_width = value_units.shape[-1]
    weight_values = solved[..., :value_width]
    weight_keys = solved[..., value_width:]
    mixing = decay_incl * jnp.einsum("bhid,bhjd->bhij", queries, key_units, precision=HIGHEST)
    zero_out = jnp.einsum("bhij,bhjd->bhid", mixing, weight_values, precision=HIGHEST)
    readout = growth[..., None] * queries - jnp.einsum(
        "bhij,bhjd->bhid", mixing, weight_keys, precision=HIGHEST
    )
    fading = jnp.exp(cumulative[..., -1:] - cumulative)[..., None] * key_units
    eye_key = jnp.eye(key_units.shape[-1], dtype=jnp.float32)
    transition = growth[..., -1][..., None, None] * eye_key - jnp.einsum(
        "bhjd,bhje->bhde", fading, weight_keys, precision=HIGHEST
    )
    offset = jnp.einsum("bhjd,bhje->bhde", fading, weight_values, precision=HIGHEST)
    return (zero_out, readout, transition, offset)


def product(left, right):
    return jnp.einsum("hde,hef->hdf", left, right, precision=HIGHEST)


def to_rows(blocks):
    return blocks.transpose(0, 2, 1, 3).reshape(-1, blocks.shape[1], blocks.shape[3])


def gated_norm(delta_rows, gate_raw, norm_gain):
    meansq = jnp.mean(delta_rows * delta_rows, axis=-1, keepdims=True)
    normed = delta_rows * lax.rsqrt(meansq + EPSILON) * norm_gain
    gate_float = gate_raw.astype(jnp.float32).reshape(delta_rows.shape)
    return (normed * jax.nn.silu(gate_float)).reshape(delta_rows.shape[0], -1).astype(jnp.bfloat16)


def shards(
    query_raw,
    key_raw,
    value_raw,
    query_scale,
    key_block_scale,
    value_scale,
    conv_query,
    key_filter_taps,
    conv_value,
    gate_input,
    beta_logit,
    decay_base,
    step_bias,
    output_gate,
    norm_gain,
):
    head_width = norm_gain.shape[0]
    margin = conv_query.shape[0] - 1
    query_deq = expand_quantized(query_raw, query_scale)
    key_deq = expand_quantized(key_raw, key_block_scale)
    value_deq = expand_quantized(value_raw, value_scale)
    query_width, key_width = (query_deq.shape[1], key_deq.shape[1])
    tails = from_behind(
        jnp.concatenate([query_deq[-margin:], key_deq[-margin:], value_deq[-margin:]], axis=1),
        "seq",
        1,
    )
    tail_rows = (
        tails[:, :query_width],
        tails[:, query_width : query_width + key_width],
        tails[:, query_width + key_width :],
    )
    query_conv = causal_filter(jnp.concatenate([tail_rows[0], query_deq], axis=0), conv_query)
    key_filtered = causal_filter(jnp.concatenate([tail_rows[1], key_deq], axis=0), key_filter_taps)
    value_conv = causal_filter(jnp.concatenate([tail_rows[2], value_deq], axis=0), conv_value)
    local_heads = gate_input.shape[1]
    first_head = lax.axis_index("head") * local_heads
    base_part = lax.dynamic_slice_in_dim(decay_base, first_head, local_heads)
    bias_part = lax.dynamic_slice_in_dim(step_bias, first_head, local_heads)
    zero_out, readout, transition, offset = block_terms(
        *head_inputs(
            query_conv,
            key_filtered,
            value_conv,
            gate_input,
            beta_logit,
            base_part,
            bias_part,
            head_width,
            CH,
        )
    )
    dev_trans, dev_offset = (transition[0], offset[0])
    local_outs, read_maps = ([zero_out[0]], [readout[0]])
    for block in range(1, transition.shape[0]):
        read_maps.append(jnp.einsum("hid,hde->hie", readout[block], dev_trans, precision=HIGHEST))
        local_outs.append(
            zero_out[block]
            + jnp.einsum("hid,hde->hie", readout[block], dev_offset, precision=HIGHEST)
        )
        dev_offset = product(transition[block], dev_offset) + offset[block]
        dev_trans = product(transition[block], dev_trans)
    incoming = scan_states(dev_trans, dev_offset, "seq")
    outputs = jnp.stack(local_outs) + jnp.einsum(
        "bhid,hde->bhie", jnp.stack(read_maps), incoming, precision=HIGHEST
    )
    gated_rows = gated_norm(to_rows(outputs), output_gate, norm_gain)
    return gated_rows


def solution(mesh):
    placed = (
        P("seq", "head"),
        P("seq", "head"),
        P("seq", "head"),
        P("seq", "head"),
        P("seq", "head"),
        P("seq", "head"),
        P(None, "head"),
        P(None, "head"),
        P(None, "head"),
        P("seq", "head"),
        P("seq", "head"),
        P(),
        P(),
        P("seq", "head"),
        P(),
    )
    return jax.shard_map(
        shards, mesh=mesh, in_specs=placed, out_specs=P("seq", "head"), check_vma=False
    )
```

```python
import jax
import jax.numpy as jnp
from jax import lax
from jax.sharding import PartitionSpec as P

CH = 64


HIGHEST = lax.Precision.HIGHEST
EPSILON = 1e-06


def from_behind(value, axis, steps):
    count = lax.axis_size(axis)
    first, last = (max(0, -steps), min(count, count - steps))
    return lax.ppermute(value, axis, [(source, source + steps) for source in range(first, last)])


def scan_states(trans, offset, axis):
    devices, mine = (lax.axis_size(axis), lax.axis_index(axis))
    spans = []
    span = 1
    while span < devices:
        spans.append(span)
        span = span * 2
    inclusive_maps, exclusive_maps = ([], [None])
    inclusive = trans
    for span in spans[:-1]:
        pairs = [(source, source + span) for source in range(devices - span)]
        inclusive_maps.append(inclusive)
        earlier = lax.ppermute(inclusive, axis, pairs)
        last_map = exclusive_maps[-1]
        exclusive_maps.append(earlier if last_map is None else product(last_map, earlier))
        if 4 * span < devices:
            inclusive = jnp.where(mine >= span, product(inclusive, earlier), inclusive)
    state = jnp.zeros_like(offset)
    carried = offset
    for step, span in enumerate(spans):
        pairs = [(source, source + span) for source in range(devices - span)]
        earlier = lax.ppermute(carried, axis, pairs)
        last_map = exclusive_maps[step]
        state = earlier if last_map is None else state + product(last_map, earlier)
        if step + 1 < len(spans):
            carried = product(inclusive_maps[step], earlier) + carried
    return state


def expand_quantized(raw_rows, scales):
    row_count = raw_rows.shape[0]
    head_count = scales.shape[1]
    shaped = raw_rows.astype(jnp.float32).reshape(row_count, head_count, -1) * scales[:, :, None]
    return shaped.reshape(row_count, -1)


def causal_filter(window, weights):
    kernel_span = weights.shape[0]
    row_count = window.shape[0] - kernel_span + 1
    summed = jnp.zeros((row_count, window.shape[1]), jnp.float32)
    for offset_tap in range(kernel_span):
        summed = summed + window[offset_tap : offset_tap + row_count] * weights[offset_tap].astype(
            jnp.float32
        )
    return lax.optimization_barrier(jax.nn.silu(summed).astype(jnp.bfloat16))


def unit_heads(conv_rows, head_width):
    row_count = conv_rows.shape[0]
    shaped = conv_rows.astype(jnp.float32).reshape(row_count, -1, head_width)
    return shaped * lax.rsqrt(jnp.sum(shaped * shaped, axis=-1, keepdims=True) + EPSILON)


def to_blocks(array, block):
    block_count = array.shape[0] // block
    return array.reshape(block_count, block, array.shape[1], -1).transpose(0, 2, 1, 3)


def to_block_rows(array, block):
    block_count = array.shape[0] // block
    return array.reshape(block_count, block, -1).transpose(0, 2, 1)


def unit_lower_inverse(strict_part):
    length = strict_part.shape[-1]
    negated = -strict_part
    inverse = jnp.eye(length, dtype=jnp.float32) + negated
    power = negated
    span = 2
    while span < length:
        power = jnp.einsum("bhij,bhjk->bhik", power, power, precision=HIGHEST)
        inverse = inverse + jnp.einsum("bhij,bhjk->bhik", inverse, power, precision=HIGHEST)
        span = span * 2
    return inverse


def key_terms(key_units, logdec, beta_units):
    length = logdec.shape[-1]
    positions = jnp.arange(length)
    lower_incl = positions[:, None] >= positions[None, :]
    lower_strict = positions[:, None] > positions[None, :]
    cumulative = jnp.cumsum(logdec, axis=-1)
    differ = cumulative[..., :, None] - cumulative[..., None, :]
    decay_incl = jnp.where(lower_incl, jnp.exp(jnp.where(lower_incl, differ, 0.0)), 0.0)
    decay_strict = jnp.where(lower_strict, decay_incl, 0.0)
    key_gram = jnp.einsum("bhid,bhjd->bhij", key_units, key_units, precision=HIGHEST)
    inverse = unit_lower_inverse(beta_units[..., :, None] * key_gram * decay_strict)
    growth = jnp.exp(cumulative)
    weight_keys = jnp.einsum(
        "bhij,bhjd->bhid",
        inverse,
        (beta_units * growth)[..., None] * key_units,
        precision=HIGHEST,
    )
    fading = jnp.exp(cumulative[..., -1:] - cumulative)[..., None] * key_units
    eye_key = jnp.eye(key_units.shape[-1], dtype=jnp.float32)
    transition = growth[..., -1][..., None, None] * eye_key - jnp.einsum(
        "bhjd,bhje->bhde", fading, weight_keys, precision=HIGHEST
    )
    return (inverse, weight_keys, fading, transition, decay_incl, growth)


def value_terms(inverse, fading, value_units, beta_units):
    weight_values = jnp.einsum(
        "bhij,bhjd->bhid", inverse, beta_units[..., None] * value_units, precision=HIGHEST
    )
    offset = jnp.einsum("bhjd,bhje->bhde", fading, weight_values, precision=HIGHEST)
    return (weight_values, offset)


def query_terms(queries, key_units, decay_incl, growth, weight_values, weight_keys):
    mixing = decay_incl * jnp.einsum("bhid,bhjd->bhij", queries, key_units, precision=HIGHEST)
    zero_out = jnp.einsum("bhij,bhjd->bhid", mixing, weight_values, precision=HIGHEST)
    readout = growth[..., None] * queries - jnp.einsum(
        "bhij,bhjd->bhid", mixing, weight_keys, precision=HIGHEST
    )
    return (zero_out, readout)


def product(left, right):
    return jnp.einsum("hde,hef->hdf", left, right, precision=HIGHEST)


def to_rows(blocks):
    return blocks.transpose(0, 2, 1, 3).reshape(-1, blocks.shape[1], blocks.shape[3])


def gated_norm(delta_rows, gate_raw, norm_gain):
    meansq = jnp.mean(delta_rows * delta_rows, axis=-1, keepdims=True)
    normed = delta_rows * lax.rsqrt(meansq + EPSILON) * norm_gain
    gate_float = gate_raw.astype(jnp.float32).reshape(delta_rows.shape)
    return (normed * jax.nn.silu(gate_float)).reshape(delta_rows.shape[0], -1).astype(jnp.bfloat16)


def shards(
    query_raw,
    key_raw,
    value_raw,
    query_scale,
    key_block_scale,
    value_scale,
    conv_query,
    key_filter_taps,
    conv_value,
    gate_input,
    beta_logit,
    decay_base,
    step_bias,
    output_gate,
    norm_gain,
):
    head_width = norm_gain.shape[0]
    margin = conv_query.shape[0] - 1
    query_deq = expand_quantized(query_raw, query_scale)
    key_deq = expand_quantized(key_raw, key_block_scale)
    value_deq = expand_quantized(value_raw, value_scale)
    query_width, key_width = (query_deq.shape[1], key_deq.shape[1])
    tails = from_behind(
        jnp.concatenate([query_deq[-margin:], key_deq[-margin:], value_deq[-margin:]], axis=1),
        "seq",
        1,
    )
    tail_rows = (
        tails[:, :query_width],
        tails[:, query_width : query_width + key_width],
        tails[:, query_width + key_width :],
    )
    local_heads = gate_input.shape[1]
    first_head = lax.axis_index("head") * local_heads
    base_part = lax.dynamic_slice_in_dim(decay_base, first_head, local_heads)
    bias_part = lax.dynamic_slice_in_dim(step_bias, first_head, local_heads)
    key_filtered = causal_filter(jnp.concatenate([tail_rows[1], key_deq], axis=0), key_filter_taps)
    row_count = key_filtered.shape[0]
    key_rows = unit_heads(key_filtered, head_width)
    repeats = local_heads // key_rows.shape[1]
    key_units = to_blocks(jnp.repeat(key_rows, repeats, axis=1), CH)
    logdec = -jnp.exp(base_part)[None, :] * jax.nn.softplus(gate_input + bias_part[None, :])
    logdec = to_block_rows(logdec, CH)
    beta_units = to_block_rows(jax.nn.sigmoid(beta_logit), CH)
    inverse, weight_keys, fading, transition, decay_incl, growth = key_terms(
        key_units, logdec, beta_units
    )
    dev_trans = transition[0]
    trans_before = [None]
    for block in range(1, transition.shape[0]):
        trans_before.append(dev_trans)
        dev_trans = product(transition[block], dev_trans)
    value_window, _ = lax.optimization_barrier(
        (jnp.concatenate([tail_rows[2], value_deq], axis=0), dev_trans)
    )
    value_conv = causal_filter(value_window, conv_value)
    value_units = to_blocks(value_conv.astype(jnp.float32).reshape(row_count, -1, head_width), CH)
    weight_values, offset = value_terms(inverse, fading, value_units, beta_units)
    dev_offset = offset[0]
    offset_before = [None]
    for block in range(1, transition.shape[0]):
        offset_before.append(dev_offset)
        dev_offset = product(transition[block], dev_offset) + offset[block]
    query_window, _ = lax.optimization_barrier(
        (jnp.concatenate([tail_rows[0], query_deq], axis=0), dev_offset)
    )
    query_conv = causal_filter(query_window, conv_query)
    query_rows = unit_heads(query_conv, head_width) * head_width ** (-0.5)
    queries = to_blocks(jnp.repeat(query_rows, repeats, axis=1), CH)
    zero_out, readout = query_terms(
        queries, key_units, decay_incl, growth, weight_values, weight_keys
    )
    local_outs, read_maps = ([zero_out[0]], [readout[0]])
    for block in range(1, transition.shape[0]):
        read_maps.append(
            jnp.einsum("hid,hde->hie", readout[block], trans_before[block], precision=HIGHEST)
        )
        local_outs.append(
            zero_out[block]
            + jnp.einsum("hid,hde->hie", readout[block], offset_before[block], precision=HIGHEST)
        )
    incoming = scan_states(dev_trans, dev_offset, "seq")
    outputs = jnp.stack(local_outs) + jnp.einsum(
        "bhid,hde->bhie", jnp.stack(read_maps), incoming, precision=HIGHEST
    )
    gated_rows = gated_norm(to_rows(outputs), output_gate, norm_gain)
    return gated_rows


def solution(mesh):
    placed = (
        P("seq", "head"),
        P("seq", "head"),
        P("seq", "head"),
        P("seq", "head"),
        P("seq", "head"),
        P("seq", "head"),
        P(None, "head"),
        P(None, "head"),
        P(None, "head"),
        P("seq", "head"),
        P("seq", "head"),
        P(),
        P(),
        P("seq", "head"),
        P(),
    )
    return jax.shard_map(
        shards, mesh=mesh, in_specs=placed, out_specs=P("seq", "head"), check_vma=False
    )
```

```python
import jax
import jax.numpy as jnp
from jax import lax
from jax.sharding import PartitionSpec as P

CH = 64


HIGHEST = lax.Precision.HIGHEST
EPSILON = 1e-06


def from_behind(value, axis, steps):
    count = lax.axis_size(axis)
    first, last = (max(0, -steps), min(count, count - steps))
    return lax.ppermute(value, axis, [(source, source + steps) for source in range(first, last)])


def scan_states(trans, offset, axis):
    devices, mine = (lax.axis_size(axis), lax.axis_index(axis))
    width = trans.shape[-1]
    eye = jnp.eye(width, dtype=jnp.float32)
    spans = []
    span = 1
    while span < devices:
        spans.append(span)
        span = span * 2
    inclusive_map, carried = (trans, offset)
    exclusive_map, state = (None, jnp.zeros_like(offset))
    for step, span in enumerate(spans):
        pairs = [(source, source + span) for source in range(devices - span)]
        reached = jnp.where(mine >= span, 1.0, 0.0)
        if step + 1 == len(spans):
            earlier = lax.ppermute(carried.astype(jnp.bfloat16), axis, pairs)
            earlier_state = earlier.astype(jnp.float32)
            if exclusive_map is None:
                state = earlier_state
            else:
                state = state + product(exclusive_map, earlier_state)
            break
        sent = jnp.concatenate([inclusive_map - eye, carried], axis=-1).astype(jnp.bfloat16)
        earlier = lax.ppermute(sent, axis, pairs).astype(jnp.float32)
        earlier_map = earlier[..., :width] + reached * eye
        earlier_state = earlier[..., width:]
        if exclusive_map is None:
            exclusive_map, state = (earlier_map, earlier_state)
        else:
            state = state + product(exclusive_map, earlier_state)
            exclusive_map = product(exclusive_map, earlier_map)
        carried = product(inclusive_map, earlier_state) + carried
        if step + 2 < len(spans):
            inclusive_map = jnp.where(
                mine >= span, product(inclusive_map, earlier_map), inclusive_map
            )
    return state


def expand_quantized(raw_rows, scales):
    row_count = raw_rows.shape[0]
    head_count = scales.shape[1]
    shaped = raw_rows.astype(jnp.float32).reshape(row_count, head_count, -1) * scales[:, :, None]
    return shaped.reshape(row_count, -1)


def causal_filter(window, weights):
    kernel_span = weights.shape[0]
    row_count = window.shape[0] - kernel_span + 1
    summed = jnp.zeros((row_count, window.shape[1]), jnp.float32)
    for offset_tap in range(kernel_span):
        summed = summed + window[offset_tap : offset_tap + row_count] * weights[offset_tap].astype(
            jnp.float32
        )
    return lax.optimization_barrier(jax.nn.silu(summed).astype(jnp.bfloat16))


def unit_heads(conv_rows, head_width):
    row_count = conv_rows.shape[0]
    shaped = conv_rows.astype(jnp.float32).reshape(row_count, -1, head_width)
    return shaped * lax.rsqrt(jnp.sum(shaped * shaped, axis=-1, keepdims=True) + EPSILON)


def to_blocks(array, block):
    block_count = array.shape[0] // block
    return array.reshape(block_count, block, array.shape[1], -1).transpose(0, 2, 1, 3)


def to_block_rows(array, block):
    block_count = array.shape[0] // block
    return array.reshape(block_count, block, -1).transpose(0, 2, 1)


def unit_lower_inverse(strict_part):
    length = strict_part.shape[-1]
    negated = -strict_part
    inverse = jnp.eye(length, dtype=jnp.float32) + negated
    power = negated
    span = 2
    while span < length:
        power = jnp.einsum("bhij,bhjk->bhik", power, power, precision=HIGHEST)
        inverse = inverse + jnp.einsum("bhij,bhjk->bhik", inverse, power, precision=HIGHEST)
        span = span * 2
    return inverse


def key_terms(key_units, logdec, beta_units):
    length = logdec.shape[-1]
    positions = jnp.arange(length)
    lower_incl = positions[:, None] >= positions[None, :]
    lower_strict = positions[:, None] > positions[None, :]
    cumulative = jnp.cumsum(logdec, axis=-1)
    differ = cumulative[..., :, None] - cumulative[..., None, :]
    decay_incl = jnp.where(lower_incl, jnp.exp(jnp.where(lower_incl, differ, 0.0)), 0.0)
    decay_strict = jnp.where(lower_strict, decay_incl, 0.0)
    key_gram = jnp.einsum("bhid,bhjd->bhij", key_units, key_units, precision=HIGHEST)
    inverse = unit_lower_inverse(beta_units[..., :, None] * key_gram * decay_strict)
    growth = jnp.exp(cumulative)
    weight_keys = jnp.einsum(
        "bhij,bhjd->bhid",
        inverse,
        (beta_units * growth)[..., None] * key_units,
        precision=HIGHEST,
    )
    fading = jnp.exp(cumulative[..., -1:] - cumulative)[..., None] * key_units
    eye_key = jnp.eye(key_units.shape[-1], dtype=jnp.float32)
    transition = growth[..., -1][..., None, None] * eye_key - jnp.einsum(
        "bhjd,bhje->bhde", fading, weight_keys, precision=HIGHEST
    )
    return (inverse, weight_keys, fading, transition, decay_incl, growth)


def value_terms(inverse, fading, value_units, beta_units):
    weight_values = jnp.einsum(
        "bhij,bhjd->bhid", inverse, beta_units[..., None] * value_units, precision=HIGHEST
    )
    offset = jnp.einsum("bhjd,bhje->bhde", fading, weight_values, precision=HIGHEST)
    return (weight_values, offset)


def query_terms(queries, key_units, decay_incl, growth, weight_values, weight_keys):
    mixing = decay_incl * jnp.einsum("bhid,bhjd->bhij", queries, key_units, precision=HIGHEST)
    zero_out = jnp.einsum("bhij,bhjd->bhid", mixing, weight_values, precision=HIGHEST)
    readout = growth[..., None] * queries - jnp.einsum(
        "bhij,bhjd->bhid", mixing, weight_keys, precision=HIGHEST
    )
    return (zero_out, readout)


def product(left, right):
    return jnp.einsum("hde,hef->hdf", left, right, precision=HIGHEST)


def to_rows(blocks):
    return blocks.transpose(0, 2, 1, 3).reshape(-1, blocks.shape[1], blocks.shape[3])


def gated_norm(delta_rows, gate_raw, norm_gain):
    meansq = jnp.mean(delta_rows * delta_rows, axis=-1, keepdims=True)
    normed = delta_rows * lax.rsqrt(meansq + EPSILON) * norm_gain
    gate_float = gate_raw.astype(jnp.float32).reshape(delta_rows.shape)
    return (normed * jax.nn.silu(gate_float)).reshape(delta_rows.shape[0], -1).astype(jnp.bfloat16)


def shards(
    query_raw,
    key_raw,
    value_raw,
    query_scale,
    key_block_scale,
    value_scale,
    conv_query,
    key_filter_taps,
    conv_value,
    gate_input,
    beta_logit,
    decay_base,
    step_bias,
    output_gate,
    norm_gain,
):
    head_width = norm_gain.shape[0]
    margin = conv_query.shape[0] - 1
    query_deq = expand_quantized(query_raw, query_scale)
    key_deq = expand_quantized(key_raw, key_block_scale)
    value_deq = expand_quantized(value_raw, value_scale)
    query_width, key_width = (query_deq.shape[1], key_deq.shape[1])
    tails = from_behind(
        jnp.concatenate([query_deq[-margin:], key_deq[-margin:], value_deq[-margin:]], axis=1),
        "seq",
        1,
    )
    tail_rows = (
        tails[:, :query_width],
        tails[:, query_width : query_width + key_width],
        tails[:, query_width + key_width :],
    )
    local_heads = gate_input.shape[1]
    first_head = lax.axis_index("head") * local_heads
    base_part = lax.dynamic_slice_in_dim(decay_base, first_head, local_heads)
    bias_part = lax.dynamic_slice_in_dim(step_bias, first_head, local_heads)
    key_filtered = causal_filter(jnp.concatenate([tail_rows[1], key_deq], axis=0), key_filter_taps)
    row_count = key_filtered.shape[0]
    key_rows = unit_heads(key_filtered, head_width)
    repeats = local_heads // key_rows.shape[1]
    key_units = to_blocks(jnp.repeat(key_rows, repeats, axis=1), CH)
    logdec = -jnp.exp(base_part)[None, :] * jax.nn.softplus(gate_input + bias_part[None, :])
    logdec = to_block_rows(logdec, CH)
    beta_units = to_block_rows(jax.nn.sigmoid(beta_logit), CH)
    inverse, weight_keys, fading, transition, decay_incl, growth = key_terms(
        key_units, logdec, beta_units
    )
    dev_trans = transition[0]
    trans_before = [None]
    for block in range(1, transition.shape[0]):
        trans_before.append(dev_trans)
        dev_trans = product(transition[block], dev_trans)
    value_window, _ = lax.optimization_barrier(
        (jnp.concatenate([tail_rows[2], value_deq], axis=0), dev_trans)
    )
    value_conv = causal_filter(value_window, conv_value)
    value_units = to_blocks(value_conv.astype(jnp.float32).reshape(row_count, -1, head_width), CH)
    weight_values, offset = value_terms(inverse, fading, value_units, beta_units)
    dev_offset = offset[0]
    offset_before = [None]
    for block in range(1, transition.shape[0]):
        offset_before.append(dev_offset)
        dev_offset = product(transition[block], dev_offset) + offset[block]
    query_window, _ = lax.optimization_barrier(
        (jnp.concatenate([tail_rows[0], query_deq], axis=0), dev_offset)
    )
    query_conv = causal_filter(query_window, conv_query)
    query_rows = unit_heads(query_conv, head_width) * head_width ** (-0.5)
    queries = to_blocks(jnp.repeat(query_rows, repeats, axis=1), CH)
    zero_out, readout = query_terms(
        queries, key_units, decay_incl, growth, weight_values, weight_keys
    )
    local_outs, read_maps = ([zero_out[0]], [readout[0]])
    for block in range(1, transition.shape[0]):
        read_maps.append(
            jnp.einsum("hid,hde->hie", readout[block], trans_before[block], precision=HIGHEST)
        )
        local_outs.append(
            zero_out[block]
            + jnp.einsum("hid,hde->hie", readout[block], offset_before[block], precision=HIGHEST)
        )
    incoming = scan_states(dev_trans, dev_offset, "seq")
    outputs = jnp.stack(local_outs) + jnp.einsum(
        "bhid,hde->bhie", jnp.stack(read_maps), incoming, precision=HIGHEST
    )
    gated_rows = gated_norm(to_rows(outputs), output_gate, norm_gain)
    return gated_rows


def solution(mesh):
    placed = (
        P("seq", "head"),
        P("seq", "head"),
        P("seq", "head"),
        P("seq", "head"),
        P("seq", "head"),
        P("seq", "head"),
        P(None, "head"),
        P(None, "head"),
        P(None, "head"),
        P("seq", "head"),
        P("seq", "head"),
        P(),
        P(),
        P("seq", "head"),
        P(),
    )
    return jax.shard_map(
        shards, mesh=mesh, in_specs=placed, out_specs=P("seq", "head"), check_vma=False
    )
```

```python
import jax
import jax.numpy as jnp
from jax import lax
from jax.sharding import PartitionSpec as P

CH = 64


HIGHEST = lax.Precision.HIGHEST
EPSILON = 1e-06


def from_behind(value, axis, steps):
    count = lax.axis_size(axis)
    first, last = (max(0, -steps), min(count, count - steps))
    return lax.ppermute(value, axis, [(source, source + steps) for source in range(first, last)])


def scan_states(trans, offset, axis, rider, side_work):
    devices, mine = (lax.axis_size(axis), lax.axis_index(axis))
    width = trans.shape[-1]
    eye = jnp.eye(width, dtype=jnp.float32)
    spans = []
    span = 1
    while span < devices:
        spans.append(span)
        span = span * 2
    inclusive_map, carried = (trans, offset)
    exclusive_map, state = (None, jnp.zeros_like(offset))
    for step, span in enumerate(spans):
        pairs = [(source, source + span) for source in range(devices - span)]
        reached = jnp.where(mine >= span, 1.0, 0.0)
        if step + 1 == len(spans):
            sent = carried.astype(jnp.bfloat16)
            if step == 0:
                rider, sent = lax.optimization_barrier((rider, sent))
            earlier = lax.ppermute(sent, axis, pairs)
            if step == 0:
                rider = side_work(rider)
                rider, earlier = lax.optimization_barrier((rider, earlier))
            earlier_state = earlier.astype(jnp.float32)
            if exclusive_map is None:
                state = earlier_state
            else:
                state = state + product(exclusive_map, earlier_state)
            break
        sent = jnp.concatenate([inclusive_map - eye, carried], axis=-1).astype(jnp.bfloat16)
        if step == 0:
            rider, sent = lax.optimization_barrier((rider, sent))
        earlier = lax.ppermute(sent, axis, pairs)
        if step == 0:
            rider = side_work(rider)
            rider, earlier = lax.optimization_barrier((rider, earlier))
        earlier = earlier.astype(jnp.float32)
        earlier_map = earlier[..., :width] + reached * eye
        earlier_state = earlier[..., width:]
        if exclusive_map is None:
            exclusive_map, state = (earlier_map, earlier_state)
        else:
            state = state + product(exclusive_map, earlier_state)
            exclusive_map = product(exclusive_map, earlier_map)
        carried = product(inclusive_map, earlier_state) + carried
        if step + 2 < len(spans):
            inclusive_map = jnp.where(
                mine >= span, product(inclusive_map, earlier_map), inclusive_map
            )
    return (state, rider)


def expand_quantized(raw_rows, scales):
    row_count = raw_rows.shape[0]
    head_count = scales.shape[1]
    shaped = raw_rows.astype(jnp.float32).reshape(row_count, head_count, -1) * scales[:, :, None]
    return shaped.reshape(row_count, -1)


def causal_filter(window, weights):
    kernel_span = weights.shape[0]
    row_count = window.shape[0] - kernel_span + 1
    summed = jnp.zeros((row_count, window.shape[1]), jnp.float32)
    for offset_tap in range(kernel_span):
        summed = summed + window[offset_tap : offset_tap + row_count] * weights[offset_tap].astype(
            jnp.float32
        )
    return lax.optimization_barrier(jax.nn.silu(summed).astype(jnp.bfloat16))


def unit_heads(conv_rows, head_width):
    row_count = conv_rows.shape[0]
    shaped = conv_rows.astype(jnp.float32).reshape(row_count, -1, head_width)
    return shaped * lax.rsqrt(jnp.sum(shaped * shaped, axis=-1, keepdims=True) + EPSILON)


def to_blocks(array, block):
    block_count = array.shape[0] // block
    return array.reshape(block_count, block, array.shape[1], -1).transpose(0, 2, 1, 3)


def to_block_rows(array, block):
    block_count = array.shape[0] // block
    return array.reshape(block_count, block, -1).transpose(0, 2, 1)


def unit_lower_inverse(strict_part):
    length = strict_part.shape[-1]
    negated = -strict_part
    inverse = jnp.eye(length, dtype=jnp.float32) + negated
    power = negated
    span = 2
    while span < length:
        power = jnp.einsum("bhij,bhjk->bhik", power, power, precision=HIGHEST)
        inverse = inverse + jnp.einsum("bhij,bhjk->bhik", inverse, power, precision=HIGHEST)
        span = span * 2
    return inverse


def key_terms(key_units, logdec, beta_units):
    length = logdec.shape[-1]
    positions = jnp.arange(length)
    lower_incl = positions[:, None] >= positions[None, :]
    lower_strict = positions[:, None] > positions[None, :]
    cumulative = jnp.cumsum(logdec, axis=-1)
    differ = cumulative[..., :, None] - cumulative[..., None, :]
    decay_incl = jnp.where(lower_incl, jnp.exp(jnp.where(lower_incl, differ, 0.0)), 0.0)
    decay_strict = jnp.where(lower_strict, decay_incl, 0.0)
    key_gram = jnp.einsum("bhid,bhjd->bhij", key_units, key_units, precision=HIGHEST)
    inverse = unit_lower_inverse(beta_units[..., :, None] * key_gram * decay_strict)
    growth = jnp.exp(cumulative)
    weight_keys = jnp.einsum(
        "bhij,bhjd->bhid",
        inverse,
        (beta_units * growth)[..., None] * key_units,
        precision=HIGHEST,
    )
    fading = jnp.exp(cumulative[..., -1:] - cumulative)[..., None] * key_units
    eye_key = jnp.eye(key_units.shape[-1], dtype=jnp.float32)
    transition = growth[..., -1][..., None, None] * eye_key - jnp.einsum(
        "bhjd,bhje->bhde", fading, weight_keys, precision=HIGHEST
    )
    return (inverse, weight_keys, fading, transition, decay_incl, growth)


def value_terms(inverse, fading, value_units, beta_units):
    weight_values = jnp.einsum(
        "bhij,bhjd->bhid", inverse, beta_units[..., None] * value_units, precision=HIGHEST
    )
    offset = jnp.einsum("bhjd,bhje->bhde", fading, weight_values, precision=HIGHEST)
    return (weight_values, offset)


def query_terms(queries, key_units, decay_incl, growth, weight_values, weight_keys):
    mixing = decay_incl * jnp.einsum("bhid,bhjd->bhij", queries, key_units, precision=HIGHEST)
    zero_out = jnp.einsum("bhij,bhjd->bhid", mixing, weight_values, precision=HIGHEST)
    readout = growth[..., None] * queries - jnp.einsum(
        "bhij,bhjd->bhid", mixing, weight_keys, precision=HIGHEST
    )
    return (zero_out, readout)


def product(left, right):
    return jnp.einsum("hde,hef->hdf", left, right, precision=HIGHEST)


def to_rows(blocks):
    return blocks.transpose(0, 2, 1, 3).reshape(-1, blocks.shape[1], blocks.shape[3])


def gated_norm(delta_rows, gate_raw, norm_gain):
    meansq = jnp.mean(delta_rows * delta_rows, axis=-1, keepdims=True)
    normed = delta_rows * lax.rsqrt(meansq + EPSILON) * norm_gain
    gate_float = gate_raw.astype(jnp.float32).reshape(delta_rows.shape)
    return (normed * jax.nn.silu(gate_float)).reshape(delta_rows.shape[0], -1).astype(jnp.bfloat16)


def shards(
    query_raw,
    key_raw,
    value_raw,
    query_scale,
    key_block_scale,
    value_scale,
    conv_query,
    key_filter_taps,
    conv_value,
    gate_input,
    beta_logit,
    decay_base,
    step_bias,
    output_gate,
    norm_gain,
):
    head_width = norm_gain.shape[0]
    margin = conv_query.shape[0] - 1
    query_deq = expand_quantized(query_raw, query_scale)
    key_deq = expand_quantized(key_raw, key_block_scale)
    value_deq = expand_quantized(value_raw, value_scale)
    query_width, key_width = (query_deq.shape[1], key_deq.shape[1])
    tails = from_behind(
        jnp.concatenate([query_deq[-margin:], key_deq[-margin:], value_deq[-margin:]], axis=1),
        "seq",
        1,
    )
    tail_rows = (
        tails[:, :query_width],
        tails[:, query_width : query_width + key_width],
        tails[:, query_width + key_width :],
    )
    local_heads = gate_input.shape[1]
    first_head = lax.axis_index("head") * local_heads
    base_part = lax.dynamic_slice_in_dim(decay_base, first_head, local_heads)
    bias_part = lax.dynamic_slice_in_dim(step_bias, first_head, local_heads)
    key_filtered = causal_filter(jnp.concatenate([tail_rows[1], key_deq], axis=0), key_filter_taps)
    row_count = key_filtered.shape[0]
    key_rows = unit_heads(key_filtered, head_width)
    repeats = local_heads // key_rows.shape[1]
    key_units = to_blocks(jnp.repeat(key_rows, repeats, axis=1), CH)
    logdec = -jnp.exp(base_part)[None, :] * jax.nn.softplus(gate_input + bias_part[None, :])
    logdec = to_block_rows(logdec, CH)
    beta_units = to_block_rows(jax.nn.sigmoid(beta_logit), CH)
    inverse, weight_keys, fading, transition, decay_incl, growth = key_terms(
        key_units, logdec, beta_units
    )
    dev_trans = transition[0]
    trans_before = [None]
    for block in range(1, transition.shape[0]):
        trans_before.append(dev_trans)
        dev_trans = product(transition[block], dev_trans)
    value_window, _ = lax.optimization_barrier(
        (jnp.concatenate([tail_rows[2], value_deq], axis=0), dev_trans)
    )
    value_conv = causal_filter(value_window, conv_value)
    value_units = to_blocks(value_conv.astype(jnp.float32).reshape(row_count, -1, head_width), CH)
    weight_values, offset = value_terms(inverse, fading, value_units, beta_units)
    dev_offset = offset[0]
    offset_before = [None]
    for block in range(1, transition.shape[0]):
        offset_before.append(dev_offset)
        dev_offset = product(transition[block], dev_offset) + offset[block]

    def query_side(query_window):
        query_conv = causal_filter(query_window, conv_query)
        query_rows = unit_heads(query_conv, head_width) * head_width ** (-0.5)
        queries = to_blocks(jnp.repeat(query_rows, repeats, axis=1), CH)
        zero_out, readout = query_terms(
            queries, key_units, decay_incl, growth, weight_values, weight_keys
        )
        local_outs, read_maps = ([zero_out[0]], [readout[0]])
        for block in range(1, transition.shape[0]):
            read_maps.append(
                jnp.einsum("hid,hde->hie", readout[block], trans_before[block], precision=HIGHEST)
            )
            local_outs.append(
                zero_out[block]
                + jnp.einsum(
                    "hid,hde->hie", readout[block], offset_before[block], precision=HIGHEST
                )
            )
        return (local_outs, read_maps)

    incoming, (local_outs, read_maps) = scan_states(
        dev_trans,
        dev_offset,
        "seq",
        jnp.concatenate([tail_rows[0], query_deq], axis=0),
        query_side,
    )
    outputs = jnp.stack(local_outs) + jnp.einsum(
        "bhid,hde->bhie", jnp.stack(read_maps), incoming, precision=HIGHEST
    )
    gated_rows = gated_norm(to_rows(outputs), output_gate, norm_gain)
    return gated_rows


def solution(mesh):
    placed = (
        P("seq", "head"),
        P("seq", "head"),
        P("seq", "head"),
        P("seq", "head"),
        P("seq", "head"),
        P("seq", "head"),
        P(None, "head"),
        P(None, "head"),
        P(None, "head"),
        P("seq", "head"),
        P("seq", "head"),
        P(),
        P(),
        P("seq", "head"),
        P(),
    )
    return jax.shard_map(
        shards, mesh=mesh, in_specs=placed, out_specs=P("seq", "head"), check_vma=False
    )
```

```python
import jax
import jax.numpy as jnp
from jax import lax
from jax.sharding import PartitionSpec as P

CH = 64


HIGHEST = lax.Precision.HIGHEST
EPSILON = 1e-06


def from_behind(value, axis, steps):
    count = lax.axis_size(axis)
    first, last = (max(0, -steps), min(count, count - steps))
    return lax.ppermute(value, axis, [(source, source + steps) for source in range(first, last)])


def scan_states(trans, offset, axis):
    devices, mine = (lax.axis_size(axis), lax.axis_index(axis))
    spans = []
    span = 1
    while span < devices:
        spans.append(span)
        span = span * 2
    eye = jnp.eye(trans.shape[-1], dtype=jnp.float32)
    inclusive_maps, exclusive_maps = ([], [None])
    inclusive = trans
    for span in spans[:-1]:
        pairs = [(source, source + span) for source in range(devices - span)]
        inclusive_maps.append(inclusive)
        reached = jnp.where(mine >= span, 1.0, 0.0)
        earlier = lax.ppermute((inclusive - eye).astype(jnp.bfloat16), axis, pairs)
        earlier = earlier.astype(jnp.float32) + reached * eye
        last_map = exclusive_maps[-1]
        exclusive_maps.append(earlier if last_map is None else product(last_map, earlier))
        if 4 * span < devices:
            inclusive = jnp.where(mine >= span, product(inclusive, earlier), inclusive)
    state = jnp.zeros_like(offset)
    carried = offset
    for step, span in enumerate(spans):
        pairs = [(source, source + span) for source in range(devices - span)]
        earlier = lax.ppermute(carried.astype(jnp.bfloat16), axis, pairs).astype(jnp.float32)
        last_map = exclusive_maps[step]
        state = earlier if last_map is None else state + product(last_map, earlier)
        if step + 1 < len(spans):
            carried = product(inclusive_maps[step], earlier) + carried
    return state


def expand_quantized(raw_rows, scales):
    row_count = raw_rows.shape[0]
    head_count = scales.shape[1]
    shaped = raw_rows.astype(jnp.float32).reshape(row_count, head_count, -1) * scales[:, :, None]
    return shaped.reshape(row_count, -1)


def causal_filter(window, weights):
    kernel_span = weights.shape[0]
    row_count = window.shape[0] - kernel_span + 1
    summed = jnp.zeros((row_count, window.shape[1]), jnp.float32)
    for offset_tap in range(kernel_span):
        summed = summed + window[offset_tap : offset_tap + row_count] * weights[offset_tap].astype(
            jnp.float32
        )
    return lax.optimization_barrier(jax.nn.silu(summed).astype(jnp.bfloat16))


def unit_heads(conv_rows, head_width):
    row_count = conv_rows.shape[0]
    shaped = conv_rows.astype(jnp.float32).reshape(row_count, -1, head_width)
    return shaped * lax.rsqrt(jnp.sum(shaped * shaped, axis=-1, keepdims=True) + EPSILON)


def to_blocks(array, block):
    block_count = array.shape[0] // block
    return array.reshape(block_count, block, array.shape[1], -1).transpose(0, 2, 1, 3)


def to_block_rows(array, block):
    block_count = array.shape[0] // block
    return array.reshape(block_count, block, -1).transpose(0, 2, 1)


def unit_lower_inverse(strict_part):
    length = strict_part.shape[-1]
    negated = -strict_part
    inverse = jnp.eye(length, dtype=jnp.float32) + negated
    power = negated
    span = 2
    while span < length:
        power = jnp.einsum("bhij,bhjk->bhik", power, power, precision=HIGHEST)
        inverse = inverse + jnp.einsum("bhij,bhjk->bhik", inverse, power, precision=HIGHEST)
        span = span * 2
    return inverse


def key_terms(key_units, logdec, beta_units):
    length = logdec.shape[-1]
    positions = jnp.arange(length)
    lower_incl = positions[:, None] >= positions[None, :]
    lower_strict = positions[:, None] > positions[None, :]
    cumulative = jnp.cumsum(logdec, axis=-1)
    differ = cumulative[..., :, None] - cumulative[..., None, :]
    decay_incl = jnp.where(lower_incl, jnp.exp(jnp.where(lower_incl, differ, 0.0)), 0.0)
    decay_strict = jnp.where(lower_strict, decay_incl, 0.0)
    key_gram = jnp.einsum("bhid,bhjd->bhij", key_units, key_units, precision=HIGHEST)
    inverse = unit_lower_inverse(beta_units[..., :, None] * key_gram * decay_strict)
    growth = jnp.exp(cumulative)
    weight_keys = jnp.einsum(
        "bhij,bhjd->bhid",
        inverse,
        (beta_units * growth)[..., None] * key_units,
        precision=HIGHEST,
    )
    fading = jnp.exp(cumulative[..., -1:] - cumulative)[..., None] * key_units
    eye_key = jnp.eye(key_units.shape[-1], dtype=jnp.float32)
    transition = growth[..., -1][..., None, None] * eye_key - jnp.einsum(
        "bhjd,bhje->bhde", fading, weight_keys, precision=HIGHEST
    )
    return (inverse, weight_keys, fading, transition, decay_incl, growth)


def value_terms(inverse, fading, value_units, beta_units):
    weight_values = jnp.einsum(
        "bhij,bhjd->bhid", inverse, beta_units[..., None] * value_units, precision=HIGHEST
    )
    offset = jnp.einsum("bhjd,bhje->bhde", fading, weight_values, precision=HIGHEST)
    return (weight_values, offset)


def query_terms(queries, key_units, decay_incl, growth, weight_values, weight_keys):
    mixing = decay_incl * jnp.einsum("bhid,bhjd->bhij", queries, key_units, precision=HIGHEST)
    zero_out = jnp.einsum("bhij,bhjd->bhid", mixing, weight_values, precision=HIGHEST)
    readout = growth[..., None] * queries - jnp.einsum(
        "bhij,bhjd->bhid", mixing, weight_keys, precision=HIGHEST
    )
    return (zero_out, readout)


def product(left, right):
    return jnp.einsum("hde,hef->hdf", left, right, precision=HIGHEST)


def to_rows(blocks):
    return blocks.transpose(0, 2, 1, 3).reshape(-1, blocks.shape[1], blocks.shape[3])


def gated_norm(delta_rows, gate_raw, norm_gain):
    meansq = jnp.mean(delta_rows * delta_rows, axis=-1, keepdims=True)
    normed = delta_rows * lax.rsqrt(meansq + EPSILON) * norm_gain
    gate_float = gate_raw.astype(jnp.float32).reshape(delta_rows.shape)
    return (normed * jax.nn.silu(gate_float)).reshape(delta_rows.shape[0], -1).astype(jnp.bfloat16)


def shards(
    query_raw,
    key_raw,
    value_raw,
    query_scale,
    key_block_scale,
    value_scale,
    conv_query,
    key_filter_taps,
    conv_value,
    gate_input,
    beta_logit,
    decay_base,
    step_bias,
    output_gate,
    norm_gain,
):
    head_width = norm_gain.shape[0]
    margin = conv_query.shape[0] - 1
    query_deq = expand_quantized(query_raw, query_scale)
    key_deq = expand_quantized(key_raw, key_block_scale)
    value_deq = expand_quantized(value_raw, value_scale)
    query_width, key_width = (query_deq.shape[1], key_deq.shape[1])
    tails = from_behind(
        jnp.concatenate([query_deq[-margin:], key_deq[-margin:], value_deq[-margin:]], axis=1),
        "seq",
        1,
    )
    tail_rows = (
        tails[:, :query_width],
        tails[:, query_width : query_width + key_width],
        tails[:, query_width + key_width :],
    )
    local_heads = gate_input.shape[1]
    first_head = lax.axis_index("head") * local_heads
    base_part = lax.dynamic_slice_in_dim(decay_base, first_head, local_heads)
    bias_part = lax.dynamic_slice_in_dim(step_bias, first_head, local_heads)
    key_filtered = causal_filter(jnp.concatenate([tail_rows[1], key_deq], axis=0), key_filter_taps)
    row_count = key_filtered.shape[0]
    key_rows = unit_heads(key_filtered, head_width)
    repeats = local_heads // key_rows.shape[1]
    key_units = to_blocks(jnp.repeat(key_rows, repeats, axis=1), CH)
    logdec = -jnp.exp(base_part)[None, :] * jax.nn.softplus(gate_input + bias_part[None, :])
    logdec = to_block_rows(logdec, CH)
    beta_units = to_block_rows(jax.nn.sigmoid(beta_logit), CH)
    inverse, weight_keys, fading, transition, decay_incl, growth = key_terms(
        key_units, logdec, beta_units
    )
    dev_trans = transition[0]
    trans_before = [None]
    for block in range(1, transition.shape[0]):
        trans_before.append(dev_trans)
        dev_trans = product(transition[block], dev_trans)
    value_window, _ = lax.optimization_barrier(
        (jnp.concatenate([tail_rows[2], value_deq], axis=0), dev_trans)
    )
    value_conv = causal_filter(value_window, conv_value)
    value_units = to_blocks(value_conv.astype(jnp.float32).reshape(row_count, -1, head_width), CH)
    weight_values, offset = value_terms(inverse, fading, value_units, beta_units)
    dev_offset = offset[0]
    offset_before = [None]
    for block in range(1, transition.shape[0]):
        offset_before.append(dev_offset)
        dev_offset = product(transition[block], dev_offset) + offset[block]
    query_window, _ = lax.optimization_barrier(
        (jnp.concatenate([tail_rows[0], query_deq], axis=0), dev_offset)
    )
    query_conv = causal_filter(query_window, conv_query)
    query_rows = unit_heads(query_conv, head_width) * head_width ** (-0.5)
    queries = to_blocks(jnp.repeat(query_rows, repeats, axis=1), CH)
    zero_out, readout = query_terms(
        queries, key_units, decay_incl, growth, weight_values, weight_keys
    )
    local_outs, read_maps = ([zero_out[0]], [readout[0]])
    for block in range(1, transition.shape[0]):
        read_maps.append(
            jnp.einsum("hid,hde->hie", readout[block], trans_before[block], precision=HIGHEST)
        )
        local_outs.append(
            zero_out[block]
            + jnp.einsum("hid,hde->hie", readout[block], offset_before[block], precision=HIGHEST)
        )
    incoming = scan_states(dev_trans, dev_offset, "seq")
    outputs = jnp.stack(local_outs) + jnp.einsum(
        "bhid,hde->bhie", jnp.stack(read_maps), incoming, precision=HIGHEST
    )
    gated_rows = gated_norm(to_rows(outputs), output_gate, norm_gain)
    return gated_rows


def solution(mesh):
    placed = (
        P("seq", "head"),
        P("seq", "head"),
        P("seq", "head"),
        P("seq", "head"),
        P("seq", "head"),
        P("seq", "head"),
        P(None, "head"),
        P(None, "head"),
        P(None, "head"),
        P("seq", "head"),
        P("seq", "head"),
        P(),
        P(),
        P("seq", "head"),
        P(),
    )
    return jax.shard_map(
        shards, mesh=mesh, in_specs=placed, out_specs=P("seq", "head"), check_vma=False
    )
```

```python
import jax
import jax.numpy as jnp
from jax import lax
from jax.sharding import PartitionSpec as P

CH = 64


HIGHEST = lax.Precision.HIGHEST
EPSILON = 1e-06


def from_behind(value, axis, steps):
    count = lax.axis_size(axis)
    first, last = (max(0, -steps), min(count, count - steps))
    return lax.ppermute(value, axis, [(source, source + steps) for source in range(first, last)])


def scan_states(trans, offset, axis, rider):
    devices, mine = (lax.axis_size(axis), lax.axis_index(axis))
    spans = []
    span = 1
    while span < devices:
        spans.append(span)
        span = span * 2
    eye = jnp.eye(trans.shape[-1], dtype=jnp.float32)
    inclusive_maps, exclusive_maps = ([], [None])
    inclusive = trans
    for span in spans[:-1]:
        pairs = [(source, source + span) for source in range(devices - span)]
        inclusive_maps.append(inclusive)
        reached = jnp.where(mine >= span, 1.0, 0.0)
        earlier = lax.ppermute((inclusive - eye).astype(jnp.bfloat16), axis, pairs)
        if span == 1:
            rider, earlier = lax.optimization_barrier((rider, earlier))
        earlier = earlier.astype(jnp.float32) + reached * eye
        last_map = exclusive_maps[-1]
        exclusive_maps.append(earlier if last_map is None else product(last_map, earlier))
        if 4 * span < devices:
            inclusive = jnp.where(mine >= span, product(inclusive, earlier), inclusive)
    state = jnp.zeros_like(offset)
    carried = offset
    for step, span in enumerate(spans):
        pairs = [(source, source + span) for source in range(devices - span)]
        earlier = lax.ppermute(carried.astype(jnp.bfloat16), axis, pairs)
        if devices == 2:
            rider, earlier = lax.optimization_barrier((rider, earlier))
        earlier = earlier.astype(jnp.float32)
        last_map = exclusive_maps[step]
        state = earlier if last_map is None else state + product(last_map, earlier)
        if step + 1 < len(spans):
            carried = product(inclusive_maps[step], earlier) + carried
    return (state, rider)


def expand_quantized(raw_rows, scales):
    row_count = raw_rows.shape[0]
    head_count = scales.shape[1]
    shaped = raw_rows.astype(jnp.float32).reshape(row_count, head_count, -1) * scales[:, :, None]
    return shaped.reshape(row_count, -1)


def causal_filter(window, weights):
    kernel_span = weights.shape[0]
    row_count = window.shape[0] - kernel_span + 1
    summed = jnp.zeros((row_count, window.shape[1]), jnp.float32)
    for offset_tap in range(kernel_span):
        summed = summed + window[offset_tap : offset_tap + row_count] * weights[offset_tap].astype(
            jnp.float32
        )
    return lax.optimization_barrier(jax.nn.silu(summed).astype(jnp.bfloat16))


def unit_heads(conv_rows, head_width):
    row_count = conv_rows.shape[0]
    shaped = conv_rows.astype(jnp.float32).reshape(row_count, -1, head_width)
    return shaped * lax.rsqrt(jnp.sum(shaped * shaped, axis=-1, keepdims=True) + EPSILON)


def to_blocks(array, block):
    block_count = array.shape[0] // block
    return array.reshape(block_count, block, array.shape[1], -1).transpose(0, 2, 1, 3)


def to_block_rows(array, block):
    block_count = array.shape[0] // block
    return array.reshape(block_count, block, -1).transpose(0, 2, 1)


def unit_lower_inverse(strict_part):
    length = strict_part.shape[-1]
    negated = -strict_part
    inverse = jnp.eye(length, dtype=jnp.float32) + negated
    power = negated
    span = 2
    while span < length:
        power = jnp.einsum("bhij,bhjk->bhik", power, power, precision=HIGHEST)
        inverse = inverse + jnp.einsum("bhij,bhjk->bhik", inverse, power, precision=HIGHEST)
        span = span * 2
    return inverse


def key_terms(key_units, logdec, beta_units):
    length = logdec.shape[-1]
    positions = jnp.arange(length)
    lower_incl = positions[:, None] >= positions[None, :]
    lower_strict = positions[:, None] > positions[None, :]
    cumulative = jnp.cumsum(logdec, axis=-1)
    differ = cumulative[..., :, None] - cumulative[..., None, :]
    decay_incl = jnp.where(lower_incl, jnp.exp(jnp.where(lower_incl, differ, 0.0)), 0.0)
    decay_strict = jnp.where(lower_strict, decay_incl, 0.0)
    key_gram = jnp.einsum("bhid,bhjd->bhij", key_units, key_units, precision=HIGHEST)
    inverse = unit_lower_inverse(beta_units[..., :, None] * key_gram * decay_strict)
    growth = jnp.exp(cumulative)
    weight_keys = jnp.einsum(
        "bhij,bhjd->bhid",
        inverse,
        (beta_units * growth)[..., None] * key_units,
        precision=HIGHEST,
    )
    fading = jnp.exp(cumulative[..., -1:] - cumulative)[..., None] * key_units
    eye_key = jnp.eye(key_units.shape[-1], dtype=jnp.float32)
    transition = growth[..., -1][..., None, None] * eye_key - jnp.einsum(
        "bhjd,bhje->bhde", fading, weight_keys, precision=HIGHEST
    )
    return (inverse, weight_keys, fading, transition, decay_incl, growth)


def value_terms(inverse, fading, value_units, beta_units):
    weight_values = jnp.einsum(
        "bhij,bhjd->bhid", inverse, beta_units[..., None] * value_units, precision=HIGHEST
    )
    offset = jnp.einsum("bhjd,bhje->bhde", fading, weight_values, precision=HIGHEST)
    return (weight_values, offset)


def query_terms(queries, key_units, decay_incl, growth, weight_values, weight_keys):
    mixing = decay_incl * jnp.einsum("bhid,bhjd->bhij", queries, key_units, precision=HIGHEST)
    zero_out = jnp.einsum("bhij,bhjd->bhid", mixing, weight_values, precision=HIGHEST)
    readout = growth[..., None] * queries - jnp.einsum(
        "bhij,bhjd->bhid", mixing, weight_keys, precision=HIGHEST
    )
    return (zero_out, readout)


def product(left, right):
    return jnp.einsum("hde,hef->hdf", left, right, precision=HIGHEST)


def to_rows(blocks):
    return blocks.transpose(0, 2, 1, 3).reshape(-1, blocks.shape[1], blocks.shape[3])


def gated_norm(delta_rows, gate_raw, norm_gain):
    meansq = jnp.mean(delta_rows * delta_rows, axis=-1, keepdims=True)
    normed = delta_rows * lax.rsqrt(meansq + EPSILON) * norm_gain
    gate_float = gate_raw.astype(jnp.float32).reshape(delta_rows.shape)
    return (normed * jax.nn.silu(gate_float)).reshape(delta_rows.shape[0], -1).astype(jnp.bfloat16)


def shards(
    query_raw,
    key_raw,
    value_raw,
    query_scale,
    key_block_scale,
    value_scale,
    conv_query,
    key_filter_taps,
    conv_value,
    gate_input,
    beta_logit,
    decay_base,
    step_bias,
    output_gate,
    norm_gain,
):
    head_width = norm_gain.shape[0]
    margin = conv_query.shape[0] - 1
    query_deq = expand_quantized(query_raw, query_scale)
    key_deq = expand_quantized(key_raw, key_block_scale)
    value_deq = expand_quantized(value_raw, value_scale)
    query_width, key_width = (query_deq.shape[1], key_deq.shape[1])
    tails = from_behind(
        jnp.concatenate([query_deq[-margin:], key_deq[-margin:], value_deq[-margin:]], axis=1),
        "seq",
        1,
    )
    tail_rows = (
        tails[:, :query_width],
        tails[:, query_width : query_width + key_width],
        tails[:, query_width + key_width :],
    )
    local_heads = gate_input.shape[1]
    first_head = lax.axis_index("head") * local_heads
    base_part = lax.dynamic_slice_in_dim(decay_base, first_head, local_heads)
    bias_part = lax.dynamic_slice_in_dim(step_bias, first_head, local_heads)
    key_filtered = causal_filter(jnp.concatenate([tail_rows[1], key_deq], axis=0), key_filter_taps)
    row_count = key_filtered.shape[0]
    key_rows = unit_heads(key_filtered, head_width)
    repeats = local_heads // key_rows.shape[1]
    key_units = to_blocks(jnp.repeat(key_rows, repeats, axis=1), CH)
    logdec = -jnp.exp(base_part)[None, :] * jax.nn.softplus(gate_input + bias_part[None, :])
    logdec = to_block_rows(logdec, CH)
    beta_units = to_block_rows(jax.nn.sigmoid(beta_logit), CH)
    inverse, weight_keys, fading, transition, decay_incl, growth = key_terms(
        key_units, logdec, beta_units
    )
    dev_trans = transition[0]
    trans_before = [None]
    for block in range(1, transition.shape[0]):
        trans_before.append(dev_trans)
        dev_trans = product(transition[block], dev_trans)
    value_window, _ = lax.optimization_barrier(
        (jnp.concatenate([tail_rows[2], value_deq], axis=0), dev_trans)
    )
    value_conv = causal_filter(value_window, conv_value)
    value_units = to_blocks(value_conv.astype(jnp.float32).reshape(row_count, -1, head_width), CH)
    weight_values, offset = value_terms(inverse, fading, value_units, beta_units)
    dev_offset = offset[0]
    offset_before = [None]
    for block in range(1, transition.shape[0]):
        offset_before.append(dev_offset)
        dev_offset = product(transition[block], dev_offset) + offset[block]
    incoming, query_window = scan_states(
        dev_trans, dev_offset, "seq", jnp.concatenate([tail_rows[0], query_deq], axis=0)
    )
    query_conv = causal_filter(query_window, conv_query)
    query_rows = unit_heads(query_conv, head_width) * head_width ** (-0.5)
    queries = to_blocks(jnp.repeat(query_rows, repeats, axis=1), CH)
    zero_out, readout = query_terms(
        queries, key_units, decay_incl, growth, weight_values, weight_keys
    )
    local_outs, read_maps = ([zero_out[0]], [readout[0]])
    for block in range(1, transition.shape[0]):
        read_maps.append(
            jnp.einsum("hid,hde->hie", readout[block], trans_before[block], precision=HIGHEST)
        )
        local_outs.append(
            zero_out[block]
            + jnp.einsum("hid,hde->hie", readout[block], offset_before[block], precision=HIGHEST)
        )
    outputs = jnp.stack(local_outs) + jnp.einsum(
        "bhid,hde->bhie", jnp.stack(read_maps), incoming, precision=HIGHEST
    )
    gated_rows = gated_norm(to_rows(outputs), output_gate, norm_gain)
    return gated_rows


def solution(mesh):
    placed = (
        P("seq", "head"),
        P("seq", "head"),
        P("seq", "head"),
        P("seq", "head"),
        P("seq", "head"),
        P("seq", "head"),
        P(None, "head"),
        P(None, "head"),
        P(None, "head"),
        P("seq", "head"),
        P("seq", "head"),
        P(),
        P(),
        P("seq", "head"),
        P(),
    )
    return jax.shard_map(
        shards, mesh=mesh, in_specs=placed, out_specs=P("seq", "head"), check_vma=False
    )
```

```python
import jax
import jax.numpy as jnp
from jax import lax
from jax.sharding import PartitionSpec as P

CH = 64


HIGHEST = lax.Precision.HIGHEST
EPSILON = 1e-06


def from_behind(value, axis, steps):
    count = lax.axis_size(axis)
    first, last = (max(0, -steps), min(count, count - steps))
    return lax.ppermute(value, axis, [(source, source + steps) for source in range(first, last)])


def scan_states(trans, offset, axis):
    devices, mine = (lax.axis_size(axis), lax.axis_index(axis))
    spans = []
    span = 1
    while span < devices:
        spans.append(span)
        span = span * 2
    eye = jnp.eye(trans.shape[-1], dtype=jnp.float32)
    inclusive_maps, exclusive_maps = ([], [None])
    inclusive = trans
    for span in spans[:-1]:
        pairs = [(source, source + span) for source in range(devices - span)]
        inclusive_maps.append(inclusive)
        reached = jnp.where(mine >= span, 1.0, 0.0)
        earlier = lax.ppermute((inclusive - eye).astype(jnp.bfloat16), axis, pairs)
        earlier = earlier.astype(jnp.float32) + reached * eye
        last_map = exclusive_maps[-1]
        if last_map is None or 4 * span >= devices:
            exclusive_maps.append(earlier if last_map is None else product(last_map, earlier))
            if 4 * span < devices:
                inclusive = jnp.where(mine >= span, product(inclusive, earlier), inclusive)
        else:
            both = jnp.einsum(
                "shde,hef->shdf", jnp.stack([last_map, inclusive]), earlier, precision=HIGHEST
            )
            exclusive_maps.append(both[0])
            inclusive = jnp.where(mine >= span, both[1], inclusive)
    state = jnp.zeros_like(offset)
    carried = offset
    for step, span in enumerate(spans):
        pairs = [(source, source + span) for source in range(devices - span)]
        earlier = lax.ppermute(carried.astype(jnp.bfloat16), axis, pairs).astype(jnp.float32)
        last_map = exclusive_maps[step]
        if last_map is None:
            state = earlier
            if step + 1 < len(spans):
                carried = product(inclusive_maps[step], earlier) + carried
        elif step + 1 < len(spans):
            both = jnp.einsum(
                "shde,hef->shdf",
                jnp.stack([last_map, inclusive_maps[step]]),
                earlier,
                precision=HIGHEST,
            )
            state = state + both[0]
            carried = both[1] + carried
        else:
            state = state + product(last_map, earlier)
    return state


def expand_quantized(raw_rows, scales):
    row_count = raw_rows.shape[0]
    head_count = scales.shape[1]
    shaped = raw_rows.astype(jnp.float32).reshape(row_count, head_count, -1) * scales[:, :, None]
    return shaped.reshape(row_count, -1)


def causal_filter(window, weights):
    kernel_span = weights.shape[0]
    row_count = window.shape[0] - kernel_span + 1
    summed = jnp.zeros((row_count, window.shape[1]), jnp.float32)
    for offset_tap in range(kernel_span):
        summed = summed + window[offset_tap : offset_tap + row_count] * weights[offset_tap].astype(
            jnp.float32
        )
    return lax.optimization_barrier(jax.nn.silu(summed).astype(jnp.bfloat16))


def unit_heads(conv_rows, head_width):
    row_count = conv_rows.shape[0]
    shaped = conv_rows.astype(jnp.float32).reshape(row_count, -1, head_width)
    return shaped * lax.rsqrt(jnp.sum(shaped * shaped, axis=-1, keepdims=True) + EPSILON)


def to_blocks(array, block):
    block_count = array.shape[0] // block
    return array.reshape(block_count, block, array.shape[1], -1).transpose(0, 2, 1, 3)


def to_block_rows(array, block):
    block_count = array.shape[0] // block
    return array.reshape(block_count, block, -1).transpose(0, 2, 1)


def unit_lower_inverse(strict_part):
    length = strict_part.shape[-1]
    eye = jnp.eye(length, dtype=jnp.float32)
    power = -strict_part
    inverse = eye + power
    span = 2
    if span < length:
        power = jnp.einsum("bhij,bhjk->bhik", power, power, precision=HIGHEST)
    while span < length:
        if 2 * span < length:
            both = jnp.einsum(
                "sbhij,sbhjk->sbhik",
                jnp.stack([inverse, power]),
                jnp.stack([eye + power, power]),
                precision=HIGHEST,
            )
            inverse, power = (both[0], both[1])
        else:
            inverse = jnp.einsum("bhij,bhjk->bhik", inverse, eye + power, precision=HIGHEST)
        span = span * 2
    return inverse


def key_terms(key_units, logdec, beta_units):
    length = logdec.shape[-1]
    positions = jnp.arange(length)
    lower_incl = positions[:, None] >= positions[None, :]
    lower_strict = positions[:, None] > positions[None, :]
    cumulative = jnp.cumsum(logdec, axis=-1)
    differ = cumulative[..., :, None] - cumulative[..., None, :]
    decay_incl = jnp.where(lower_incl, jnp.exp(jnp.where(lower_incl, differ, 0.0)), 0.0)
    decay_strict = jnp.where(lower_strict, decay_incl, 0.0)
    key_gram = jnp.einsum("bhid,bhjd->bhij", key_units, key_units, precision=HIGHEST)
    inverse = unit_lower_inverse(beta_units[..., :, None] * key_gram * decay_strict)
    growth = jnp.exp(cumulative)
    weight_keys = jnp.einsum(
        "bhij,bhjd->bhid",
        inverse,
        (beta_units * growth)[..., None] * key_units,
        precision=HIGHEST,
    )
    fading = jnp.exp(cumulative[..., -1:] - cumulative)[..., None] * key_units
    eye_key = jnp.eye(key_units.shape[-1], dtype=jnp.float32)
    transition = growth[..., -1][..., None, None] * eye_key - jnp.einsum(
        "bhjd,bhje->bhde", fading, weight_keys, precision=HIGHEST
    )
    return (inverse, weight_keys, fading, transition, decay_incl, growth)


def value_terms(inverse, fading, value_units, beta_units):
    weight_values = jnp.einsum(
        "bhij,bhjd->bhid", inverse, beta_units[..., None] * value_units, precision=HIGHEST
    )
    offset = jnp.einsum("bhjd,bhje->bhde", fading, weight_values, precision=HIGHEST)
    return (weight_values, offset)


def query_terms(queries, key_units, decay_incl, growth, weight_values, weight_keys):
    mixing = decay_incl * jnp.einsum("bhid,bhjd->bhij", queries, key_units, precision=HIGHEST)
    zero_out = jnp.einsum("bhij,bhjd->bhid", mixing, weight_values, precision=HIGHEST)
    readout = growth[..., None] * queries - jnp.einsum(
        "bhij,bhjd->bhid", mixing, weight_keys, precision=HIGHEST
    )
    return (zero_out, readout)


def product(left, right):
    return jnp.einsum("hde,hef->hdf", left, right, precision=HIGHEST)


def to_rows(blocks):
    return blocks.transpose(0, 2, 1, 3).reshape(-1, blocks.shape[1], blocks.shape[3])


def gated_norm(delta_rows, gate_raw, norm_gain):
    meansq = jnp.mean(delta_rows * delta_rows, axis=-1, keepdims=True)
    normed = delta_rows * lax.rsqrt(meansq + EPSILON) * norm_gain
    gate_float = gate_raw.astype(jnp.float32).reshape(delta_rows.shape)
    return (normed * jax.nn.silu(gate_float)).reshape(delta_rows.shape[0], -1).astype(jnp.bfloat16)


def shards(
    query_raw,
    key_raw,
    value_raw,
    query_scale,
    key_block_scale,
    value_scale,
    conv_query,
    key_filter_taps,
    conv_value,
    gate_input,
    beta_logit,
    decay_base,
    step_bias,
    output_gate,
    norm_gain,
):
    head_width = norm_gain.shape[0]
    margin = conv_query.shape[0] - 1
    query_deq = expand_quantized(query_raw, query_scale)
    key_deq = expand_quantized(key_raw, key_block_scale)
    value_deq = expand_quantized(value_raw, value_scale)
    query_width, key_width = (query_deq.shape[1], key_deq.shape[1])
    tails = from_behind(
        jnp.concatenate([query_deq[-margin:], key_deq[-margin:], value_deq[-margin:]], axis=1),
        "seq",
        1,
    )
    tail_rows = (
        tails[:, :query_width],
        tails[:, query_width : query_width + key_width],
        tails[:, query_width + key_width :],
    )
    local_heads = gate_input.shape[1]
    first_head = lax.axis_index("head") * local_heads
    base_part = lax.dynamic_slice_in_dim(decay_base, first_head, local_heads)
    bias_part = lax.dynamic_slice_in_dim(step_bias, first_head, local_heads)
    key_filtered = causal_filter(jnp.concatenate([tail_rows[1], key_deq], axis=0), key_filter_taps)
    row_count = key_filtered.shape[0]
    key_rows = unit_heads(key_filtered, head_width)
    repeats = local_heads // key_rows.shape[1]
    key_units = to_blocks(jnp.repeat(key_rows, repeats, axis=1), CH)
    logdec = -jnp.exp(base_part)[None, :] * jax.nn.softplus(gate_input + bias_part[None, :])
    logdec = to_block_rows(logdec, CH)
    beta_units = to_block_rows(jax.nn.sigmoid(beta_logit), CH)
    inverse, weight_keys, fading, transition, decay_incl, growth = key_terms(
        key_units, logdec, beta_units
    )
    dev_trans = transition[0]
    trans_before = [None]
    for block in range(1, transition.shape[0]):
        trans_before.append(dev_trans)
        dev_trans = product(transition[block], dev_trans)
    value_window, _ = lax.optimization_barrier(
        (jnp.concatenate([tail_rows[2], value_deq], axis=0), dev_trans)
    )
    value_conv = causal_filter(value_window, conv_value)
    value_units = to_blocks(value_conv.astype(jnp.float32).reshape(row_count, -1, head_width), CH)
    weight_values, offset = value_terms(inverse, fading, value_units, beta_units)
    dev_offset = offset[0]
    offset_before = [None]
    for block in range(1, transition.shape[0]):
        offset_before.append(dev_offset)
        dev_offset = product(transition[block], dev_offset) + offset[block]
    query_window, _ = lax.optimization_barrier(
        (jnp.concatenate([tail_rows[0], query_deq], axis=0), dev_offset)
    )
    query_conv = causal_filter(query_window, conv_query)
    query_rows = unit_heads(query_conv, head_width) * head_width ** (-0.5)
    queries = to_blocks(jnp.repeat(query_rows, repeats, axis=1), CH)
    zero_out, readout = query_terms(
        queries, key_units, decay_incl, growth, weight_values, weight_keys
    )
    local_outs, read_maps = ([zero_out[0]], [readout[0]])
    for block in range(1, transition.shape[0]):
        read_maps.append(
            jnp.einsum("hid,hde->hie", readout[block], trans_before[block], precision=HIGHEST)
        )
        local_outs.append(
            zero_out[block]
            + jnp.einsum("hid,hde->hie", readout[block], offset_before[block], precision=HIGHEST)
        )
    incoming = scan_states(dev_trans, dev_offset, "seq")
    outputs = jnp.stack(local_outs) + jnp.einsum(
        "bhid,hde->bhie", jnp.stack(read_maps), incoming, precision=HIGHEST
    )
    gated_rows = gated_norm(to_rows(outputs), output_gate, norm_gain)
    return gated_rows


def solution(mesh):
    placed = (
        P("seq", "head"),
        P("seq", "head"),
        P("seq", "head"),
        P("seq", "head"),
        P("seq", "head"),
        P("seq", "head"),
        P(None, "head"),
        P(None, "head"),
        P(None, "head"),
        P("seq", "head"),
        P("seq", "head"),
        P(),
        P(),
        P("seq", "head"),
        P(),
    )
    return jax.shard_map(
        shards, mesh=mesh, in_specs=placed, out_specs=P("seq", "head"), check_vma=False
    )
```

```python
import jax
import jax.numpy as jnp
from jax import lax
from jax.sharding import PartitionSpec as P

CH = 64


HIGHEST = lax.Precision.HIGHEST
EPSILON = 1e-06


def from_behind(value, axis, steps):
    count = lax.axis_size(axis)
    first, last = (max(0, -steps), min(count, count - steps))
    return lax.ppermute(value, axis, [(source, source + steps) for source in range(first, last)])


def scan_states(trans, offset, axis):
    devices, mine = (lax.axis_size(axis), lax.axis_index(axis))
    spans = []
    span = 1
    while span < devices:
        spans.append(span)
        span = span * 2
    eye = jnp.eye(trans.shape[-1], dtype=jnp.float32)
    inclusive_maps, exclusive_maps = ([], [None])
    inclusive = trans
    for span in spans[:-1]:
        pairs = [(source, source + span) for source in range(devices - span)]
        inclusive_maps.append(inclusive)
        reached = jnp.where(mine >= span, 1.0, 0.0)
        earlier = lax.ppermute((inclusive - eye).astype(jnp.bfloat16), axis, pairs)
        earlier = earlier.astype(jnp.float32) + reached * eye
        last_map = exclusive_maps[-1]
        if last_map is None or 4 * span >= devices:
            exclusive_maps.append(earlier if last_map is None else product(last_map, earlier))
            if 4 * span < devices:
                inclusive = jnp.where(mine >= span, product(inclusive, earlier), inclusive)
        else:
            both = jnp.einsum(
                "shde,hef->shdf", jnp.stack([last_map, inclusive]), earlier, precision=HIGHEST
            )
            exclusive_maps.append(both[0])
            inclusive = jnp.where(mine >= span, both[1], inclusive)
    state = jnp.zeros_like(offset)
    carried = offset
    for step, span in enumerate(spans):
        pairs = [(source, source + span) for source in range(devices - span)]
        earlier = lax.ppermute(carried.astype(jnp.bfloat16), axis, pairs).astype(jnp.float32)
        last_map = exclusive_maps[step]
        if last_map is None:
            state = earlier
            if step + 1 < len(spans):
                carried = product(inclusive_maps[step], earlier) + carried
        elif step + 1 < len(spans):
            both = jnp.einsum(
                "shde,hef->shdf",
                jnp.stack([last_map, inclusive_maps[step]]),
                earlier,
                precision=HIGHEST,
            )
            state = state + both[0]
            carried = both[1] + carried
        else:
            state = state + product(last_map, earlier)
    return state


def expand_quantized(raw_rows, scales):
    row_count = raw_rows.shape[0]
    head_count = scales.shape[1]
    shaped = raw_rows.astype(jnp.float32).reshape(row_count, head_count, -1) * scales[:, :, None]
    return shaped.reshape(row_count, -1)


def causal_filter(window, weights):
    kernel_span = weights.shape[0]
    row_count = window.shape[0] - kernel_span + 1
    summed = jnp.zeros((row_count, window.shape[1]), jnp.float32)
    for offset_tap in range(kernel_span):
        summed = summed + window[offset_tap : offset_tap + row_count] * weights[offset_tap].astype(
            jnp.float32
        )
    return lax.optimization_barrier(jax.nn.silu(summed).astype(jnp.bfloat16))


def unit_heads(conv_rows, head_width):
    row_count = conv_rows.shape[0]
    shaped = conv_rows.astype(jnp.float32).reshape(row_count, -1, head_width)
    return shaped * lax.rsqrt(jnp.sum(shaped * shaped, axis=-1, keepdims=True) + EPSILON)


def to_blocks(array, block):
    block_count = array.shape[0] // block
    return array.reshape(block_count, block, array.shape[1], -1).transpose(0, 2, 1, 3)


def to_block_rows(array, block):
    block_count = array.shape[0] // block
    return array.reshape(block_count, block, -1).transpose(0, 2, 1)


def unit_lower_inverse(strict_part):
    length = strict_part.shape[-1]
    eye = jnp.eye(length, dtype=jnp.float32)
    power = -strict_part
    inverse = eye + power
    span = 2
    if span < length:
        power = jnp.einsum("bhij,bhjk->bhik", power, power, precision=HIGHEST)
    while span < length:
        if 2 * span < length:
            both = jnp.einsum(
                "sbhij,sbhjk->sbhik",
                jnp.stack([inverse, power]),
                jnp.stack([eye + power, power]),
                precision=HIGHEST,
            )
            inverse, power = (both[0], both[1])
        else:
            inverse = jnp.einsum("bhij,bhjk->bhik", inverse, eye + power, precision=HIGHEST)
        span = span * 2
    return inverse


def block_maps(key_units, value_units, logdec, beta_units):
    length = logdec.shape[-1]
    positions = jnp.arange(length)
    lower_incl = positions[:, None] >= positions[None, :]
    lower_strict = positions[:, None] > positions[None, :]
    cumulative = jnp.cumsum(logdec, axis=-1)
    differ = cumulative[..., :, None] - cumulative[..., None, :]
    decay_incl = jnp.where(lower_incl, jnp.exp(jnp.where(lower_incl, differ, 0.0)), 0.0)
    decay_strict = jnp.where(lower_strict, decay_incl, 0.0)
    key_gram = jnp.einsum("bhid,bhjd->bhij", key_units, key_units, precision=HIGHEST)
    inverse = unit_lower_inverse(beta_units[..., :, None] * key_gram * decay_strict)
    growth = jnp.exp(cumulative)
    stacked = jnp.concatenate(
        [(beta_units * growth)[..., None] * key_units, beta_units[..., None] * value_units],
        axis=-1,
    )
    solved = jnp.einsum("bhij,bhjd->bhid", inverse, stacked, precision=HIGHEST)
    key_width = key_units.shape[-1]
    fading = jnp.exp(cumulative[..., -1:] - cumulative)[..., None] * key_units
    faded = jnp.einsum("bhjd,bhje->bhde", fading, solved, precision=HIGHEST)
    eye_key = jnp.eye(key_width, dtype=jnp.float32)
    transition = growth[..., -1][..., None, None] * eye_key - faded[..., :key_width]
    maps = jnp.concatenate([transition, faded[..., key_width:]], axis=-1)
    return (solved[..., key_width:], solved[..., :key_width], maps, decay_incl, growth)


def query_terms(queries, key_units, decay_incl, growth, weight_values, weight_keys):
    mixing = decay_incl * jnp.einsum("bhid,bhjd->bhij", queries, key_units, precision=HIGHEST)
    zero_out = jnp.einsum("bhij,bhjd->bhid", mixing, weight_values, precision=HIGHEST)
    readout = growth[..., None] * queries - jnp.einsum(
        "bhij,bhjd->bhid", mixing, weight_keys, precision=HIGHEST
    )
    return (zero_out, readout)


def product(left, right):
    return jnp.einsum("hde,hef->hdf", left, right, precision=HIGHEST)


def to_rows(blocks):
    return blocks.transpose(0, 2, 1, 3).reshape(-1, blocks.shape[1], blocks.shape[3])


def gated_norm(delta_rows, gate_raw, norm_gain):
    meansq = jnp.mean(delta_rows * delta_rows, axis=-1, keepdims=True)
    normed = delta_rows * lax.rsqrt(meansq + EPSILON) * norm_gain
    gate_float = gate_raw.astype(jnp.float32).reshape(delta_rows.shape)
    return (normed * jax.nn.silu(gate_float)).reshape(delta_rows.shape[0], -1).astype(jnp.bfloat16)


def shards(
    query_raw,
    key_raw,
    value_raw,
    query_scale,
    key_block_scale,
    value_scale,
    conv_query,
    key_filter_taps,
    conv_value,
    gate_input,
    beta_logit,
    decay_base,
    step_bias,
    output_gate,
    norm_gain,
):
    head_width = norm_gain.shape[0]
    margin = conv_query.shape[0] - 1
    query_deq = expand_quantized(query_raw, query_scale)
    key_deq = expand_quantized(key_raw, key_block_scale)
    value_deq = expand_quantized(value_raw, value_scale)
    query_width, key_width = (query_deq.shape[1], key_deq.shape[1])
    tails = from_behind(
        jnp.concatenate([query_deq[-margin:], key_deq[-margin:], value_deq[-margin:]], axis=1),
        "seq",
        1,
    )
    tail_rows = (
        tails[:, :query_width],
        tails[:, query_width : query_width + key_width],
        tails[:, query_width + key_width :],
    )
    local_heads = gate_input.shape[1]
    first_head = lax.axis_index("head") * local_heads
    base_part = lax.dynamic_slice_in_dim(decay_base, first_head, local_heads)
    bias_part = lax.dynamic_slice_in_dim(step_bias, first_head, local_heads)
    key_filtered = causal_filter(jnp.concatenate([tail_rows[1], key_deq], axis=0), key_filter_taps)
    row_count = key_filtered.shape[0]
    key_rows = unit_heads(key_filtered, head_width)
    repeats = local_heads // key_rows.shape[1]
    key_units = to_blocks(jnp.repeat(key_rows, repeats, axis=1), CH)
    logdec = -jnp.exp(base_part)[None, :] * jax.nn.softplus(gate_input + bias_part[None, :])
    logdec = to_block_rows(logdec, CH)
    beta_units = to_block_rows(jax.nn.sigmoid(beta_logit), CH)
    value_conv = causal_filter(jnp.concatenate([tail_rows[2], value_deq], axis=0), conv_value)
    value_units = to_blocks(value_conv.astype(jnp.float32).reshape(row_count, -1, head_width), CH)
    weight_values, weight_keys, maps, decay_incl, growth = block_maps(
        key_units, value_units, logdec, beta_units
    )
    key_width = key_units.shape[-1]
    device_map = maps[0]
    maps_before = [None]
    for block in range(1, maps.shape[0]):
        maps_before.append(device_map)
        device_map = jnp.einsum(
            "hde,hef->hdf", maps[block][..., :key_width], device_map, precision=HIGHEST
        ).at[..., key_width:].add(maps[block][..., key_width:])
    dev_trans, dev_offset = (device_map[..., :key_width], device_map[..., key_width:])
    query_window, _ = lax.optimization_barrier(
        (jnp.concatenate([tail_rows[0], query_deq], axis=0), dev_offset)
    )
    query_conv = causal_filter(query_window, conv_query)
    query_rows = unit_heads(query_conv, head_width) * head_width ** (-0.5)
    queries = to_blocks(jnp.repeat(query_rows, repeats, axis=1), CH)
    zero_out, readout = query_terms(
        queries, key_units, decay_incl, growth, weight_values, weight_keys
    )
    local_outs, read_maps = ([zero_out[0]], [readout[0]])
    for block in range(1, maps.shape[0]):
        read = jnp.einsum("hid,hde->hie", readout[block], maps_before[block], precision=HIGHEST)
        read_maps.append(read[..., :key_width])
        local_outs.append(zero_out[block] + read[..., key_width:])
    incoming = scan_states(dev_trans, dev_offset, "seq")
    outputs = jnp.stack(local_outs) + jnp.einsum(
        "bhid,hde->bhie", jnp.stack(read_maps), incoming, precision=HIGHEST
    )
    gated_rows = gated_norm(to_rows(outputs), output_gate, norm_gain)
    return gated_rows


def solution(mesh):
    placed = (
        P("seq", "head"),
        P("seq", "head"),
        P("seq", "head"),
        P("seq", "head"),
        P("seq", "head"),
        P("seq", "head"),
        P(None, "head"),
        P(None, "head"),
        P(None, "head"),
        P("seq", "head"),
        P("seq", "head"),
        P(),
        P(),
        P("seq", "head"),
        P(),
    )
    return jax.shard_map(
        shards, mesh=mesh, in_specs=placed, out_specs=P("seq", "head"), check_vma=False
    )
```

```python
import jax
import jax.numpy as jnp
from jax import lax
from jax.sharding import PartitionSpec as P

CH = 64


HIGHEST = lax.Precision.HIGHEST
EPSILON = 1e-06


def from_behind(value, axis, steps):
    count = lax.axis_size(axis)
    first, last = (max(0, -steps), min(count, count - steps))
    return lax.ppermute(value, axis, [(source, source + steps) for source in range(first, last)])


def scan_states(trans, offset, axis, rider):
    devices, mine = (lax.axis_size(axis), lax.axis_index(axis))
    spans = []
    span = 1
    while span < devices:
        spans.append(span)
        span = span * 2
    eye = jnp.eye(trans.shape[-1], dtype=jnp.float32)
    inclusive_maps, exclusive_maps = ([], [None])
    inclusive = trans
    for span in spans[:-1]:
        pairs = [(source, source + span) for source in range(devices - span)]
        inclusive_maps.append(inclusive)
        reached = jnp.where(mine >= span, 1.0, 0.0)
        earlier = lax.ppermute((inclusive - eye).astype(jnp.bfloat16), axis, pairs)
        earlier = earlier.astype(jnp.float32) + reached * eye
        last_map = exclusive_maps[-1]
        if last_map is None or 4 * span >= devices:
            exclusive_maps.append(earlier if last_map is None else product(last_map, earlier))
            if 4 * span < devices:
                inclusive = jnp.where(mine >= span, product(inclusive, earlier), inclusive)
        else:
            both = jnp.einsum(
                "shde,hef->shdf", jnp.stack([last_map, inclusive]), earlier, precision=HIGHEST
            )
            exclusive_maps.append(both[0])
            inclusive = jnp.where(mine >= span, both[1], inclusive)
    state = jnp.zeros_like(offset)
    carried = offset
    for step, span in enumerate(spans):
        pairs = [(source, source + span) for source in range(devices - span)]
        earlier = lax.ppermute(carried.astype(jnp.bfloat16), axis, pairs)
        if step == 0:
            rider, earlier = lax.optimization_barrier((rider, earlier))
        earlier = earlier.astype(jnp.float32)
        last_map = exclusive_maps[step]
        if last_map is None:
            state = earlier
            if step + 1 < len(spans):
                carried = product(inclusive_maps[step], earlier) + carried
        elif step + 1 < len(spans):
            both = jnp.einsum(
                "shde,hef->shdf",
                jnp.stack([last_map, inclusive_maps[step]]),
                earlier,
                precision=HIGHEST,
            )
            state = state + both[0]
            carried = both[1] + carried
        else:
            state = state + product(last_map, earlier)
    return (state, rider)


def expand_quantized(raw_rows, scales):
    row_count = raw_rows.shape[0]
    head_count = scales.shape[1]
    shaped = raw_rows.astype(jnp.float32).reshape(row_count, head_count, -1) * scales[:, :, None]
    return shaped.reshape(row_count, -1)


def causal_filter(window, weights):
    kernel_span = weights.shape[0]
    row_count = window.shape[0] - kernel_span + 1
    summed = jnp.zeros((row_count, window.shape[1]), jnp.float32)
    for offset_tap in range(kernel_span):
        summed = summed + window[offset_tap : offset_tap + row_count] * weights[offset_tap].astype(
            jnp.float32
        )
    return lax.optimization_barrier(jax.nn.silu(summed).astype(jnp.bfloat16))


def unit_heads(conv_rows, head_width):
    row_count = conv_rows.shape[0]
    shaped = conv_rows.astype(jnp.float32).reshape(row_count, -1, head_width)
    return shaped * lax.rsqrt(jnp.sum(shaped * shaped, axis=-1, keepdims=True) + EPSILON)


def to_blocks(array, block):
    block_count = array.shape[0] // block
    return array.reshape(block_count, block, array.shape[1], -1).transpose(0, 2, 1, 3)


def to_block_rows(array, block):
    block_count = array.shape[0] // block
    return array.reshape(block_count, block, -1).transpose(0, 2, 1)


def unit_lower_inverse(strict_part):
    length = strict_part.shape[-1]
    eye = jnp.eye(length, dtype=jnp.float32)
    power = -strict_part
    inverse = eye + power
    span = 2
    if span < length:
        power = jnp.einsum("bhij,bhjk->bhik", power, power, precision=HIGHEST)
    while span < length:
        if 2 * span < length:
            both = jnp.einsum(
                "sbhij,sbhjk->sbhik",
                jnp.stack([inverse, power]),
                jnp.stack([eye + power, power]),
                precision=HIGHEST,
            )
            inverse, power = (both[0], both[1])
        else:
            inverse = jnp.einsum("bhij,bhjk->bhik", inverse, eye + power, precision=HIGHEST)
        span = span * 2
    return inverse


def block_maps(key_units, value_units, logdec, beta_units):
    length = logdec.shape[-1]
    positions = jnp.arange(length)
    lower_incl = positions[:, None] >= positions[None, :]
    lower_strict = positions[:, None] > positions[None, :]
    cumulative = jnp.cumsum(logdec, axis=-1)
    differ = cumulative[..., :, None] - cumulative[..., None, :]
    decay_incl = jnp.where(lower_incl, jnp.exp(jnp.where(lower_incl, differ, 0.0)), 0.0)
    decay_strict = jnp.where(lower_strict, decay_incl, 0.0)
    key_gram = jnp.einsum("bhid,bhjd->bhij", key_units, key_units, precision=HIGHEST)
    inverse = unit_lower_inverse(beta_units[..., :, None] * key_gram * decay_strict)
    growth = jnp.exp(cumulative)
    stacked = jnp.concatenate(
        [(beta_units * growth)[..., None] * key_units, beta_units[..., None] * value_units],
        axis=-1,
    )
    solved = jnp.einsum("bhij,bhjd->bhid", inverse, stacked, precision=HIGHEST)
    key_width = key_units.shape[-1]
    fading = jnp.exp(cumulative[..., -1:] - cumulative)[..., None] * key_units
    faded = jnp.einsum("bhjd,bhje->bhde", fading, solved, precision=HIGHEST)
    eye_key = jnp.eye(key_width, dtype=jnp.float32)
    transition = growth[..., -1][..., None, None] * eye_key - faded[..., :key_width]
    maps = jnp.concatenate([transition, faded[..., key_width:]], axis=-1)
    return (solved[..., key_width:], solved[..., :key_width], maps, decay_incl, growth)


def query_terms(queries, key_units, decay_incl, growth, weight_values, weight_keys):
    mixing = decay_incl * jnp.einsum("bhid,bhjd->bhij", queries, key_units, precision=HIGHEST)
    zero_out = jnp.einsum("bhij,bhjd->bhid", mixing, weight_values, precision=HIGHEST)
    readout = growth[..., None] * queries - jnp.einsum(
        "bhij,bhjd->bhid", mixing, weight_keys, precision=HIGHEST
    )
    return (zero_out, readout)


def product(left, right):
    return jnp.einsum("hde,hef->hdf", left, right, precision=HIGHEST)


def to_rows(blocks):
    return blocks.transpose(0, 2, 1, 3).reshape(-1, blocks.shape[1], blocks.shape[3])


def gated_norm(delta_rows, gate_raw, norm_gain):
    meansq = jnp.mean(delta_rows * delta_rows, axis=-1, keepdims=True)
    normed = delta_rows * lax.rsqrt(meansq + EPSILON) * norm_gain
    gate_float = gate_raw.astype(jnp.float32).reshape(delta_rows.shape)
    return (normed * jax.nn.silu(gate_float)).reshape(delta_rows.shape[0], -1).astype(jnp.bfloat16)


def shards(
    query_raw,
    key_raw,
    value_raw,
    query_scale,
    key_block_scale,
    value_scale,
    conv_query,
    key_filter_taps,
    conv_value,
    gate_input,
    beta_logit,
    decay_base,
    step_bias,
    output_gate,
    norm_gain,
):
    head_width = norm_gain.shape[0]
    margin = conv_query.shape[0] - 1
    query_deq = expand_quantized(query_raw, query_scale)
    key_deq = expand_quantized(key_raw, key_block_scale)
    value_deq = expand_quantized(value_raw, value_scale)
    query_width, key_width = (query_deq.shape[1], key_deq.shape[1])
    tails = from_behind(
        jnp.concatenate([query_deq[-margin:], key_deq[-margin:], value_deq[-margin:]], axis=1),
        "seq",
        1,
    )
    tail_rows = (
        tails[:, :query_width],
        tails[:, query_width : query_width + key_width],
        tails[:, query_width + key_width :],
    )
    local_heads = gate_input.shape[1]
    first_head = lax.axis_index("head") * local_heads
    base_part = lax.dynamic_slice_in_dim(decay_base, first_head, local_heads)
    bias_part = lax.dynamic_slice_in_dim(step_bias, first_head, local_heads)
    key_filtered = causal_filter(jnp.concatenate([tail_rows[1], key_deq], axis=0), key_filter_taps)
    row_count = key_filtered.shape[0]
    key_rows = unit_heads(key_filtered, head_width)
    repeats = local_heads // key_rows.shape[1]
    key_units = to_blocks(jnp.repeat(key_rows, repeats, axis=1), CH)
    logdec = -jnp.exp(base_part)[None, :] * jax.nn.softplus(gate_input + bias_part[None, :])
    logdec = to_block_rows(logdec, CH)
    beta_units = to_block_rows(jax.nn.sigmoid(beta_logit), CH)
    value_conv = causal_filter(jnp.concatenate([tail_rows[2], value_deq], axis=0), conv_value)
    value_units = to_blocks(value_conv.astype(jnp.float32).reshape(row_count, -1, head_width), CH)
    weight_values, weight_keys, maps, decay_incl, growth = block_maps(
        key_units, value_units, logdec, beta_units
    )
    key_width = key_units.shape[-1]
    device_map = maps[0]
    maps_before = [None]
    for block in range(1, maps.shape[0]):
        maps_before.append(device_map)
        device_map = jnp.einsum(
            "hde,hef->hdf", maps[block][..., :key_width], device_map, precision=HIGHEST
        ).at[..., key_width:].add(maps[block][..., key_width:])
    dev_trans, dev_offset = (device_map[..., :key_width], device_map[..., key_width:])
    incoming, query_window = scan_states(
        dev_trans, dev_offset, "seq", jnp.concatenate([tail_rows[0], query_deq], axis=0)
    )
    query_conv = causal_filter(query_window, conv_query)
    query_rows = unit_heads(query_conv, head_width) * head_width ** (-0.5)
    queries = to_blocks(jnp.repeat(query_rows, repeats, axis=1), CH)
    zero_out, readout = query_terms(
        queries, key_units, decay_incl, growth, weight_values, weight_keys
    )
    local_outs, read_maps = ([zero_out[0]], [readout[0]])
    for block in range(1, maps.shape[0]):
        read = jnp.einsum("hid,hde->hie", readout[block], maps_before[block], precision=HIGHEST)
        read_maps.append(read[..., :key_width])
        local_outs.append(zero_out[block] + read[..., key_width:])
    outputs = jnp.stack(local_outs) + jnp.einsum(
        "bhid,hde->bhie", jnp.stack(read_maps), incoming, precision=HIGHEST
    )
    gated_rows = gated_norm(to_rows(outputs), output_gate, norm_gain)
    return gated_rows


def solution(mesh):
    placed = (
        P("seq", "head"),
        P("seq", "head"),
        P("seq", "head"),
        P("seq", "head"),
        P("seq", "head"),
        P("seq", "head"),
        P(None, "head"),
        P(None, "head"),
        P(None, "head"),
        P("seq", "head"),
        P("seq", "head"),
        P(),
        P(),
        P("seq", "head"),
        P(),
    )
    return jax.shard_map(
        shards, mesh=mesh, in_specs=placed, out_specs=P("seq", "head"), check_vma=False
    )
```

```python
import jax
import jax.numpy as jnp
from jax import lax
from jax.sharding import PartitionSpec as P

CH = 64


HIGHEST = lax.Precision.HIGHEST
EPSILON = 1e-06


def from_behind(value, axis, steps):
    count = lax.axis_size(axis)
    first, last = (max(0, -steps), min(count, count - steps))
    return lax.ppermute(value, axis, [(source, source + steps) for source in range(first, last)])


def scan_states(trans, offset, axis, rider):
    devices, mine = (lax.axis_size(axis), lax.axis_index(axis))
    spans = []
    span = 1
    while span < devices:
        spans.append(span)
        span = span * 2
    eye = jnp.eye(trans.shape[-1], dtype=jnp.float32)
    inclusive_maps, exclusive_maps = ([], [None])
    inclusive = trans
    for span in spans[:-1]:
        pairs = [(source, source + span) for source in range(devices - span)]
        inclusive_maps.append(inclusive)
        reached = jnp.where(mine >= span, 1.0, 0.0)
        earlier = lax.ppermute((inclusive - eye).astype(jnp.bfloat16), axis, pairs)
        earlier = earlier.astype(jnp.float32) + reached * eye
        last_map = exclusive_maps[-1]
        if last_map is None or 4 * span >= devices:
            exclusive_maps.append(earlier if last_map is None else product(last_map, earlier))
            if 4 * span < devices:
                inclusive = jnp.where(mine >= span, product(inclusive, earlier), inclusive)
        else:
            both = jnp.einsum(
                "shde,hef->shdf", jnp.stack([last_map, inclusive]), earlier, precision=HIGHEST
            )
            exclusive_maps.append(both[0])
            inclusive = jnp.where(mine >= span, both[1], inclusive)
    state = jnp.zeros_like(offset)
    carried = offset
    for step, span in enumerate(spans):
        pairs = [(source, source + span) for source in range(devices - span)]
        earlier = lax.ppermute(carried.astype(jnp.bfloat16), axis, pairs)
        if step == 0:
            rider, earlier = lax.optimization_barrier((rider, earlier))
        earlier = earlier.astype(jnp.float32)
        last_map = exclusive_maps[step]
        if last_map is None:
            state = earlier
            if step + 1 < len(spans):
                carried = product(inclusive_maps[step], earlier) + carried
        elif step + 1 < len(spans):
            both = jnp.einsum(
                "shde,hef->shdf",
                jnp.stack([last_map, inclusive_maps[step]]),
                earlier,
                precision=HIGHEST,
            )
            state = state + both[0]
            carried = both[1] + carried
        else:
            state = state + product(last_map, earlier)
    return (state, rider)


def expand_quantized(raw_rows, scales):
    head_count = scales.shape[1]
    width = raw_rows.shape[1] // head_count
    return raw_rows.astype(jnp.float32) * jnp.repeat(scales, width, axis=1)


def causal_filter(window, weights):
    kernel_span = weights.shape[0]
    row_count = window.shape[0] - kernel_span + 1
    summed = jnp.zeros((row_count, window.shape[1]), jnp.float32)
    for offset_tap in range(kernel_span):
        summed = summed + window[offset_tap : offset_tap + row_count] * weights[offset_tap].astype(
            jnp.float32
        )
    return lax.optimization_barrier(jax.nn.silu(summed).astype(jnp.bfloat16))


def unit_heads(conv_rows, head_width):
    row_count = conv_rows.shape[0]
    shaped = conv_rows.astype(jnp.float32).reshape(row_count, -1, head_width)
    return shaped * lax.rsqrt(jnp.sum(shaped * shaped, axis=-1, keepdims=True) + EPSILON)


def to_blocks(array, block):
    block_count = array.shape[0] // block
    return array.reshape(block_count, block, array.shape[1], -1).transpose(0, 2, 1, 3)


def to_block_rows(array, block):
    block_count = array.shape[0] // block
    return array.reshape(block_count, block, -1).transpose(0, 2, 1)


def unit_lower_inverse(strict_part):
    length = strict_part.shape[-1]
    eye = jnp.eye(length, dtype=jnp.float32)
    power = -strict_part
    inverse = eye + power
    span = 2
    if span < length:
        power = jnp.einsum("bhij,bhjk->bhik", power, power, precision=HIGHEST)
    while span < length:
        if 2 * span < length:
            both = jnp.einsum(
                "sbhij,sbhjk->sbhik",
                jnp.stack([inverse, power]),
                jnp.stack([eye + power, power]),
                precision=HIGHEST,
            )
            inverse, power = (both[0], both[1])
        else:
            inverse = jnp.einsum("bhij,bhjk->bhik", inverse, eye + power, precision=HIGHEST)
        span = span * 2
    return inverse


def block_maps(key_units, value_units, logdec, beta_units):
    length = logdec.shape[-1]
    positions = jnp.arange(length)
    lower_incl = positions[:, None] >= positions[None, :]
    lower_strict = positions[:, None] > positions[None, :]
    cumulative = jnp.cumsum(logdec, axis=-1)
    differ = cumulative[..., :, None] - cumulative[..., None, :]
    decay_incl = jnp.where(lower_incl, jnp.exp(jnp.where(lower_incl, differ, 0.0)), 0.0)
    decay_strict = jnp.where(lower_strict, decay_incl, 0.0)
    key_gram = jnp.einsum("bhid,bhjd->bhij", key_units, key_units, precision=HIGHEST)
    inverse = unit_lower_inverse(beta_units[..., :, None] * key_gram * decay_strict)
    growth = jnp.exp(cumulative)
    stacked = jnp.concatenate(
        [(beta_units * growth)[..., None] * key_units, beta_units[..., None] * value_units],
        axis=-1,
    )
    solved = jnp.einsum("bhij,bhjd->bhid", inverse, stacked, precision=HIGHEST)
    key_width = key_units.shape[-1]
    fading = jnp.exp(cumulative[..., -1:] - cumulative)[..., None] * key_units
    faded = jnp.einsum("bhjd,bhje->bhde", fading, solved, precision=HIGHEST)
    eye_key = jnp.eye(key_width, dtype=jnp.float32)
    transition = growth[..., -1][..., None, None] * eye_key - faded[..., :key_width]
    maps = jnp.concatenate([transition, faded[..., key_width:]], axis=-1)
    return (solved[..., key_width:], solved[..., :key_width], maps, decay_incl, growth)


def query_terms(queries, key_units, decay_incl, growth, weight_values, weight_keys):
    mixing = decay_incl * jnp.einsum("bhid,bhjd->bhij", queries, key_units, precision=HIGHEST)
    zero_out = jnp.einsum("bhij,bhjd->bhid", mixing, weight_values, precision=HIGHEST)
    readout = growth[..., None] * queries - jnp.einsum(
        "bhij,bhjd->bhid", mixing, weight_keys, precision=HIGHEST
    )
    return (zero_out, readout)


def product(left, right):
    return jnp.einsum("hde,hef->hdf", left, right, precision=HIGHEST)


def to_rows(blocks):
    return blocks.transpose(0, 2, 1, 3).reshape(-1, blocks.shape[1], blocks.shape[3])


def gated_norm(delta_rows, gate_raw, norm_gain):
    meansq = jnp.mean(delta_rows * delta_rows, axis=-1, keepdims=True)
    normed = delta_rows * lax.rsqrt(meansq + EPSILON) * norm_gain
    gate_float = gate_raw.astype(jnp.float32).reshape(delta_rows.shape)
    return (normed * jax.nn.silu(gate_float)).reshape(delta_rows.shape[0], -1).astype(jnp.bfloat16)


def shards(
    query_raw,
    key_raw,
    value_raw,
    query_scale,
    key_block_scale,
    value_scale,
    conv_query,
    key_filter_taps,
    conv_value,
    gate_input,
    beta_logit,
    decay_base,
    step_bias,
    output_gate,
    norm_gain,
):
    head_width = norm_gain.shape[0]
    margin = conv_query.shape[0] - 1
    query_deq = expand_quantized(query_raw, query_scale)
    key_deq = expand_quantized(key_raw, key_block_scale)
    value_deq = expand_quantized(value_raw, value_scale)
    query_width, key_width = (query_deq.shape[1], key_deq.shape[1])
    tails = from_behind(
        jnp.concatenate([query_deq[-margin:], key_deq[-margin:], value_deq[-margin:]], axis=1),
        "seq",
        1,
    )
    tail_rows = (
        tails[:, :query_width],
        tails[:, query_width : query_width + key_width],
        tails[:, query_width + key_width :],
    )
    local_heads = gate_input.shape[1]
    first_head = lax.axis_index("head") * local_heads
    base_part = lax.dynamic_slice_in_dim(decay_base, first_head, local_heads)
    bias_part = lax.dynamic_slice_in_dim(step_bias, first_head, local_heads)
    key_filtered = causal_filter(jnp.concatenate([tail_rows[1], key_deq], axis=0), key_filter_taps)
    row_count = key_filtered.shape[0]
    key_rows = unit_heads(key_filtered, head_width)
    repeats = local_heads // key_rows.shape[1]
    key_units = to_blocks(jnp.repeat(key_rows, repeats, axis=1), CH)
    logdec = -jnp.exp(base_part)[None, :] * jax.nn.softplus(gate_input + bias_part[None, :])
    logdec = to_block_rows(logdec, CH)
    beta_units = to_block_rows(jax.nn.sigmoid(beta_logit), CH)
    value_conv = causal_filter(jnp.concatenate([tail_rows[2], value_deq], axis=0), conv_value)
    value_units = to_blocks(value_conv.astype(jnp.float32).reshape(row_count, -1, head_width), CH)
    weight_values, weight_keys, maps, decay_incl, growth = block_maps(
        key_units, value_units, logdec, beta_units
    )
    key_width = key_units.shape[-1]
    device_map = maps[0]
    maps_before = [None]
    for block in range(1, maps.shape[0]):
        maps_before.append(device_map)
        device_map = jnp.einsum(
            "hde,hef->hdf", maps[block][..., :key_width], device_map, precision=HIGHEST
        ).at[..., key_width:].add(maps[block][..., key_width:])
    dev_trans, dev_offset = (device_map[..., :key_width], device_map[..., key_width:])
    incoming, query_window = scan_states(
        dev_trans, dev_offset, "seq", jnp.concatenate([tail_rows[0], query_deq], axis=0)
    )
    query_conv = causal_filter(query_window, conv_query)
    query_rows = unit_heads(query_conv, head_width) * head_width ** (-0.5)
    queries = to_blocks(jnp.repeat(query_rows, repeats, axis=1), CH)
    zero_out, readout = query_terms(
        queries, key_units, decay_incl, growth, weight_values, weight_keys
    )
    local_outs, read_maps = ([zero_out[0]], [readout[0]])
    for block in range(1, maps.shape[0]):
        read = jnp.einsum("hid,hde->hie", readout[block], maps_before[block], precision=HIGHEST)
        read_maps.append(read[..., :key_width])
        local_outs.append(zero_out[block] + read[..., key_width:])
    outputs = jnp.stack(local_outs) + jnp.einsum(
        "bhid,hde->bhie", jnp.stack(read_maps), incoming, precision=HIGHEST
    )
    gated_rows = gated_norm(to_rows(outputs), output_gate, norm_gain)
    return gated_rows


def solution(mesh):
    placed = (
        P("seq", "head"),
        P("seq", "head"),
        P("seq", "head"),
        P("seq", "head"),
        P("seq", "head"),
        P("seq", "head"),
        P(None, "head"),
        P(None, "head"),
        P(None, "head"),
        P("seq", "head"),
        P("seq", "head"),
        P(),
        P(),
        P("seq", "head"),
        P(),
    )
    return jax.shard_map(
        shards, mesh=mesh, in_specs=placed, out_specs=P("seq", "head"), check_vma=False
    )
```

```python
import jax
import jax.numpy as jnp
from jax import lax
from jax.sharding import PartitionSpec as P

CH = 64


HIGHEST = lax.Precision.HIGHEST
EPSILON = 1e-06


def from_behind(value, axis, steps):
    count = lax.axis_size(axis)
    first, last = (max(0, -steps), min(count, count - steps))
    return lax.ppermute(value, axis, [(source, source + steps) for source in range(first, last)])


def scan_states(trans, offset, axis, rider):
    devices, mine = (lax.axis_size(axis), lax.axis_index(axis))
    spans = []
    span = 1
    while span < devices:
        spans.append(span)
        span = span * 2
    eye = jnp.eye(trans.shape[-1], dtype=jnp.float32)
    inclusive_maps, exclusive_maps = ([], [None])
    inclusive = trans
    for span in spans[:-1]:
        pairs = [(source, source + span) for source in range(devices - span)]
        inclusive_maps.append(inclusive)
        reached = jnp.where(mine >= span, 1.0, 0.0)
        earlier = lax.ppermute((inclusive - eye).astype(jnp.bfloat16), axis, pairs)
        earlier = earlier.astype(jnp.float32) + reached * eye
        last_map = exclusive_maps[-1]
        if last_map is None or 4 * span >= devices:
            exclusive_maps.append(earlier if last_map is None else product(last_map, earlier))
            if 4 * span < devices:
                inclusive = jnp.where(mine >= span, product(inclusive, earlier), inclusive)
        else:
            both = jnp.einsum(
                "shde,hef->shdf", jnp.stack([last_map, inclusive]), earlier, precision=HIGHEST
            )
            exclusive_maps.append(both[0])
            inclusive = jnp.where(mine >= span, both[1], inclusive)
    state = jnp.zeros_like(offset)
    carried = offset
    for step, span in enumerate(spans):
        pairs = [(source, source + span) for source in range(devices - span)]
        earlier = lax.ppermute(carried.astype(jnp.bfloat16), axis, pairs)
        if step == 0:
            rider, earlier = lax.optimization_barrier((rider, earlier))
        earlier = earlier.astype(jnp.float32)
        last_map = exclusive_maps[step]
        if last_map is None:
            state = earlier
            if step + 1 < len(spans):
                carried = product(inclusive_maps[step], earlier) + carried
        elif step + 1 < len(spans):
            both = jnp.einsum(
                "shde,hef->shdf",
                jnp.stack([last_map, inclusive_maps[step]]),
                earlier,
                precision=HIGHEST,
            )
            state = state + both[0]
            carried = both[1] + carried
        else:
            state = state + product(last_map, earlier)
    return (state, rider)


def expand_quantized(raw_rows, scales):
    head_count = scales.shape[1]
    width = raw_rows.shape[1] // head_count
    return raw_rows.astype(jnp.float32) * jnp.repeat(scales, width, axis=1)


def causal_filter(window, weights):
    kernel_span = weights.shape[0]
    row_count = window.shape[0] - kernel_span + 1
    summed = jnp.zeros((row_count, window.shape[1]), jnp.float32)
    for offset_tap in range(kernel_span):
        summed = summed + window[offset_tap : offset_tap + row_count] * weights[offset_tap].astype(
            jnp.float32
        )
    return lax.optimization_barrier(jax.nn.silu(summed).astype(jnp.bfloat16))


def unit_heads(conv_rows, head_width):
    rows = conv_rows.astype(jnp.float32)
    head_count = rows.shape[1] // head_width
    member = jnp.arange(rows.shape[1])[:, None] // head_width == jnp.arange(head_count)[None, :]
    sums = jnp.dot(rows * rows, member.astype(jnp.float32), precision=HIGHEST)
    scale = jnp.repeat(lax.rsqrt(sums + EPSILON), head_width, axis=1)
    return (rows * scale).reshape(rows.shape[0], head_count, head_width)


def to_blocks(array, block):
    block_count = array.shape[0] // block
    return array.reshape(block_count, block, array.shape[1], -1).transpose(0, 2, 1, 3)


def to_block_rows(array, block):
    block_count = array.shape[0] // block
    return array.reshape(block_count, block, -1).transpose(0, 2, 1)


def unit_lower_inverse(strict_part):
    length = strict_part.shape[-1]
    eye = jnp.eye(length, dtype=jnp.float32)
    power = -strict_part
    inverse = eye + power
    span = 2
    if span < length:
        power = jnp.einsum("bhij,bhjk->bhik", power, power, precision=HIGHEST)
    while span < length:
        if 2 * span < length:
            both = jnp.einsum(
                "sbhij,sbhjk->sbhik",
                jnp.stack([inverse, power]),
                jnp.stack([eye + power, power]),
                precision=HIGHEST,
            )
            inverse, power = (both[0], both[1])
        else:
            inverse = jnp.einsum("bhij,bhjk->bhik", inverse, eye + power, precision=HIGHEST)
        span = span * 2
    return inverse


def block_maps(key_units, value_units, logdec, beta_units):
    length = logdec.shape[-1]
    positions = jnp.arange(length)
    lower_incl = positions[:, None] >= positions[None, :]
    lower_strict = positions[:, None] > positions[None, :]
    cumulative = jnp.cumsum(logdec, axis=-1)
    differ = cumulative[..., :, None] - cumulative[..., None, :]
    decay_incl = jnp.where(lower_incl, jnp.exp(jnp.where(lower_incl, differ, 0.0)), 0.0)
    decay_strict = jnp.where(lower_strict, decay_incl, 0.0)
    key_gram = jnp.einsum("bhid,bhjd->bhij", key_units, key_units, precision=HIGHEST)
    inverse = unit_lower_inverse(beta_units[..., :, None] * key_gram * decay_strict)
    growth = jnp.exp(cumulative)
    stacked = jnp.concatenate(
        [(beta_units * growth)[..., None] * key_units, beta_units[..., None] * value_units],
        axis=-1,
    )
    solved = jnp.einsum("bhij,bhjd->bhid", inverse, stacked, precision=HIGHEST)
    key_width = key_units.shape[-1]
    fading = jnp.exp(cumulative[..., -1:] - cumulative)[..., None] * key_units
    faded = jnp.einsum("bhjd,bhje->bhde", fading, solved, precision=HIGHEST)
    eye_key = jnp.eye(key_width, dtype=jnp.float32)
    transition = growth[..., -1][..., None, None] * eye_key - faded[..., :key_width]
    maps = jnp.concatenate([transition, faded[..., key_width:]], axis=-1)
    return (solved[..., key_width:], solved[..., :key_width], maps, decay_incl, growth)


def query_terms(queries, key_units, decay_incl, growth, weight_values, weight_keys):
    mixing = decay_incl * jnp.einsum("bhid,bhjd->bhij", queries, key_units, precision=HIGHEST)
    zero_out = jnp.einsum("bhij,bhjd->bhid", mixing, weight_values, precision=HIGHEST)
    readout = growth[..., None] * queries - jnp.einsum(
        "bhij,bhjd->bhid", mixing, weight_keys, precision=HIGHEST
    )
    return (zero_out, readout)


def product(left, right):
    return jnp.einsum("hde,hef->hdf", left, right, precision=HIGHEST)


def to_rows(blocks):
    return blocks.transpose(0, 2, 1, 3).reshape(-1, blocks.shape[1], blocks.shape[3])


def gated_norm(delta_rows, gate_raw, norm_gain):
    meansq = jnp.mean(delta_rows * delta_rows, axis=-1, keepdims=True)
    normed = delta_rows * lax.rsqrt(meansq + EPSILON) * norm_gain
    gate_float = gate_raw.astype(jnp.float32).reshape(delta_rows.shape)
    return (normed * jax.nn.silu(gate_float)).reshape(delta_rows.shape[0], -1).astype(jnp.bfloat16)


def shards(
    query_raw,
    key_raw,
    value_raw,
    query_scale,
    key_block_scale,
    value_scale,
    conv_query,
    key_filter_taps,
    conv_value,
    gate_input,
    beta_logit,
    decay_base,
    step_bias,
    output_gate,
    norm_gain,
):
    head_width = norm_gain.shape[0]
    margin = conv_query.shape[0] - 1
    query_deq = expand_quantized(query_raw, query_scale)
    key_deq = expand_quantized(key_raw, key_block_scale)
    value_deq = expand_quantized(value_raw, value_scale)
    query_width, key_width = (query_deq.shape[1], key_deq.shape[1])
    tails = from_behind(
        jnp.concatenate([query_deq[-margin:], key_deq[-margin:], value_deq[-margin:]], axis=1),
        "seq",
        1,
    )
    tail_rows = (
        tails[:, :query_width],
        tails[:, query_width : query_width + key_width],
        tails[:, query_width + key_width :],
    )
    local_heads = gate_input.shape[1]
    first_head = lax.axis_index("head") * local_heads
    base_part = lax.dynamic_slice_in_dim(decay_base, first_head, local_heads)
    bias_part = lax.dynamic_slice_in_dim(step_bias, first_head, local_heads)
    key_filtered = causal_filter(jnp.concatenate([tail_rows[1], key_deq], axis=0), key_filter_taps)
    row_count = key_filtered.shape[0]
    key_rows = unit_heads(key_filtered, head_width)
    repeats = local_heads // key_rows.shape[1]
    key_units = to_blocks(jnp.repeat(key_rows, repeats, axis=1), CH)
    logdec = -jnp.exp(base_part)[None, :] * jax.nn.softplus(gate_input + bias_part[None, :])
    logdec = to_block_rows(logdec, CH)
    beta_units = to_block_rows(jax.nn.sigmoid(beta_logit), CH)
    value_conv = causal_filter(jnp.concatenate([tail_rows[2], value_deq], axis=0), conv_value)
    value_units = to_blocks(value_conv.astype(jnp.float32).reshape(row_count, -1, head_width), CH)
    weight_values, weight_keys, maps, decay_incl, growth = block_maps(
        key_units, value_units, logdec, beta_units
    )
    key_width = key_units.shape[-1]
    device_map = maps[0]
    maps_before = [None]
    for block in range(1, maps.shape[0]):
        maps_before.append(device_map)
        device_map = jnp.einsum(
            "hde,hef->hdf", maps[block][..., :key_width], device_map, precision=HIGHEST
        ).at[..., key_width:].add(maps[block][..., key_width:])
    dev_trans, dev_offset = (device_map[..., :key_width], device_map[..., key_width:])
    incoming, query_window = scan_states(
        dev_trans, dev_offset, "seq", jnp.concatenate([tail_rows[0], query_deq], axis=0)
    )
    query_conv = causal_filter(query_window, conv_query)
    query_rows = unit_heads(query_conv, head_width) * head_width ** (-0.5)
    queries = to_blocks(jnp.repeat(query_rows, repeats, axis=1), CH)
    zero_out, readout = query_terms(
        queries, key_units, decay_incl, growth, weight_values, weight_keys
    )
    local_outs, read_maps = ([zero_out[0]], [readout[0]])
    for block in range(1, maps.shape[0]):
        read = jnp.einsum("hid,hde->hie", readout[block], maps_before[block], precision=HIGHEST)
        read_maps.append(read[..., :key_width])
        local_outs.append(zero_out[block] + read[..., key_width:])
    outputs = jnp.stack(local_outs) + jnp.einsum(
        "bhid,hde->bhie", jnp.stack(read_maps), incoming, precision=HIGHEST
    )
    gated_rows = gated_norm(to_rows(outputs), output_gate, norm_gain)
    return gated_rows


def solution(mesh):
    placed = (
        P("seq", "head"),
        P("seq", "head"),
        P("seq", "head"),
        P("seq", "head"),
        P("seq", "head"),
        P("seq", "head"),
        P(None, "head"),
        P(None, "head"),
        P(None, "head"),
        P("seq", "head"),
        P("seq", "head"),
        P(),
        P(),
        P("seq", "head"),
        P(),
    )
    return jax.shard_map(
        shards, mesh=mesh, in_specs=placed, out_specs=P("seq", "head"), check_vma=False
    )
```

```python
import jax
import jax.numpy as jnp
from jax import lax
from jax.sharding import PartitionSpec as P

CH = 64


HIGHEST = lax.Precision.HIGHEST
EPSILON = 1e-06


def from_behind(value, axis, steps):
    count = lax.axis_size(axis)
    first, last = (max(0, -steps), min(count, count - steps))
    return lax.ppermute(value, axis, [(source, source + steps) for source in range(first, last)])


def scan_states(trans, offset, axis, rider):
    devices, mine = (lax.axis_size(axis), lax.axis_index(axis))
    spans = []
    span = 1
    while span < devices:
        spans.append(span)
        span = span * 2
    eye = jnp.eye(trans.shape[-1], dtype=jnp.float32)
    inclusive_maps, exclusive_maps = ([], [None])
    inclusive = trans
    for span in spans[:-1]:
        pairs = [(source, source + span) for source in range(devices - span)]
        inclusive_maps.append(inclusive)
        reached = jnp.where(mine >= span, 1.0, 0.0)
        earlier = lax.ppermute((inclusive - eye).astype(jnp.bfloat16), axis, pairs)
        earlier = earlier.astype(jnp.float32) + reached * eye
        last_map = exclusive_maps[-1]
        if last_map is None or 4 * span >= devices:
            exclusive_maps.append(earlier if last_map is None else product_high(last_map, earlier))
            if 4 * span < devices:
                inclusive = jnp.where(mine >= span, product_high(inclusive, earlier), inclusive)
        else:
            both = jnp.einsum(
                "shde,hef->shdf", jnp.stack([last_map, inclusive]), earlier, precision=lax.Precision.HIGH
            )
            exclusive_maps.append(both[0])
            inclusive = jnp.where(mine >= span, both[1], inclusive)
    state = jnp.zeros_like(offset)
    carried = offset
    for step, span in enumerate(spans):
        pairs = [(source, source + span) for source in range(devices - span)]
        earlier = lax.ppermute(carried.astype(jnp.bfloat16), axis, pairs)
        if step == 0:
            rider, earlier = lax.optimization_barrier((rider, earlier))
        earlier = earlier.astype(jnp.float32)
        last_map = exclusive_maps[step]
        if last_map is None:
            state = earlier
            if step + 1 < len(spans):
                carried = product_high(inclusive_maps[step], earlier) + carried
        elif step + 1 < len(spans):
            both = jnp.einsum(
                "shde,hef->shdf",
                jnp.stack([last_map, inclusive_maps[step]]),
                earlier,
                precision=lax.Precision.HIGH,
            )
            state = state + both[0]
            carried = both[1] + carried
        else:
            state = state + product_high(last_map, earlier)
    return (state, rider)


def expand_quantized(raw_rows, scales):
    head_count = scales.shape[1]
    width = raw_rows.shape[1] // head_count
    return raw_rows.astype(jnp.float32) * jnp.repeat(scales, width, axis=1)


def causal_filter(window, weights):
    kernel_span = weights.shape[0]
    row_count = window.shape[0] - kernel_span + 1
    summed = jnp.zeros((row_count, window.shape[1]), jnp.float32)
    for offset_tap in range(kernel_span):
        summed = summed + window[offset_tap : offset_tap + row_count] * weights[offset_tap].astype(
            jnp.float32
        )
    return lax.optimization_barrier(jax.nn.silu(summed).astype(jnp.bfloat16))


def unit_heads(conv_rows, head_width):
    row_count = conv_rows.shape[0]
    shaped = conv_rows.astype(jnp.float32).reshape(row_count, -1, head_width)
    return shaped * lax.rsqrt(jnp.sum(shaped * shaped, axis=-1, keepdims=True) + EPSILON)


def to_blocks(array, block):
    block_count = array.shape[0] // block
    return array.reshape(block_count, block, array.shape[1], -1).transpose(0, 2, 1, 3)


def to_block_rows(array, block):
    block_count = array.shape[0] // block
    return array.reshape(block_count, block, -1).transpose(0, 2, 1)


def unit_lower_inverse(strict_part):
    length = strict_part.shape[-1]
    eye = jnp.eye(length, dtype=jnp.float32)
    power = -strict_part
    inverse = eye + power
    span = 2
    if span < length:
        power = jnp.einsum("bhij,bhjk->bhik", power, power, precision=HIGHEST)
    while span < length:
        if 2 * span < length:
            both = jnp.einsum(
                "sbhij,sbhjk->sbhik",
                jnp.stack([inverse, power]),
                jnp.stack([eye + power, power]),
                precision=HIGHEST,
            )
            inverse, power = (both[0], both[1])
        else:
            inverse = jnp.einsum("bhij,bhjk->bhik", inverse, eye + power, precision=HIGHEST)
        span = span * 2
    return inverse


def block_maps(key_units, value_units, logdec, beta_units):
    length = logdec.shape[-1]
    positions = jnp.arange(length)
    lower_incl = positions[:, None] >= positions[None, :]
    lower_strict = positions[:, None] > positions[None, :]
    cumulative = jnp.cumsum(logdec, axis=-1)
    differ = cumulative[..., :, None] - cumulative[..., None, :]
    decay_incl = jnp.where(lower_incl, jnp.exp(jnp.where(lower_incl, differ, 0.0)), 0.0)
    decay_strict = jnp.where(lower_strict, decay_incl, 0.0)
    key_gram = jnp.einsum("bhid,bhjd->bhij", key_units, key_units, precision=HIGHEST)
    inverse = unit_lower_inverse(beta_units[..., :, None] * key_gram * decay_strict)
    growth = jnp.exp(cumulative)
    stacked = jnp.concatenate(
        [(beta_units * growth)[..., None] * key_units, beta_units[..., None] * value_units],
        axis=-1,
    )
    solved = jnp.einsum("bhij,bhjd->bhid", inverse, stacked, precision=HIGHEST)
    key_width = key_units.shape[-1]
    fading = jnp.exp(cumulative[..., -1:] - cumulative)[..., None] * key_units
    faded = jnp.einsum("bhjd,bhje->bhde", fading, solved, precision=HIGHEST)
    eye_key = jnp.eye(key_width, dtype=jnp.float32)
    transition = growth[..., -1][..., None, None] * eye_key - faded[..., :key_width]
    maps = jnp.concatenate([transition, faded[..., key_width:]], axis=-1)
    return (solved[..., key_width:], solved[..., :key_width], maps, decay_incl, growth)


def query_terms(queries, key_units, decay_incl, growth, weight_values, weight_keys):
    mixing = decay_incl * jnp.einsum("bhid,bhjd->bhij", queries, key_units, precision=HIGHEST)
    zero_out = jnp.einsum("bhij,bhjd->bhid", mixing, weight_values, precision=HIGHEST)
    readout = growth[..., None] * queries - jnp.einsum(
        "bhij,bhjd->bhid", mixing, weight_keys, precision=HIGHEST
    )
    return (zero_out, readout)


def product_high(left, right):
    return jnp.einsum("hde,hef->hdf", left, right, precision=lax.Precision.HIGH)


def product(left, right):
    return jnp.einsum("hde,hef->hdf", left, right, precision=HIGHEST)


def to_rows(blocks):
    return blocks.transpose(0, 2, 1, 3).reshape(-1, blocks.shape[1], blocks.shape[3])


def gated_norm(delta_rows, gate_raw, norm_gain):
    meansq = jnp.mean(delta_rows * delta_rows, axis=-1, keepdims=True)
    normed = delta_rows * lax.rsqrt(meansq + EPSILON) * norm_gain
    gate_float = gate_raw.astype(jnp.float32).reshape(delta_rows.shape)
    return (normed * jax.nn.silu(gate_float)).reshape(delta_rows.shape[0], -1).astype(jnp.bfloat16)


def shards(
    query_raw,
    key_raw,
    value_raw,
    query_scale,
    key_block_scale,
    value_scale,
    conv_query,
    key_filter_taps,
    conv_value,
    gate_input,
    beta_logit,
    decay_base,
    step_bias,
    output_gate,
    norm_gain,
):
    head_width = norm_gain.shape[0]
    margin = conv_query.shape[0] - 1
    query_deq = expand_quantized(query_raw, query_scale)
    key_deq = expand_quantized(key_raw, key_block_scale)
    value_deq = expand_quantized(value_raw, value_scale)
    query_width, key_width = (query_deq.shape[1], key_deq.shape[1])
    tails = from_behind(
        jnp.concatenate([query_deq[-margin:], key_deq[-margin:], value_deq[-margin:]], axis=1),
        "seq",
        1,
    )
    tail_rows = (
        tails[:, :query_width],
        tails[:, query_width : query_width + key_width],
        tails[:, query_width + key_width :],
    )
    local_heads = gate_input.shape[1]
    first_head = lax.axis_index("head") * local_heads
    base_part = lax.dynamic_slice_in_dim(decay_base, first_head, local_heads)
    bias_part = lax.dynamic_slice_in_dim(step_bias, first_head, local_heads)
    key_filtered = causal_filter(jnp.concatenate([tail_rows[1], key_deq], axis=0), key_filter_taps)
    row_count = key_filtered.shape[0]
    key_rows = unit_heads(key_filtered, head_width)
    repeats = local_heads // key_rows.shape[1]
    key_units = to_blocks(jnp.repeat(key_rows, repeats, axis=1), CH)
    logdec = -jnp.exp(base_part)[None, :] * jax.nn.softplus(gate_input + bias_part[None, :])
    logdec = to_block_rows(logdec, CH)
    beta_units = to_block_rows(jax.nn.sigmoid(beta_logit), CH)
    value_conv = causal_filter(jnp.concatenate([tail_rows[2], value_deq], axis=0), conv_value)
    value_units = to_blocks(value_conv.astype(jnp.float32).reshape(row_count, -1, head_width), CH)
    weight_values, weight_keys, maps, decay_incl, growth = block_maps(
        key_units, value_units, logdec, beta_units
    )
    key_width = key_units.shape[-1]
    device_map = maps[0]
    maps_before = [None]
    for block in range(1, maps.shape[0]):
        maps_before.append(device_map)
        device_map = jnp.einsum(
            "hde,hef->hdf", maps[block][..., :key_width], device_map, precision=HIGHEST
        ).at[..., key_width:].add(maps[block][..., key_width:])
    dev_trans, dev_offset = (device_map[..., :key_width], device_map[..., key_width:])
    incoming, query_window = scan_states(
        dev_trans, dev_offset, "seq", jnp.concatenate([tail_rows[0], query_deq], axis=0)
    )
    query_conv = causal_filter(query_window, conv_query)
    query_rows = unit_heads(query_conv, head_width) * head_width ** (-0.5)
    queries = to_blocks(jnp.repeat(query_rows, repeats, axis=1), CH)
    zero_out, readout = query_terms(
        queries, key_units, decay_incl, growth, weight_values, weight_keys
    )
    local_outs, read_maps = ([zero_out[0]], [readout[0]])
    for block in range(1, maps.shape[0]):
        read = jnp.einsum("hid,hde->hie", readout[block], maps_before[block], precision=HIGHEST)
        read_maps.append(read[..., :key_width])
        local_outs.append(zero_out[block] + read[..., key_width:])
    outputs = jnp.stack(local_outs) + jnp.einsum(
        "bhid,hde->bhie", jnp.stack(read_maps), incoming, precision=HIGHEST
    )
    gated_rows = gated_norm(to_rows(outputs), output_gate, norm_gain)
    return gated_rows


def solution(mesh):
    placed = (
        P("seq", "head"),
        P("seq", "head"),
        P("seq", "head"),
        P("seq", "head"),
        P("seq", "head"),
        P("seq", "head"),
        P(None, "head"),
        P(None, "head"),
        P(None, "head"),
        P("seq", "head"),
        P("seq", "head"),
        P(),
        P(),
        P("seq", "head"),
        P(),
    )
    return jax.shard_map(
        shards, mesh=mesh, in_specs=placed, out_specs=P("seq", "head"), check_vma=False
    )
```

```python
import jax
import jax.numpy as jnp
from jax import lax
from jax.sharding import PartitionSpec as P

CH = 64


HIGHEST = lax.Precision.HIGHEST
EPSILON = 1e-06


def from_behind(value, axis, steps):
    count = lax.axis_size(axis)
    first, last = (max(0, -steps), min(count, count - steps))
    return lax.ppermute(value, axis, [(source, source + steps) for source in range(first, last)])


def scan_states(trans, offset, axis, rider):
    devices, mine = (lax.axis_size(axis), lax.axis_index(axis))
    spans = []
    span = 1
    while span < devices:
        spans.append(span)
        span = span * 2
    eye = jnp.eye(trans.shape[-1], dtype=jnp.float32)
    inclusive_maps, exclusive_maps = ([], [None])
    inclusive = trans
    for span in spans[:-1]:
        pairs = [(source, source + span) for source in range(devices - span)]
        inclusive_maps.append(inclusive)
        reached = jnp.where(mine >= span, 1.0, 0.0)
        earlier = lax.ppermute((inclusive - eye).astype(jnp.bfloat16), axis, pairs)
        earlier = earlier.astype(jnp.float32) + reached * eye
        last_map = exclusive_maps[-1]
        if last_map is None or 4 * span >= devices:
            exclusive_maps.append(earlier if last_map is None else product(last_map, earlier))
            if 4 * span < devices:
                inclusive = jnp.where(mine >= span, product(inclusive, earlier), inclusive)
        else:
            both = jnp.einsum(
                "shde,hef->shdf", jnp.stack([last_map, inclusive]), earlier, precision=HIGHEST
            )
            exclusive_maps.append(both[0])
            inclusive = jnp.where(mine >= span, both[1], inclusive)
    state = jnp.zeros_like(offset)
    carried = offset
    final_map, final_state = (None, None)
    for step, span in enumerate(spans):
        pairs = [(source, source + span) for source in range(devices - span)]
        earlier = lax.ppermute(carried.astype(jnp.bfloat16), axis, pairs)
        if step == 0:
            rider, earlier = lax.optimization_barrier((rider, earlier))
        earlier = earlier.astype(jnp.float32)
        last_map = exclusive_maps[step]
        if last_map is None:
            state = earlier
            if step + 1 < len(spans):
                carried = product(inclusive_maps[step], earlier) + carried
        elif step + 1 < len(spans):
            both = jnp.einsum(
                "shde,hef->shdf",
                jnp.stack([last_map, inclusive_maps[step]]),
                earlier,
                precision=HIGHEST,
            )
            state = state + both[0]
            carried = both[1] + carried
        else:
            final_map, final_state = (last_map, earlier)
    return (state, final_map, final_state, rider)


def expand_quantized(raw_rows, scales):
    head_count = scales.shape[1]
    width = raw_rows.shape[1] // head_count
    return raw_rows.astype(jnp.float32) * jnp.repeat(scales, width, axis=1)


def causal_filter(window, weights):
    kernel_span = weights.shape[0]
    row_count = window.shape[0] - kernel_span + 1
    summed = jnp.zeros((row_count, window.shape[1]), jnp.float32)
    for offset_tap in range(kernel_span):
        summed = summed + window[offset_tap : offset_tap + row_count] * weights[offset_tap].astype(
            jnp.float32
        )
    return lax.optimization_barrier(jax.nn.silu(summed).astype(jnp.bfloat16))


def unit_heads(conv_rows, head_width):
    row_count = conv_rows.shape[0]
    shaped = conv_rows.astype(jnp.float32).reshape(row_count, -1, head_width)
    return shaped * lax.rsqrt(jnp.sum(shaped * shaped, axis=-1, keepdims=True) + EPSILON)


def to_blocks(array, block):
    block_count = array.shape[0] // block
    return array.reshape(block_count, block, array.shape[1], -1).transpose(0, 2, 1, 3)


def to_block_rows(array, block):
    block_count = array.shape[0] // block
    return array.reshape(block_count, block, -1).transpose(0, 2, 1)


def unit_lower_inverse(strict_part):
    length = strict_part.shape[-1]
    eye = jnp.eye(length, dtype=jnp.float32)
    power = -strict_part
    inverse = eye + power
    span = 2
    if span < length:
        power = jnp.einsum("bhij,bhjk->bhik", power, power, precision=HIGHEST)
    while span < length:
        if 2 * span < length:
            both = jnp.einsum(
                "sbhij,sbhjk->sbhik",
                jnp.stack([inverse, power]),
                jnp.stack([eye + power, power]),
                precision=HIGHEST,
            )
            inverse, power = (both[0], both[1])
        else:
            inverse = jnp.einsum("bhij,bhjk->bhik", inverse, eye + power, precision=HIGHEST)
        span = span * 2
    return inverse


def block_maps(key_units, value_units, logdec, beta_units):
    length = logdec.shape[-1]
    positions = jnp.arange(length)
    lower_incl = positions[:, None] >= positions[None, :]
    lower_strict = positions[:, None] > positions[None, :]
    cumulative = jnp.cumsum(logdec, axis=-1)
    differ = cumulative[..., :, None] - cumulative[..., None, :]
    decay_incl = jnp.where(lower_incl, jnp.exp(jnp.where(lower_incl, differ, 0.0)), 0.0)
    decay_strict = jnp.where(lower_strict, decay_incl, 0.0)
    key_gram = jnp.einsum("bhid,bhjd->bhij", key_units, key_units, precision=HIGHEST)
    inverse = unit_lower_inverse(beta_units[..., :, None] * key_gram * decay_strict)
    growth = jnp.exp(cumulative)
    stacked = jnp.concatenate(
        [(beta_units * growth)[..., None] * key_units, beta_units[..., None] * value_units],
        axis=-1,
    )
    solved = jnp.einsum("bhij,bhjd->bhid", inverse, stacked, precision=HIGHEST)
    key_width = key_units.shape[-1]
    fading = jnp.exp(cumulative[..., -1:] - cumulative)[..., None] * key_units
    faded = jnp.einsum("bhjd,bhje->bhde", fading, solved, precision=HIGHEST)
    eye_key = jnp.eye(key_width, dtype=jnp.float32)
    transition = growth[..., -1][..., None, None] * eye_key - faded[..., :key_width]
    maps = jnp.concatenate([transition, faded[..., key_width:]], axis=-1)
    return (solved[..., key_width:], solved[..., :key_width], maps, decay_incl, growth)


def query_terms(queries, key_units, decay_incl, growth, weight_values, weight_keys):
    mixing = decay_incl * jnp.einsum("bhid,bhjd->bhij", queries, key_units, precision=HIGHEST)
    zero_out = jnp.einsum("bhij,bhjd->bhid", mixing, weight_values, precision=HIGHEST)
    readout = growth[..., None] * queries - jnp.einsum(
        "bhij,bhjd->bhid", mixing, weight_keys, precision=HIGHEST
    )
    return (zero_out, readout)


def product(left, right):
    return jnp.einsum("hde,hef->hdf", left, right, precision=HIGHEST)


def to_rows(blocks):
    return blocks.transpose(0, 2, 1, 3).reshape(-1, blocks.shape[1], blocks.shape[3])


def gated_norm(delta_rows, gate_raw, norm_gain):
    meansq = jnp.mean(delta_rows * delta_rows, axis=-1, keepdims=True)
    normed = delta_rows * lax.rsqrt(meansq + EPSILON) * norm_gain
    gate_float = gate_raw.astype(jnp.float32).reshape(delta_rows.shape)
    return (normed * jax.nn.silu(gate_float)).reshape(delta_rows.shape[0], -1).astype(jnp.bfloat16)


def shards(
    query_raw,
    key_raw,
    value_raw,
    query_scale,
    key_block_scale,
    value_scale,
    conv_query,
    key_filter_taps,
    conv_value,
    gate_input,
    beta_logit,
    decay_base,
    step_bias,
    output_gate,
    norm_gain,
):
    head_width = norm_gain.shape[0]
    margin = conv_query.shape[0] - 1
    query_deq = expand_quantized(query_raw, query_scale)
    key_deq = expand_quantized(key_raw, key_block_scale)
    value_deq = expand_quantized(value_raw, value_scale)
    query_width, key_width = (query_deq.shape[1], key_deq.shape[1])
    tails = from_behind(
        jnp.concatenate([query_deq[-margin:], key_deq[-margin:], value_deq[-margin:]], axis=1),
        "seq",
        1,
    )
    tail_rows = (
        tails[:, :query_width],
        tails[:, query_width : query_width + key_width],
        tails[:, query_width + key_width :],
    )
    local_heads = gate_input.shape[1]
    first_head = lax.axis_index("head") * local_heads
    base_part = lax.dynamic_slice_in_dim(decay_base, first_head, local_heads)
    bias_part = lax.dynamic_slice_in_dim(step_bias, first_head, local_heads)
    key_filtered = causal_filter(jnp.concatenate([tail_rows[1], key_deq], axis=0), key_filter_taps)
    row_count = key_filtered.shape[0]
    key_rows = unit_heads(key_filtered, head_width)
    repeats = local_heads // key_rows.shape[1]
    key_units = to_blocks(jnp.repeat(key_rows, repeats, axis=1), CH)
    logdec = -jnp.exp(base_part)[None, :] * jax.nn.softplus(gate_input + bias_part[None, :])
    logdec = to_block_rows(logdec, CH)
    beta_units = to_block_rows(jax.nn.sigmoid(beta_logit), CH)
    value_conv = causal_filter(jnp.concatenate([tail_rows[2], value_deq], axis=0), conv_value)
    value_units = to_blocks(value_conv.astype(jnp.float32).reshape(row_count, -1, head_width), CH)
    weight_values, weight_keys, maps, decay_incl, growth = block_maps(
        key_units, value_units, logdec, beta_units
    )
    key_width = key_units.shape[-1]
    device_map = maps[0]
    maps_before = [None]
    for block in range(1, maps.shape[0]):
        maps_before.append(device_map)
        device_map = jnp.einsum(
            "hde,hef->hdf", maps[block][..., :key_width], device_map, precision=HIGHEST
        ).at[..., key_width:].add(maps[block][..., key_width:])
    dev_trans, dev_offset = (device_map[..., :key_width], device_map[..., key_width:])
    incoming, final_map, final_state, query_window = scan_states(
        dev_trans, dev_offset, "seq", jnp.concatenate([tail_rows[0], query_deq], axis=0)
    )
    query_conv = causal_filter(query_window, conv_query)
    query_rows = unit_heads(query_conv, head_width) * head_width ** (-0.5)
    queries = to_blocks(jnp.repeat(query_rows, repeats, axis=1), CH)
    zero_out, readout = query_terms(
        queries, key_units, decay_incl, growth, weight_values, weight_keys
    )
    local_outs, read_maps = ([zero_out[0]], [readout[0]])
    for block in range(1, maps.shape[0]):
        read = jnp.einsum("hid,hde->hie", readout[block], maps_before[block], precision=HIGHEST)
        read_maps.append(read[..., :key_width])
        local_outs.append(zero_out[block] + read[..., key_width:])
    reads = jnp.stack(read_maps)
    outputs = jnp.stack(local_outs) + jnp.einsum(
        "bhid,hde->bhie", reads, incoming, precision=HIGHEST
    )
    if final_map is not None:
        lead = jnp.einsum("bhid,hde->bhie", reads, final_map, precision=HIGHEST)
        outputs = outputs + jnp.einsum("bhid,hde->bhie", lead, final_state, precision=HIGHEST)
    gated_rows = gated_norm(to_rows(outputs), output_gate, norm_gain)
    return gated_rows


def solution(mesh):
    placed = (
        P("seq", "head"),
        P("seq", "head"),
        P("seq", "head"),
        P("seq", "head"),
        P("seq", "head"),
        P("seq", "head"),
        P(None, "head"),
        P(None, "head"),
        P(None, "head"),
        P("seq", "head"),
        P("seq", "head"),
        P(),
        P(),
        P("seq", "head"),
        P(),
    )
    return jax.shard_map(
        shards, mesh=mesh, in_specs=placed, out_specs=P("seq", "head"), check_vma=False
    )
```

```python
import jax
import jax.numpy as jnp
from jax import lax
from jax.sharding import PartitionSpec as P

CH = 64


HIGHEST = lax.Precision.HIGHEST
EPSILON = 1e-06


def from_behind(value, axis, steps):
    count = lax.axis_size(axis)
    first, last = (max(0, -steps), min(count, count - steps))
    return lax.ppermute(value, axis, [(source, source + steps) for source in range(first, last)])


def scan_states(trans, offset, axis, rider):
    devices, mine = (lax.axis_size(axis), lax.axis_index(axis))
    spans = []
    span = 1
    while span < devices:
        spans.append(span)
        span = span * 2
    eye = jnp.eye(trans.shape[-1], dtype=jnp.float32)
    inclusive_maps, exclusive_maps = ([], [None])
    inclusive = trans
    for span in spans[:-1]:
        pairs = [(source, source + span) for source in range(devices - span)]
        inclusive_maps.append(inclusive)
        reached = jnp.where(mine >= span, 1.0, 0.0)
        earlier = lax.ppermute((inclusive - eye).astype(jnp.bfloat16), axis, pairs)
        earlier = earlier.astype(jnp.float32) + reached * eye
        last_map = exclusive_maps[-1]
        if last_map is None or 4 * span >= devices:
            exclusive_maps.append(earlier if last_map is None else product(last_map, earlier))
            if 4 * span < devices:
                inclusive = jnp.where(mine >= span, product(inclusive, earlier), inclusive)
        else:
            both = jnp.einsum(
                "shde,hef->shdf", jnp.stack([last_map, inclusive]), earlier, precision=HIGHEST
            )
            exclusive_maps.append(both[0])
            inclusive = jnp.where(mine >= span, both[1], inclusive)
    state = jnp.zeros_like(offset)
    carried = offset
    final_map, final_state = (None, None)
    for step, span in enumerate(spans):
        pairs = [(source, source + span) for source in range(devices - span)]
        earlier = lax.ppermute(carried.astype(jnp.bfloat16), axis, pairs)
        if step == 0:
            rider, earlier = lax.optimization_barrier((rider, earlier))
        earlier = earlier.astype(jnp.float32)
        last_map = exclusive_maps[step]
        if last_map is None:
            state = earlier
            if step + 1 < len(spans):
                carried = product(inclusive_maps[step], earlier) + carried
        elif step + 1 < len(spans):
            carried = product(inclusive_maps[step], earlier) + carried
            state = state + product(last_map, earlier)
        else:
            final_map, final_state = (last_map, earlier)
    return (state, final_map, final_state, rider)


def expand_quantized(raw_rows, scales):
    head_count = scales.shape[1]
    width = raw_rows.shape[1] // head_count
    return raw_rows.astype(jnp.float32) * jnp.repeat(scales, width, axis=1)


def causal_filter(window, weights):
    kernel_span = weights.shape[0]
    row_count = window.shape[0] - kernel_span + 1
    summed = jnp.zeros((row_count, window.shape[1]), jnp.float32)
    for offset_tap in range(kernel_span):
        summed = summed + window[offset_tap : offset_tap + row_count] * weights[offset_tap].astype(
            jnp.float32
        )
    return lax.optimization_barrier(jax.nn.silu(summed).astype(jnp.bfloat16))


def unit_heads(conv_rows, head_width):
    row_count = conv_rows.shape[0]
    shaped = conv_rows.astype(jnp.float32).reshape(row_count, -1, head_width)
    return shaped * lax.rsqrt(jnp.sum(shaped * shaped, axis=-1, keepdims=True) + EPSILON)


def to_blocks(array, block):
    block_count = array.shape[0] // block
    return array.reshape(block_count, block, array.shape[1], -1).transpose(0, 2, 1, 3)


def to_block_rows(array, block):
    block_count = array.shape[0] // block
    return array.reshape(block_count, block, -1).transpose(0, 2, 1)


def unit_lower_inverse(strict_part):
    length = strict_part.shape[-1]
    eye = jnp.eye(length, dtype=jnp.float32)
    power = -strict_part
    inverse = eye + power
    span = 2
    if span < length:
        power = jnp.einsum("bhij,bhjk->bhik", power, power, precision=HIGHEST)
    while span < length:
        if 2 * span < length:
            both = jnp.einsum(
                "sbhij,sbhjk->sbhik",
                jnp.stack([inverse, power]),
                jnp.stack([eye + power, power]),
                precision=HIGHEST,
            )
            inverse, power = (both[0], both[1])
        else:
            inverse = jnp.einsum("bhij,bhjk->bhik", inverse, eye + power, precision=HIGHEST)
        span = span * 2
    return inverse


def block_maps(key_units, value_units, logdec, beta_units):
    length = logdec.shape[-1]
    positions = jnp.arange(length)
    lower_incl = positions[:, None] >= positions[None, :]
    lower_strict = positions[:, None] > positions[None, :]
    cumulative = jnp.cumsum(logdec, axis=-1)
    differ = cumulative[..., :, None] - cumulative[..., None, :]
    decay_incl = jnp.where(lower_incl, jnp.exp(jnp.where(lower_incl, differ, 0.0)), 0.0)
    decay_strict = jnp.where(lower_strict, decay_incl, 0.0)
    key_gram = jnp.einsum("bhid,bhjd->bhij", key_units, key_units, precision=HIGHEST)
    inverse = unit_lower_inverse(beta_units[..., :, None] * key_gram * decay_strict)
    growth = jnp.exp(cumulative)
    stacked = jnp.concatenate(
        [(beta_units * growth)[..., None] * key_units, beta_units[..., None] * value_units],
        axis=-1,
    )
    solved = jnp.einsum("bhij,bhjd->bhid", inverse, stacked, precision=HIGHEST)
    key_width = key_units.shape[-1]
    fading = jnp.exp(cumulative[..., -1:] - cumulative)[..., None] * key_units
    faded = jnp.einsum("bhjd,bhje->bhde", fading, solved, precision=HIGHEST)
    eye_key = jnp.eye(key_width, dtype=jnp.float32)
    transition = growth[..., -1][..., None, None] * eye_key - faded[..., :key_width]
    maps = jnp.concatenate([transition, faded[..., key_width:]], axis=-1)
    return (solved[..., key_width:], solved[..., :key_width], maps, decay_incl, growth)


def query_terms(queries, key_units, decay_incl, growth, weight_values, weight_keys):
    mixing = decay_incl * jnp.einsum("bhid,bhjd->bhij", queries, key_units, precision=HIGHEST)
    zero_out = jnp.einsum("bhij,bhjd->bhid", mixing, weight_values, precision=HIGHEST)
    readout = growth[..., None] * queries - jnp.einsum(
        "bhij,bhjd->bhid", mixing, weight_keys, precision=HIGHEST
    )
    return (zero_out, readout)


def product(left, right):
    return jnp.einsum("hde,hef->hdf", left, right, precision=HIGHEST)


def to_rows(blocks):
    return blocks.transpose(0, 2, 1, 3).reshape(-1, blocks.shape[1], blocks.shape[3])


def gated_norm(delta_rows, gate_raw, norm_gain):
    meansq = jnp.mean(delta_rows * delta_rows, axis=-1, keepdims=True)
    normed = delta_rows * lax.rsqrt(meansq + EPSILON) * norm_gain
    gate_float = gate_raw.astype(jnp.float32).reshape(delta_rows.shape)
    return (normed * jax.nn.silu(gate_float)).reshape(delta_rows.shape[0], -1).astype(jnp.bfloat16)


def shards(
    query_raw,
    key_raw,
    value_raw,
    query_scale,
    key_block_scale,
    value_scale,
    conv_query,
    key_filter_taps,
    conv_value,
    gate_input,
    beta_logit,
    decay_base,
    step_bias,
    output_gate,
    norm_gain,
):
    head_width = norm_gain.shape[0]
    margin = conv_query.shape[0] - 1
    query_deq = expand_quantized(query_raw, query_scale)
    key_deq = expand_quantized(key_raw, key_block_scale)
    value_deq = expand_quantized(value_raw, value_scale)
    query_width, key_width = (query_deq.shape[1], key_deq.shape[1])
    tails = from_behind(
        jnp.concatenate([query_deq[-margin:], key_deq[-margin:], value_deq[-margin:]], axis=1),
        "seq",
        1,
    )
    tail_rows = (
        tails[:, :query_width],
        tails[:, query_width : query_width + key_width],
        tails[:, query_width + key_width :],
    )
    local_heads = gate_input.shape[1]
    first_head = lax.axis_index("head") * local_heads
    base_part = lax.dynamic_slice_in_dim(decay_base, first_head, local_heads)
    bias_part = lax.dynamic_slice_in_dim(step_bias, first_head, local_heads)
    key_filtered = causal_filter(jnp.concatenate([tail_rows[1], key_deq], axis=0), key_filter_taps)
    row_count = key_filtered.shape[0]
    key_rows = unit_heads(key_filtered, head_width)
    repeats = local_heads // key_rows.shape[1]
    key_units = to_blocks(jnp.repeat(key_rows, repeats, axis=1), CH)
    logdec = -jnp.exp(base_part)[None, :] * jax.nn.softplus(gate_input + bias_part[None, :])
    logdec = to_block_rows(logdec, CH)
    beta_units = to_block_rows(jax.nn.sigmoid(beta_logit), CH)
    value_conv = causal_filter(jnp.concatenate([tail_rows[2], value_deq], axis=0), conv_value)
    value_units = to_blocks(value_conv.astype(jnp.float32).reshape(row_count, -1, head_width), CH)
    weight_values, weight_keys, maps, decay_incl, growth = block_maps(
        key_units, value_units, logdec, beta_units
    )
    key_width = key_units.shape[-1]
    device_map = maps[0]
    maps_before = [None]
    for block in range(1, maps.shape[0]):
        maps_before.append(device_map)
        device_map = jnp.einsum(
            "hde,hef->hdf", maps[block][..., :key_width], device_map, precision=HIGHEST
        ).at[..., key_width:].add(maps[block][..., key_width:])
    dev_trans, dev_offset = (device_map[..., :key_width], device_map[..., key_width:])
    incoming, final_map, final_state, query_window = scan_states(
        dev_trans, dev_offset, "seq", jnp.concatenate([tail_rows[0], query_deq], axis=0)
    )
    query_conv = causal_filter(query_window, conv_query)
    query_rows = unit_heads(query_conv, head_width) * head_width ** (-0.5)
    queries = to_blocks(jnp.repeat(query_rows, repeats, axis=1), CH)
    zero_out, readout = query_terms(
        queries, key_units, decay_incl, growth, weight_values, weight_keys
    )
    local_outs, read_maps = ([zero_out[0]], [readout[0]])
    for block in range(1, maps.shape[0]):
        read = jnp.einsum("hid,hde->hie", readout[block], maps_before[block], precision=HIGHEST)
        read_maps.append(read[..., :key_width])
        local_outs.append(zero_out[block] + read[..., key_width:])
    reads = jnp.stack(read_maps)
    outputs = jnp.stack(local_outs) + jnp.einsum(
        "bhid,hde->bhie", reads, incoming, precision=HIGHEST
    )
    if final_map is not None:
        lead = jnp.einsum("bhid,hde->bhie", reads, final_map, precision=HIGHEST)
        outputs = outputs + jnp.einsum("bhid,hde->bhie", lead, final_state, precision=HIGHEST)
    gated_rows = gated_norm(to_rows(outputs), output_gate, norm_gain)
    return gated_rows


def solution(mesh):
    placed = (
        P("seq", "head"),
        P("seq", "head"),
        P("seq", "head"),
        P("seq", "head"),
        P("seq", "head"),
        P("seq", "head"),
        P(None, "head"),
        P(None, "head"),
        P(None, "head"),
        P("seq", "head"),
        P("seq", "head"),
        P(),
        P(),
        P("seq", "head"),
        P(),
    )
    return jax.shard_map(
        shards, mesh=mesh, in_specs=placed, out_specs=P("seq", "head"), check_vma=False
    )
```

```python
import jax
import jax.numpy as jnp
from jax import lax
from jax.sharding import PartitionSpec as P

CH = 64


HIGHEST = lax.Precision.HIGHEST
EPSILON = 1e-06


def from_behind(value, axis, steps):
    count = lax.axis_size(axis)
    first, last = (max(0, -steps), min(count, count - steps))
    return lax.ppermute(value, axis, [(source, source + steps) for source in range(first, last)])


def scan_states(trans, offset, axis, rider):
    devices, mine = (lax.axis_size(axis), lax.axis_index(axis))
    spans = []
    span = 1
    while span < devices:
        spans.append(span)
        span = span * 2
    eye = jnp.eye(trans.shape[-1], dtype=jnp.float32)
    inclusive_maps, exclusive_maps = ([], [None])
    inclusive = trans
    for span in spans[:-1]:
        pairs = [(source, source + span) for source in range(devices - span)]
        inclusive_maps.append(inclusive)
        reached = jnp.where(mine >= span, 1.0, 0.0)
        earlier = lax.ppermute((inclusive - eye).astype(jnp.bfloat16), axis, pairs)
        earlier = earlier.astype(jnp.float32) + reached * eye
        last_map = exclusive_maps[-1]
        if last_map is None or 4 * span >= devices:
            exclusive_maps.append(earlier if last_map is None else product(last_map, earlier))
            if 4 * span < devices:
                inclusive = jnp.where(mine >= span, product(inclusive, earlier), inclusive)
        else:
            both = jnp.einsum(
                "shde,hef->shdf", jnp.stack([last_map, inclusive]), earlier, precision=HIGHEST
            )
            exclusive_maps.append(both[0])
            inclusive = jnp.where(mine >= span, both[1], inclusive)
    state = jnp.zeros_like(offset)
    carried = offset
    final_map, final_state = (None, None)
    for step, span in enumerate(spans):
        pairs = [(source, source + span) for source in range(devices - span)]
        earlier = lax.ppermute(carried.astype(jnp.bfloat16), axis, pairs)
        if step == 0:
            rider, earlier = lax.optimization_barrier((rider, earlier))
        earlier = earlier.astype(jnp.float32)
        last_map = exclusive_maps[step]
        if last_map is None:
            state = earlier
            if step + 1 < len(spans):
                carried = product(inclusive_maps[step], earlier) + carried
        elif step + 1 < len(spans):
            both = jnp.einsum(
                "shde,hef->shdf",
                jnp.stack([last_map, inclusive_maps[step]]),
                earlier,
                precision=HIGHEST,
            )
            state = state + both[0]
            carried = both[1] + carried
        else:
            final_map, final_state = (last_map, earlier)
    return (state, final_map, final_state, rider)


def expand_quantized(raw_rows, scales):
    head_count = scales.shape[1]
    width = raw_rows.shape[1] // head_count
    return raw_rows.astype(jnp.float32) * jnp.repeat(scales, width, axis=1)


def causal_filter(window, weights):
    kernel_span = weights.shape[0]
    row_count = window.shape[0] - kernel_span + 1
    summed = jnp.zeros((row_count, window.shape[1]), jnp.float32)
    for offset_tap in range(kernel_span):
        summed = summed + window[offset_tap : offset_tap + row_count] * weights[offset_tap].astype(
            jnp.float32
        )
    return lax.optimization_barrier(jax.nn.silu(summed).astype(jnp.bfloat16))


def unit_heads(conv_rows, head_width):
    row_count = conv_rows.shape[0]
    shaped = conv_rows.astype(jnp.float32).reshape(row_count, -1, head_width)
    return shaped * lax.rsqrt(jnp.sum(shaped * shaped, axis=-1, keepdims=True) + EPSILON)


def to_blocks(array, block):
    block_count = array.shape[0] // block
    return array.reshape(block_count, block, array.shape[1], -1).transpose(0, 2, 1, 3)


def to_block_rows(array, block):
    block_count = array.shape[0] // block
    return array.reshape(block_count, block, -1).transpose(0, 2, 1)


def unit_lower_inverse(strict_part):
    length = strict_part.shape[-1]
    eye = jnp.eye(length, dtype=jnp.float32)
    power = -strict_part
    inverse = eye + power
    span = 2
    if span < length:
        power = jnp.einsum("bhij,bhjk->bhik", power, power, precision=HIGHEST)
    while span < length:
        if 2 * span < length:
            both = jnp.einsum(
                "sbhij,sbhjk->sbhik",
                jnp.stack([inverse, power]),
                jnp.stack([eye + power, power]),
                precision=HIGHEST,
            )
            inverse, power = (both[0], both[1])
        else:
            inverse = jnp.einsum("bhij,bhjk->bhik", inverse, eye + power, precision=HIGHEST)
        span = span * 2
    return inverse


def block_maps(key_units, value_units, logdec, beta_units):
    length = logdec.shape[-1]
    positions = jnp.arange(length)
    lower_incl = positions[:, None] >= positions[None, :]
    lower_strict = positions[:, None] > positions[None, :]
    cumulative = jnp.cumsum(logdec, axis=-1)
    differ = cumulative[..., :, None] - cumulative[..., None, :]
    decay_incl = jnp.where(lower_incl, jnp.exp(jnp.where(lower_incl, differ, 0.0)), 0.0)
    decay_strict = jnp.where(lower_strict, decay_incl, 0.0)
    key_gram = jnp.einsum("bhid,bhjd->bhij", key_units, key_units, precision=HIGHEST)
    inverse = unit_lower_inverse(beta_units[..., :, None] * key_gram * decay_strict)
    growth = jnp.exp(cumulative)
    stacked = jnp.concatenate(
        [(beta_units * growth)[..., None] * key_units, beta_units[..., None] * value_units],
        axis=-1,
    )
    solved = jnp.einsum("bhij,bhjd->bhid", inverse, stacked, precision=HIGHEST)
    key_width = key_units.shape[-1]
    fading = jnp.exp(cumulative[..., -1:] - cumulative)[..., None] * key_units
    faded = jnp.einsum("bhjd,bhje->bhde", fading, solved, precision=HIGHEST)
    eye_key = jnp.eye(key_width, dtype=jnp.float32)
    transition = growth[..., -1][..., None, None] * eye_key - faded[..., :key_width]
    maps = jnp.concatenate([transition, faded[..., key_width:]], axis=-1)
    return (solved[..., key_width:], solved[..., :key_width], maps, decay_incl, growth)


def query_terms(queries, key_units, decay_incl, growth, weight_values, weight_keys):
    mixing = decay_incl * jnp.einsum("bhid,bhjd->bhij", queries, key_units, precision=HIGHEST)
    zero_out = jnp.einsum("bhij,bhjd->bhid", mixing, weight_values, precision=HIGHEST)
    readout = growth[..., None] * queries - jnp.einsum(
        "bhij,bhjd->bhid", mixing, weight_keys, precision=HIGHEST
    )
    return (zero_out, readout)


def product(left, right):
    return jnp.einsum("hde,hef->hdf", left, right, precision=HIGHEST)


def to_rows(blocks):
    return blocks.transpose(0, 2, 1, 3).reshape(-1, blocks.shape[1], blocks.shape[3])


def gated_norm(delta_rows, gate_raw, norm_gain):
    meansq = jnp.mean(delta_rows * delta_rows, axis=-1, keepdims=True)
    normed = delta_rows * lax.rsqrt(meansq + EPSILON) * norm_gain
    gate_float = gate_raw.astype(jnp.float32).reshape(delta_rows.shape)
    return (normed * jax.nn.silu(gate_float)).reshape(delta_rows.shape[0], -1).astype(jnp.bfloat16)


def shards(
    query_raw,
    key_raw,
    value_raw,
    query_scale,
    key_block_scale,
    value_scale,
    conv_query,
    key_filter_taps,
    conv_value,
    gate_input,
    beta_logit,
    decay_base,
    step_bias,
    output_gate,
    norm_gain,
):
    head_width = norm_gain.shape[0]
    margin = conv_query.shape[0] - 1
    query_deq = expand_quantized(query_raw, query_scale)
    key_deq = expand_quantized(key_raw, key_block_scale)
    value_deq = expand_quantized(value_raw, value_scale)
    query_width, key_width = (query_deq.shape[1], key_deq.shape[1])
    tails = from_behind(
        jnp.concatenate([query_deq[-margin:], key_deq[-margin:], value_deq[-margin:]], axis=1),
        "seq",
        1,
    )
    tail_rows = (
        tails[:, :query_width],
        tails[:, query_width : query_width + key_width],
        tails[:, query_width + key_width :],
    )
    local_heads = gate_input.shape[1]
    first_head = lax.axis_index("head") * local_heads
    base_part = lax.dynamic_slice_in_dim(decay_base, first_head, local_heads)
    bias_part = lax.dynamic_slice_in_dim(step_bias, first_head, local_heads)
    key_filtered = causal_filter(jnp.concatenate([tail_rows[1], key_deq], axis=0), key_filter_taps)
    row_count = key_filtered.shape[0]
    key_rows = unit_heads(key_filtered, head_width)
    repeats = local_heads // key_rows.shape[1]
    key_units = to_blocks(jnp.repeat(key_rows, repeats, axis=1), CH)
    logdec = -jnp.exp(base_part)[None, :] * jax.nn.softplus(gate_input + bias_part[None, :])
    logdec = to_block_rows(logdec, CH)
    beta_units = to_block_rows(jax.nn.sigmoid(beta_logit), CH)
    value_conv = causal_filter(jnp.concatenate([tail_rows[2], value_deq], axis=0), conv_value)
    value_units = to_blocks(value_conv.astype(jnp.float32).reshape(row_count, -1, head_width), CH)
    weight_values, weight_keys, maps, decay_incl, growth = block_maps(
        key_units, value_units, logdec, beta_units
    )
    key_width = key_units.shape[-1]
    device_map = maps[0]
    maps_before = [None]
    for block in range(1, maps.shape[0]):
        maps_before.append(device_map)
        device_map = jnp.einsum(
            "hde,hef->hdf", maps[block][..., :key_width], device_map, precision=HIGHEST
        ).at[..., key_width:].add(maps[block][..., key_width:])
    dev_trans, dev_offset = (device_map[..., :key_width], device_map[..., key_width:])
    incoming, final_map, final_state, query_window = scan_states(
        dev_trans, dev_offset, "seq", jnp.concatenate([tail_rows[0], query_deq], axis=0)
    )
    query_conv = causal_filter(query_window, conv_query)
    query_rows = unit_heads(query_conv, head_width) * head_width ** (-0.5)
    queries = to_blocks(jnp.repeat(query_rows, repeats, axis=1), CH)
    zero_out, readout = query_terms(
        queries, key_units, decay_incl, growth, weight_values, weight_keys
    )
    local_outs, read_maps = ([zero_out[0]], [readout[0]])
    for block in range(1, maps.shape[0]):
        read = jnp.einsum("hid,hde->hie", readout[block], maps_before[block], precision=HIGHEST)
        read_maps.append(read[..., :key_width])
        local_outs.append(zero_out[block] + read[..., key_width:])
    reads = jnp.stack(read_maps)
    state_width = incoming.shape[-1]
    if final_map is None:
        outputs = jnp.stack(local_outs) + jnp.einsum(
            "bhid,hde->bhie", reads, incoming, precision=HIGHEST
        )
    else:
        both = jnp.einsum(
            "bhid,hde->bhie",
            reads,
            jnp.concatenate([incoming, final_map], axis=-1),
            precision=HIGHEST,
        )
        outputs = (
            jnp.stack(local_outs)
            + both[..., :state_width]
            + jnp.einsum(
                "bhid,hde->bhie", both[..., state_width:], final_state, precision=HIGHEST
            )
        )
    gated_rows = gated_norm(to_rows(outputs), output_gate, norm_gain)
    return gated_rows


def solution(mesh):
    placed = (
        P("seq", "head"),
        P("seq", "head"),
        P("seq", "head"),
        P("seq", "head"),
        P("seq", "head"),
        P("seq", "head"),
        P(None, "head"),
        P(None, "head"),
        P(None, "head"),
        P("seq", "head"),
        P("seq", "head"),
        P(),
        P(),
        P("seq", "head"),
        P(),
    )
    return jax.shard_map(
        shards, mesh=mesh, in_specs=placed, out_specs=P("seq", "head"), check_vma=False
    )
```

```python
import jax
import jax.numpy as jnp
from jax import lax
from jax.sharding import PartitionSpec as P

CH = 64


HIGHEST = lax.Precision.HIGHEST
EPSILON = 1e-06


def from_behind(value, axis, steps):
    count = lax.axis_size(axis)
    first, last = (max(0, -steps), min(count, count - steps))
    return lax.ppermute(value, axis, [(source, source + steps) for source in range(first, last)])


def scan_states(trans, offset, axis, rider):
    devices, mine = (lax.axis_size(axis), lax.axis_index(axis))
    spans = []
    span = 1
    while span < devices:
        spans.append(span)
        span = span * 2
    eye = jnp.eye(trans.shape[-1], dtype=jnp.float32)
    inclusive_maps, exclusive_maps = ([], [None])
    inclusive = trans
    for span in spans[:-1]:
        pairs = [(source, source + span) for source in range(devices - span)]
        inclusive_maps.append(inclusive)
        reached = jnp.where(mine >= span, 1.0, 0.0)
        earlier = lax.ppermute((inclusive - eye).astype(jnp.bfloat16), axis, pairs)
        earlier = earlier.astype(jnp.float32) + reached * eye
        last_map = exclusive_maps[-1]
        if last_map is None or 4 * span >= devices:
            exclusive_maps.append(earlier if last_map is None else product(last_map, earlier))
            if 4 * span < devices:
                inclusive = jnp.where(mine >= span, product(inclusive, earlier), inclusive)
        else:
            both = jnp.einsum(
                "shde,hef->shdf", jnp.stack([last_map, inclusive]), earlier, precision=HIGHEST
            )
            exclusive_maps.append(both[0])
            inclusive = jnp.where(mine >= span, both[1], inclusive)
    state = jnp.zeros_like(offset)
    carried = offset
    final_map, final_state = (None, None)
    for step, span in enumerate(spans):
        pairs = [(source, source + span) for source in range(devices - span)]
        earlier = lax.ppermute(carried.astype(jnp.bfloat16), axis, pairs)
        if step == 0:
            rider, earlier = lax.optimization_barrier((rider, earlier))
        earlier = earlier.astype(jnp.float32)
        last_map = exclusive_maps[step]
        if last_map is None:
            state = earlier
            if step + 1 < len(spans):
                carried = product(inclusive_maps[step], earlier) + carried
        elif step + 1 < len(spans):
            both = jnp.einsum(
                "shde,hef->shdf",
                jnp.stack([last_map, inclusive_maps[step]]),
                earlier,
                precision=HIGHEST,
            )
            state = state + both[0]
            carried = both[1] + carried
        else:
            final_map, final_state = (last_map, earlier)
    return (state, final_map, final_state, rider)


def expand_quantized(raw_rows, scales):
    head_count = scales.shape[1]
    width = raw_rows.shape[1] // head_count
    spread = jnp.arange(raw_rows.shape[1])[None, :] // width == jnp.arange(head_count)[:, None]
    expanded = jnp.dot(scales, spread.astype(jnp.float32), precision=HIGHEST)
    return raw_rows.astype(jnp.float32) * expanded


def causal_filter(window, weights):
    kernel_span = weights.shape[0]
    row_count = window.shape[0] - kernel_span + 1
    summed = jnp.zeros((row_count, window.shape[1]), jnp.float32)
    for offset_tap in range(kernel_span):
        summed = summed + window[offset_tap : offset_tap + row_count] * weights[offset_tap].astype(
            jnp.float32
        )
    return lax.optimization_barrier(jax.nn.silu(summed).astype(jnp.bfloat16))


def unit_heads(conv_rows, head_width):
    row_count = conv_rows.shape[0]
    shaped = conv_rows.astype(jnp.float32).reshape(row_count, -1, head_width)
    return shaped * lax.rsqrt(jnp.sum(shaped * shaped, axis=-1, keepdims=True) + EPSILON)


def to_blocks(array, block):
    block_count = array.shape[0] // block
    return array.reshape(block_count, block, array.shape[1], -1).transpose(0, 2, 1, 3)


def to_block_rows(array, block):
    block_count = array.shape[0] // block
    return array.reshape(block_count, block, -1).transpose(0, 2, 1)


def unit_lower_inverse(strict_part):
    length = strict_part.shape[-1]
    eye = jnp.eye(length, dtype=jnp.float32)
    power = -strict_part
    inverse = eye + power
    span = 2
    if span < length:
        power = jnp.einsum("bhij,bhjk->bhik", power, power, precision=HIGHEST)
    while span < length:
        if 2 * span < length:
            both = jnp.einsum(
                "sbhij,sbhjk->sbhik",
                jnp.stack([inverse, power]),
                jnp.stack([eye + power, power]),
                precision=HIGHEST,
            )
            inverse, power = (both[0], both[1])
        else:
            inverse = jnp.einsum("bhij,bhjk->bhik", inverse, eye + power, precision=HIGHEST)
        span = span * 2
    return inverse


def block_maps(key_units, value_units, logdec, beta_units):
    length = logdec.shape[-1]
    positions = jnp.arange(length)
    lower_incl = positions[:, None] >= positions[None, :]
    lower_strict = positions[:, None] > positions[None, :]
    cumulative = jnp.cumsum(logdec, axis=-1)
    differ = cumulative[..., :, None] - cumulative[..., None, :]
    decay_incl = jnp.where(lower_incl, jnp.exp(jnp.where(lower_incl, differ, 0.0)), 0.0)
    decay_strict = jnp.where(lower_strict, decay_incl, 0.0)
    key_gram = jnp.einsum("bhid,bhjd->bhij", key_units, key_units, precision=HIGHEST)
    inverse = unit_lower_inverse(beta_units[..., :, None] * key_gram * decay_strict)
    growth = jnp.exp(cumulative)
    stacked = jnp.concatenate(
        [(beta_units * growth)[..., None] * key_units, beta_units[..., None] * value_units],
        axis=-1,
    )
    solved = jnp.einsum("bhij,bhjd->bhid", inverse, stacked, precision=HIGHEST)
    key_width = key_units.shape[-1]
    fading = jnp.exp(cumulative[..., -1:] - cumulative)[..., None] * key_units
    faded = jnp.einsum("bhjd,bhje->bhde", fading, solved, precision=HIGHEST)
    eye_key = jnp.eye(key_width, dtype=jnp.float32)
    transition = growth[..., -1][..., None, None] * eye_key - faded[..., :key_width]
    maps = jnp.concatenate([transition, faded[..., key_width:]], axis=-1)
    return (solved[..., key_width:], solved[..., :key_width], maps, decay_incl, growth)


def query_terms(queries, key_units, decay_incl, growth, weight_values, weight_keys):
    mixing = decay_incl * jnp.einsum("bhid,bhjd->bhij", queries, key_units, precision=HIGHEST)
    zero_out = jnp.einsum("bhij,bhjd->bhid", mixing, weight_values, precision=HIGHEST)
    readout = growth[..., None] * queries - jnp.einsum(
        "bhij,bhjd->bhid", mixing, weight_keys, precision=HIGHEST
    )
    return (zero_out, readout)


def product(left, right):
    return jnp.einsum("hde,hef->hdf", left, right, precision=HIGHEST)


def to_rows(blocks):
    return blocks.transpose(0, 2, 1, 3).reshape(-1, blocks.shape[1], blocks.shape[3])


def gated_norm(delta_rows, gate_raw, norm_gain):
    meansq = jnp.mean(delta_rows * delta_rows, axis=-1, keepdims=True)
    normed = delta_rows * lax.rsqrt(meansq + EPSILON) * norm_gain
    gate_float = gate_raw.astype(jnp.float32).reshape(delta_rows.shape)
    return (normed * jax.nn.silu(gate_float)).reshape(delta_rows.shape[0], -1).astype(jnp.bfloat16)


def shards(
    query_raw,
    key_raw,
    value_raw,
    query_scale,
    key_block_scale,
    value_scale,
    conv_query,
    key_filter_taps,
    conv_value,
    gate_input,
    beta_logit,
    decay_base,
    step_bias,
    output_gate,
    norm_gain,
):
    head_width = norm_gain.shape[0]
    margin = conv_query.shape[0] - 1
    query_deq = expand_quantized(query_raw, query_scale)
    key_deq = expand_quantized(key_raw, key_block_scale)
    value_deq = expand_quantized(value_raw, value_scale)
    query_width, key_width = (query_deq.shape[1], key_deq.shape[1])
    tails = from_behind(
        jnp.concatenate([query_deq[-margin:], key_deq[-margin:], value_deq[-margin:]], axis=1),
        "seq",
        1,
    )
    tail_rows = (
        tails[:, :query_width],
        tails[:, query_width : query_width + key_width],
        tails[:, query_width + key_width :],
    )
    local_heads = gate_input.shape[1]
    first_head = lax.axis_index("head") * local_heads
    base_part = lax.dynamic_slice_in_dim(decay_base, first_head, local_heads)
    bias_part = lax.dynamic_slice_in_dim(step_bias, first_head, local_heads)
    key_filtered = causal_filter(jnp.concatenate([tail_rows[1], key_deq], axis=0), key_filter_taps)
    row_count = key_filtered.shape[0]
    key_rows = unit_heads(key_filtered, head_width)
    repeats = local_heads // key_rows.shape[1]
    key_units = to_blocks(jnp.repeat(key_rows, repeats, axis=1), CH)
    logdec = -jnp.exp(base_part)[None, :] * jax.nn.softplus(gate_input + bias_part[None, :])
    logdec = to_block_rows(logdec, CH)
    beta_units = to_block_rows(jax.nn.sigmoid(beta_logit), CH)
    value_conv = causal_filter(jnp.concatenate([tail_rows[2], value_deq], axis=0), conv_value)
    value_units = to_blocks(value_conv.astype(jnp.float32).reshape(row_count, -1, head_width), CH)
    weight_values, weight_keys, maps, decay_incl, growth = block_maps(
        key_units, value_units, logdec, beta_units
    )
    key_width = key_units.shape[-1]
    device_map = maps[0]
    maps_before = [None]
    for block in range(1, maps.shape[0]):
        maps_before.append(device_map)
        device_map = jnp.einsum(
            "hde,hef->hdf", maps[block][..., :key_width], device_map, precision=HIGHEST
        ).at[..., key_width:].add(maps[block][..., key_width:])
    dev_trans, dev_offset = (device_map[..., :key_width], device_map[..., key_width:])
    incoming, final_map, final_state, query_window = scan_states(
        dev_trans, dev_offset, "seq", jnp.concatenate([tail_rows[0], query_deq], axis=0)
    )
    query_conv = causal_filter(query_window, conv_query)
    query_rows = unit_heads(query_conv, head_width) * head_width ** (-0.5)
    queries = to_blocks(jnp.repeat(query_rows, repeats, axis=1), CH)
    zero_out, readout = query_terms(
        queries, key_units, decay_incl, growth, weight_values, weight_keys
    )
    local_outs, read_maps = ([zero_out[0]], [readout[0]])
    for block in range(1, maps.shape[0]):
        read = jnp.einsum("hid,hde->hie", readout[block], maps_before[block], precision=HIGHEST)
        read_maps.append(read[..., :key_width])
        local_outs.append(zero_out[block] + read[..., key_width:])
    reads = jnp.stack(read_maps)
    outputs = jnp.stack(local_outs) + jnp.einsum(
        "bhid,hde->bhie", reads, incoming, precision=HIGHEST
    )
    if final_map is not None:
        lead = jnp.einsum("bhid,hde->bhie", reads, final_map, precision=HIGHEST)
        outputs = outputs + jnp.einsum("bhid,hde->bhie", lead, final_state, precision=HIGHEST)
    gated_rows = gated_norm(to_rows(outputs), output_gate, norm_gain)
    return gated_rows


def solution(mesh):
    placed = (
        P("seq", "head"),
        P("seq", "head"),
        P("seq", "head"),
        P("seq", "head"),
        P("seq", "head"),
        P("seq", "head"),
        P(None, "head"),
        P(None, "head"),
        P(None, "head"),
        P("seq", "head"),
        P("seq", "head"),
        P(),
        P(),
        P("seq", "head"),
        P(),
    )
    return jax.shard_map(
        shards, mesh=mesh, in_specs=placed, out_specs=P("seq", "head"), check_vma=False
    )
```
